32 devices in a mesh: groups: 2 (over x), date: 8 (over z, y), row: 2 (over core).
Axes of the slice: x: 2, y: 2, z: 4, core: 2. Of those that a mesh axis runs over, the one named last changes fastest.
Arguments:
- scenes: bfloat16 [16, 4, 512, 1024], P(('groups', 'date'), None, 'row'), parts along dimension 0, may hold values from -6 to 6
- resample_taps: float32 [2, 4, 7], replicated, may hold values from 0 to 0.35
- clear_mask: int32 [16, 128, 8], P('groups', ('row', 'date')), parts along dimension 0, may hold values 0 or 1
Outputs:
- smooth_fine: bfloat16 [16, 4, 512, 1024], P('groups', None, ('row', 'date')), parts along dimension 0
- smooth_half: bfloat16 [16, 4, 256, 512], P('groups', None, ('row', 'date')), parts along dimension 0
- smooth_quarter: bfloat16 [16, 4, 128, 256], P('groups', None, ('row', 'date')), parts along dimension 0
The draws below stay inside these ranges and needn't reach their ends.
There are 2 independent parts, one for each index of `groups`. The reference program is written for one: setup_inputs(seed, part) draws one part's arguments, and reference() takes and returns one part's arrays. A program takes and returns all parts, laid end to end along the dimension named above; an argument that names none is the same for every part. Nothing has to cross between parts.
Inputs may be any that keep to these rules, and one draw needn't show every extreme that they name: `clear_mask`: 1 marks a clear block, 0 a cloudy one.
All inputs are finite; a program needn't handle non-finite values.
Results may differ from the reference program's by a relative error of at most 0.005.
Values may be sent and summed in bfloat16 or wider, within the bound.
No kernel may reach another device: no remote copies, remote signals or barrier semaphores. Data moves between devices by JAX's collectives and lax.ppermute only.
A program may use at most 128 MiB of HBM per device.

```python
import math
import jax
import jax.numpy as jnp
from jax import lax

BANDS = 4
W = 1024
DATES = 8
H = 512


def set_ends(array, stream_key, smallest, top_value):
    place = [jax.random.randint(jax.random.fold_in(stream_key, axis), (), 0, length) for axis, length in enumerate(array.shape)]
    main_axis = array.shape.index(max(array.shape))
    beside = place[:main_axis] + [(place[main_axis] + 1) % array.shape[main_axis]] + place[main_axis + 1:]
    return array.at[tuple(place)].set(smallest).at[tuple(beside)].set(top_value)


def shard_levels(stream_key, extent, cuts, low, high):
    level = 1.0
    for axis_at, blocks in cuts:
        steps = jax.random.uniform(jax.random.fold_in(jax.random.fold_in(stream_key, 6), axis_at), (blocks,), jnp.float32, low / len(cuts), high / len(cuts))
        level = level * jnp.repeat(jnp.exp(steps), extent[axis_at] // blocks).reshape((-1,) + (1,) * (len(extent) - 1 - axis_at))
    return level


def normal_values(key, dims, spread, bound, shards=(), kind=jnp.bfloat16):
    values = spread * jax.random.normal(key, dims, jnp.float32)
    if shards:
        values = values * shard_levels(key, dims, shards, -0.22, 0.18)
    return jnp.clip(values, -bound, bound).astype(kind)


def setup_inputs(seed: int = 0, part: int = 0) -> dict:
    streams_of = jax.random.split(jax.random.key(seed), 4)
    own_keys = jax.random.split(jax.random.fold_in(streams_of[3], part), 4)
    scenes = normal_values(own_keys[0], (DATES, BANDS, H, W), 1.0, 6.0, ((0, 8), (2, 2)))
    resample_taps = jnp.clip(jax.random.uniform(streams_of[1], (2, BANDS, 7), jnp.float32, 0.0, 0.35), 0.0, 0.35)
    clear_mask = set_ends((jax.random.randint(own_keys[2], (DATES, H // 4, W // 128), 0, 4) < 3).astype(jnp.int32), jax.random.fold_in(own_keys[2], 1), 0, 1)
    return dict(scenes=scenes, resample_taps=resample_taps, clear_mask=clear_mask)


gap_weights = [math.exp(-((k - 4) ** 2) / 8.0) for k in range(9)]
savgol_coeffs = [c / 231.0 for c in [-21.0, 14.0, 39.0, 54.0, 59.0, 54.0, 39.0, 14.0, -21.0]]
pyramid_filter = [0.125, 0.375, 0.375, 0.125]


def valid_taps(values, taps, axis):
    count = values.shape[axis] - 6
    total = jnp.zeros(values.shape[:axis] + (count,) + values.shape[axis + 1:], jnp.float32)
    for k in range(7):
        shape = [1] * values.ndim
        shape[-3] = taps.shape[0]
        total = total + taps[:, k].reshape(shape) * lax.slice_in_dim(values, k, k + count, 1, axis)
    return total


def decimate_valid(values, axis):
    count = (values.shape[axis] - 2) // 2
    total = jnp.zeros(values.shape[:axis] + (count,) + values.shape[axis + 1:], jnp.float32)
    for p in range(4):
        total = total + pyramid_filter[p] * lax.slice_in_dim(values, p, p + 2 * count - 1, 2, axis)
    return total


def pad_axis(values, width, axis):
    widths = [(0, 0)] * values.ndim
    widths[axis] = (width, width)
    return jnp.pad(values, widths)


def decimate_both(values):
    rows_done = decimate_valid(pad_axis(values, 1, values.ndim - 2), values.ndim - 2)
    return decimate_valid(pad_axis(rows_done, 1, values.ndim - 1), values.ndim - 1)


def smooth(level, clear):
    values = level.astype(jnp.float32)
    dates = values.shape[0]
    clear4 = clear[:, None]
    weight = 0.1 + 0.9 * clear4
    weighted = jnp.pad(weight * values, ((4, 4), (0, 0), (0, 0), (0, 0)))
    weight_pad = jnp.pad(weight, ((4, 4), (0, 0), (0, 0), (0, 0)))
    numer = jnp.zeros_like(values)
    denom = jnp.zeros_like(weight)
    for k in range(9):
        numer = numer + gap_weights[k] * weighted[k:k + dates]
        denom = denom + gap_weights[k] * weight_pad[k:k + dates]
    filled = clear4 * values + (1.0 - clear4) * (numer / denom)
    edged = jnp.pad(filled, ((4, 4), (0, 0), (0, 0), (0, 0)), mode="edge")
    result = jnp.zeros_like(values)
    for k in range(9):
        result = result + savgol_coeffs[k] * edged[k:k + dates]
    return result.astype(jnp.bfloat16)


def expand_mask(clear_mask, row_rep, col_rep):
    grown = jnp.repeat(jnp.repeat(clear_mask, row_rep, axis=1), col_rep, axis=2)
    return grown.astype(jnp.float32)


def pyramid_one(scene, resample_taps):
    across = valid_taps(pad_axis(scene.astype(jnp.float32), 3, 2), resample_taps[0], 2)
    resampled = valid_taps(pad_axis(across, 3, 1), resample_taps[1], 1)
    half = decimate_both(resampled)
    quarter = decimate_both(half)
    return resampled.astype(jnp.bfloat16), half.astype(jnp.bfloat16), quarter.astype(jnp.bfloat16)


def smooth_level(level, clear):
    bands_first = jnp.moveaxis(level, 1, 0)
    result = lax.map(lambda band: smooth(band[:, None], clear)[:, 0], bands_first)
    return jnp.moveaxis(result, 0, 1)


def reference(scenes, resample_taps, clear_mask):
    level_zero, level_one, level_two = lax.map(lambda scene: pyramid_one(scene, resample_taps), scenes)
    smooth_fine = smooth_level(level_zero, expand_mask(clear_mask, 4, 128))
    smooth_half = smooth_level(level_one, expand_mask(clear_mask, 2, 64))
    smooth_quarter = smooth_level(level_two, expand_mask(clear_mask, 1, 32))
    return smooth_fine, smooth_half, smooth_quarter
```

```python
import math

import jax
import jax.numpy as jnp
import numpy as np
from jax import lax
from jax.sharding import PartitionSpec as P

gap_weights = [math.exp(-((k - 4) ** 2) / 8.0) for k in range(9)]
savgol_coeffs = [c / 231.0 for c in [-21.0, 14.0, 39.0, 54.0, 59.0, 54.0, 39.0, 14.0, -21.0]]
pyramid_filter = [0.125, 0.375, 0.375, 0.125]


def padded(block, sides, width):
    for axis, dim in sides:
        count = lax.axis_size(axis)
        forward = [(i, i + 1) for i in range(count - 1)]
        backward = [(target, source) for source, target in forward]
        low = lax.ppermute(
            lax.slice_in_dim(block, block.shape[dim] - width, None, axis=dim), axis, forward
        )
        high = lax.ppermute(lax.slice_in_dim(block, 0, width, axis=dim), axis, backward)
        block = jnp.concatenate([low, block, high], axis=dim)
    return block


def column_taps(values, taps):
    width = values.shape[-1]
    wide = jnp.pad(values, ((0, 0), (0, 0), (3, 3)))
    total = taps[0] * wide[..., 0:width]
    for k in range(1, 7):
        total = total + taps[k] * wide[..., k : k + width]
    return total


def row_taps(values, taps):
    count = values.shape[1] - 6
    total = taps[0] * values[:, 0:count]
    for k in range(1, 7):
        total = total + taps[k] * values[:, k : k + count]
    return total


def halve_table(width):
    source = np.arange(width)[:, None]
    target = np.arange(width // 2)[None, :]
    place = source - 2 * target + 1
    table = np.zeros((width, width // 2), np.float32)
    for p in range(4):
        table = table + pyramid_filter[p] * (place == p)
    return jnp.asarray(table, jnp.bfloat16)


def halve_columns(values):
    table = halve_table(values.shape[-1])
    high = values.astype(jnp.bfloat16)
    low = (values - high.astype(jnp.float32)).astype(jnp.bfloat16)
    dims = (((values.ndim - 1,), (0,)), ((), ()))
    return lax.dot_general(high, table, dims, preferred_element_type=jnp.float32) + lax.dot_general(
        low, table, dims, preferred_element_type=jnp.float32
    )


def halve_rows(extended):
    pairs_count = extended.shape[1] // 2
    pairs = extended.reshape(extended.shape[:1] + (pairs_count, 2) + extended.shape[2:])
    even = pairs[:, :, 0]
    odd = pairs[:, :, 1]
    return (
        pyramid_filter[0] * even[:, :-1]
        + pyramid_filter[1] * odd[:, :-1]
        + pyramid_filter[2] * even[:, 1:]
        + pyramid_filter[3] * odd[:, 1:]
    )


def decimate_rim(extended):
    return halve_columns(halve_rows(extended))


def keep_rows(values, first, total):
    places = first + lax.iota(jnp.int32, values.shape[1])
    inside = (places >= 0) & (places < total)
    return jnp.where(inside[None, :, None], values, 0.0)


def smooth_operator(dates):
    clamp = np.zeros((dates, dates), np.float64)
    near = np.zeros((dates, dates), np.float64)
    for t in range(dates):
        for k in range(9):
            clamp[t, min(max(t + k - 4, 0), dates - 1)] += savgol_coeffs[k]
            if 0 <= t + k - 4 < dates:
                near[t, t + k - 4] = gap_weights[k]
    return clamp.astype(np.float32), near.astype(np.float32)


def smooth_coefficients(clear):
    dates = clear.shape[0]
    clamp, near = smooth_operator(dates)
    weight = 0.1 + 0.9 * clear
    denom = jnp.einsum("su,uxy->sxy", near, weight, precision=lax.Precision.HIGHEST)
    gap = (1.0 - clear) / denom
    fill = near[:, :, None, None] * weight[None, :] * gap[:, None]
    fill = fill + jnp.eye(dates, dtype=jnp.float32)[:, :, None, None] * clear[None, :]
    return jnp.einsum("ts,suxy->tuxy", clamp, fill, precision=lax.Precision.HIGHEST)


def expand(coeff, rows, cols):
    lead = coeff.shape[:-2]
    rm, cm = coeff.shape[-2:]
    grown = jnp.broadcast_to(coeff[..., :, None, :, None], lead + (rm, rows, cm, cols))
    return grown.reshape(lead + (rm * rows, cm * cols))


def smooth(level, coeff, rows, cols):
    values = level.astype(jnp.float32)
    grown = expand(coeff, rows, cols)
    return jnp.sum(grown * values[None], axis=1).astype(jnp.bfloat16)


def local(scenes, resample_taps, clear_mask):
    rows = scenes.shape[2]
    bands = scenes.shape[1]
    band_index = lax.axis_index("row")
    total_rows = rows * lax.axis_size("row")
    ndate = lax.axis_size("date")
    extended = padded(scenes, (("row", 2),), 6)
    clear = clear_mask.astype(jnp.float32)
    coeff = smooth_coefficients(clear)
    mask_rows = clear.shape[1]
    mask_cols = clear.shape[2]
    fine_rows = rows // ndate
    width = scenes.shape[3]
    fine = []
    half = []
    quarter = []
    for b in range(bands):
        source = extended[:, b].astype(jnp.float32)
        across = column_taps(source, resample_taps[0, b])
        resampled_wide = row_taps(across, resample_taps[1, b])
        resampled_wide = keep_rows(resampled_wide, band_index * rows - 3, total_rows)
        half_wide = decimate_rim(resampled_wide)
        half_wide = keep_rows(half_wide, band_index * (rows // 2) - 1, total_rows // 2)
        level_zero = resampled_wide[:, 3 : 3 + rows].astype(jnp.bfloat16)
        level_one = half_wide[:, 1 : 1 + rows // 2].astype(jnp.bfloat16)
        level_two = decimate_rim(half_wide).astype(jnp.bfloat16)
        got = [
            lax.all_to_all(level, "date", split_axis=1, concat_axis=0, tiled=True)
            for level in (level_zero, level_one, level_two)
        ]
        fine.append(smooth(got[0], coeff, fine_rows // mask_rows, width // mask_cols))
        half.append(smooth(got[1], coeff, fine_rows // 2 // mask_rows, width // 2 // mask_cols))
        quarter.append(smooth(got[2], coeff, fine_rows // 4 // mask_rows, width // 4 // mask_cols))
    return tuple(jnp.stack(parts, axis=1) for parts in (fine, half, quarter))


def solution(mesh):
    in_specs = (P(("groups", "date"), None, "row", None), P(), P("groups", ("row", "date"), None))
    out_specs = (
        P("groups", None, ("row", "date"), None),
        P("groups", None, ("row", "date"), None),
        P("groups", None, ("row", "date"), None),
    )
    return jax.shard_map(local, mesh=mesh, in_specs=in_specs, out_specs=out_specs, check_vma=False)
```

```python
import math

import jax
import jax.numpy as jnp
from jax import lax
from jax.sharding import PartitionSpec as P

gap_weights = [math.exp(-((k - 4) ** 2) / 8.0) for k in range(9)]
savgol_coeffs = [c / 231.0 for c in [-21.0, 14.0, 39.0, 54.0, 59.0, 54.0, 39.0, 14.0, -21.0]]
pyramid_filter = [0.125, 0.375, 0.375, 0.125]


def padded(block, sides, width):
    for axis, dim in sides:
        count = lax.axis_size(axis)
        forward = [(i, i + 1) for i in range(count - 1)]
        backward = [(target, source) for source, target in forward]
        low = lax.ppermute(
            lax.slice_in_dim(block, block.shape[dim] - width, None, axis=dim), axis, forward
        )
        high = lax.ppermute(lax.slice_in_dim(block, 0, width, axis=dim), axis, backward)
        block = jnp.concatenate([low, block, high], axis=dim)
    return block


def valid_taps(values, taps, axis):
    count = values.shape[axis] - 6
    total = jnp.zeros(values.shape[:axis] + (count,) + values.shape[axis + 1 :], jnp.float32)
    for k in range(7):
        shape = [1] * values.ndim
        shape[-3] = taps.shape[0]
        total = total + taps[:, k].reshape(shape) * lax.slice_in_dim(values, k, k + count, 1, axis)
    return total


def column_resample(values, taps):
    lead = values.shape[:3]
    width = values.shape[3]
    tiles = width // 128
    source = lax.broadcasted_iota(jnp.int32, (3 * 128, 128), 0)
    target = lax.broadcasted_iota(jnp.int32, (3 * 128, 128), 1)
    offset = source - target - 125
    table = jnp.zeros((taps.shape[0], 3 * 128, 128), jnp.float32)
    for k in range(7):
        table = table + taps[:, k][:, None, None] * (offset == k).astype(jnp.float32)[None]
    high = table.astype(jnp.bfloat16)
    rest = table - high.astype(jnp.float32)
    mid = rest.astype(jnp.bfloat16)
    low = (rest - mid.astype(jnp.float32)).astype(jnp.bfloat16)
    parts = jnp.concatenate([high, mid, low], axis=2)
    blocks = values.reshape(lead + (tiles, 128))
    blocks = jnp.pad(blocks, ((0, 0), (0, 0), (0, 0), (1, 1), (0, 0)))
    total = None
    for d in range(3):
        window = blocks[:, :, :, d : d + tiles]
        term = jnp.einsum(
            "tbrjs,bsc->tbrjc",
            window,
            parts[:, d * 128 : (d + 1) * 128],
            preferred_element_type=jnp.float32,
        )
        total = term if total is None else total + term
    total = total[..., 0:128] + total[..., 128:256] + total[..., 256:384]
    return total.reshape(lead + (width,))


def halve_columns(values):
    width = values.shape[3]
    source = lax.broadcasted_iota(jnp.int32, (width, width // 2), 0)
    target = lax.broadcasted_iota(jnp.int32, (width, width // 2), 1)
    place = source - 2 * target + 1
    table = jnp.zeros((width, width // 2), jnp.float32)
    for p in range(4):
        table = table + pyramid_filter[p] * (place == p).astype(jnp.float32)
    return jnp.dot(values, table, precision=lax.Precision.HIGHEST)


def halve_rows(extended):
    pairs_count = extended.shape[2] // 2
    pairs = extended.reshape(extended.shape[:2] + (pairs_count, 2) + extended.shape[3:])
    even = pairs[:, :, :, 0]
    odd = pairs[:, :, :, 1]
    return (
        pyramid_filter[0] * even[:, :, :-1]
        + pyramid_filter[1] * odd[:, :, :-1]
        + pyramid_filter[2] * even[:, :, 1:]
        + pyramid_filter[3] * odd[:, :, 1:]
    )


def decimate_rim(extended):
    return halve_columns(halve_rows(extended))


def keep_rows(values, first, total):
    places = first + lax.iota(jnp.int32, values.shape[2])
    inside = (places >= 0) & (places < total)
    return jnp.where(inside[None, None, :, None], values, 0.0)


def smooth(level, clear):
    values = level.astype(jnp.float32)
    dates = values.shape[0]
    clear4 = clear[:, None]
    weight = 0.1 + 0.9 * clear4
    weighted = jnp.pad(weight * values, ((4, 4), (0, 0), (0, 0), (0, 0)))
    weight_pad = jnp.pad(weight, ((4, 4), (0, 0), (0, 0), (0, 0)))
    numer = jnp.zeros_like(values)
    denom = jnp.zeros_like(weight)
    for k in range(9):
        numer = numer + gap_weights[k] * weighted[k : k + dates]
        denom = denom + gap_weights[k] * weight_pad[k : k + dates]
    filled = clear4 * values + (1.0 - clear4) * (numer / denom)
    edged = jnp.pad(filled, ((4, 4), (0, 0), (0, 0), (0, 0)), mode="edge")
    result = jnp.zeros_like(values)
    for k in range(9):
        result = result + savgol_coeffs[k] * edged[k : k + dates]
    return result.astype(jnp.bfloat16)


def expand_mask(clear_mask, row_rep, col_rep):
    grown = jnp.repeat(jnp.repeat(clear_mask, row_rep, axis=1), col_rep, axis=2)
    return grown.astype(jnp.float32)


def local(scenes, resample_taps, clear_mask):
    rows = scenes.shape[2]
    extended = padded(scenes, (("row", 2),), 6)
    across = column_resample(extended, resample_taps[0])
    resampled_wide = valid_taps(across, resample_taps[1], 2)
    band_index = lax.axis_index("row")
    total_rows = rows * lax.axis_size("row")
    resampled_wide = keep_rows(resampled_wide, band_index * rows - 3, total_rows)
    half_wide = decimate_rim(resampled_wide)
    half_wide = keep_rows(half_wide, band_index * (rows // 2) - 1, total_rows // 2)
    resampled = resampled_wide[:, :, 3 : 3 + rows]
    half = half_wide[:, :, 1 : 1 + rows // 2]
    quarter = decimate_rim(half_wide)
    level_zero = resampled.astype(jnp.bfloat16)
    level_one = half.astype(jnp.bfloat16)
    level_two = quarter.astype(jnp.bfloat16)
    clear_fine = expand_mask(clear_mask, 4, 128)
    clear_half = expand_mask(clear_mask, 2, 64)
    clear_quarter = expand_mask(clear_mask, 1, 32)
    smooth_fine = smooth(
        lax.all_to_all(level_zero, "date", split_axis=2, concat_axis=0, tiled=True), clear_fine
    )
    smooth_half = smooth(
        lax.all_to_all(level_one, "date", split_axis=2, concat_axis=0, tiled=True), clear_half
    )
    smooth_quarter = smooth(
        lax.all_to_all(level_two, "date", split_axis=2, concat_axis=0, tiled=True), clear_quarter
    )
    return (smooth_fine, smooth_half, smooth_quarter)


def solution(mesh):
    in_specs = (P(("groups", "date"), None, "row", None), P(), P("groups", ("row", "date"), None))
    out_specs = (
        P("groups", None, ("row", "date"), None),
        P("groups", None, ("row", "date"), None),
        P("groups", None, ("row", "date"), None),
    )
    return jax.shard_map(local, mesh=mesh, in_specs=in_specs, out_specs=out_specs, check_vma=False)
```

```python
import math

import jax
import jax.numpy as jnp
from jax import lax
from jax.sharding import PartitionSpec as P
from jax.experimental import pallas as pl
from jax.experimental.pallas import tpu as pltpu

gap_weights = [math.exp(-((k - 4) ** 2) / 8.0) for k in range(9)]
savgol_coeffs = [c / 231.0 for c in [-21.0, 14.0, 39.0, 54.0, 59.0, 54.0, 39.0, 14.0, -21.0]]
pyramid_filter = [0.125, 0.375, 0.375, 0.125]


def padded(block, sides, width):
    for axis, dim in sides:
        count = lax.axis_size(axis)
        forward = [(i, i + 1) for i in range(count - 1)]
        backward = [(target, source) for source, target in forward]
        low = lax.ppermute(
            lax.slice_in_dim(block, block.shape[dim] - width, None, axis=dim), axis, forward
        )
        high = lax.ppermute(lax.slice_in_dim(block, 0, width, axis=dim), axis, backward)
        block = jnp.concatenate([low, block, high], axis=dim)
    return block


def filter_matrix(out_count, in_count, step, shift, taps):
    out_at = lax.broadcasted_iota(jnp.int32, (out_count, in_count), 0)
    in_at = lax.broadcasted_iota(jnp.int32, (out_count, in_count), 1)
    place = in_at - step * out_at - shift
    total = jnp.zeros((out_count, in_count), jnp.float32)
    for k in range(len(taps)):
        total = total + jnp.where(place == k, taps[k], 0.0)
    return total


def inside_rows(count, first, total):
    places = first + lax.iota(jnp.int32, count)
    return ((places >= 0) & (places < total)).astype(jnp.float32)


def row_operators(taps, band_index, rows, total_rows, depth):
    hi = lax.Precision.HIGHEST
    wide = rows + 6
    keep_wide = inside_rows(wide, band_index * rows - 3, total_rows)
    keep_half = inside_rows(rows // 2 + 2, band_index * (rows // 2) - 1, total_rows // 2)
    down = filter_matrix(rows // 2 + 2, wide, 2, 0, pyramid_filter)
    down_two = filter_matrix(rows // 4, rows // 2 + 2, 2, 0, pyramid_filter)
    zs, hs, qs = [], [], []
    for b in range(taps.shape[0]):
        resample = filter_matrix(wide, rows + 12, 1, 0, [taps[b, k] for k in range(7)])
        resample = resample * keep_wide[:, None]
        half = jnp.dot(down, resample, precision=hi) * keep_half[:, None]
        quarter = jnp.dot(down_two, half, precision=hi)
        zs.append(resample[3 : 3 + rows])
        hs.append(half[1 : 1 + rows // 2])
        qs.append(quarter)
    pad = ((0, 0), (0, 0), (0, depth - (rows + 12)))
    return tuple(jnp.pad(jnp.stack(m), pad) for m in (zs, hs, qs))


def column_operators(taps, width):
    hi = lax.Precision.HIGHEST
    band = jnp.stack(
        [filter_matrix(128, 3 * 128, 1, 125, [taps[b, k] for k in range(7)]).T for b in range(taps.shape[0])]
    )
    halve = filter_matrix(width // 2, width, 2, -1, pyramid_filter).T
    halve_two = filter_matrix(width // 4, width // 2, 2, -1, pyramid_filter).T
    both = jnp.dot(halve, halve_two, precision=hi)
    return band, halve.astype(jnp.bfloat16), both.astype(jnp.bfloat16)


def split_two(a):
    high = a.astype(jnp.bfloat16)
    low = (a - high.astype(jnp.float32)).astype(jnp.bfloat16)
    return high, low


def mm(a, b):
    return jnp.dot(a, b, preferred_element_type=jnp.float32)


def pyramid_kernel(x_ref, band_ref, z_ref, h_ref, q_ref, halve_ref, both_ref, o0_ref, o1_ref, o2_ref, across_ref):
    x = x_ref[0, 0]
    used = x.shape[0]
    width = x.shape[1]
    tiles = width // 128
    table = band_ref[0]
    t_high = table.astype(jnp.bfloat16)
    rest = table - t_high.astype(jnp.float32)
    t_mid = rest.astype(jnp.bfloat16)
    t_low = (rest - t_mid.astype(jnp.float32)).astype(jnp.bfloat16)
    for j in range(tiles):
        lo = max(j - 1, 0) * 128
        hi_col = min(j + 2, tiles) * 128
        first = lo - (j - 1) * 128
        last = first + (hi_col - lo)
        window = x[:, lo:hi_col]
        acc = mm(window, t_high[first:last]) + mm(window, t_mid[first:last]) + mm(window, t_low[first:last])
        across_ref[0:used, j * 128 : (j + 1) * 128] = acc
    depth = across_ref.shape[0]
    across_ref[used:depth, :] = jnp.zeros((depth - used, width), jnp.float32)
    a_high, a_low = split_two(across_ref[...])

    def rows_of(m_ref):
        m_high, m_low = split_two(m_ref[0])
        return mm(m_high, a_high) + mm(m_high, a_low) + mm(m_low, a_high)

    o0_ref[0, 0] = rows_of(z_ref).astype(o0_ref.dtype)
    h_high, h_low = split_two(rows_of(h_ref))
    o1_ref[0, 0] = (mm(h_high, halve_ref[...]) + mm(h_low, halve_ref[...])).astype(o1_ref.dtype)
    q_high, q_low = split_two(rows_of(q_ref))
    o2_ref[0, 0] = (mm(q_high, both_ref[...]) + mm(q_low, both_ref[...])).astype(o2_ref.dtype)


def pyramid(extended, resample_taps, band_index, total_rows):
    dates, bands, used, width = extended.shape
    rows = used - 16
    depth = ((used + 127) // 128) * 128
    zs, hs, qs = row_operators(resample_taps[1], band_index, rows, total_rows, depth)
    band, halve, both = column_operators(resample_taps[0], width)
    out_shape = (
        jax.ShapeDtypeStruct((dates, bands, rows, width), jnp.bfloat16),
        jax.ShapeDtypeStruct((dates, bands, rows // 2, width // 2), jnp.bfloat16),
        jax.ShapeDtypeStruct((dates, bands, rows // 4, width // 4), jnp.bfloat16),
    )
    return pl.pallas_call(
        pyramid_kernel,
        grid=(dates, bands),
        in_specs=[
            pl.BlockSpec((1, 1, used, width), lambda d, b: (d, b, 0, 0)),
            pl.BlockSpec((1, 3 * 128, 128), lambda d, b: (b, 0, 0)),
            pl.BlockSpec((1, rows, depth), lambda d, b: (b, 0, 0)),
            pl.BlockSpec((1, rows // 2, depth), lambda d, b: (b, 0, 0)),
            pl.BlockSpec((1, rows // 4, depth), lambda d, b: (b, 0, 0)),
            pl.BlockSpec((width, width // 2), lambda d, b: (0, 0)),
            pl.BlockSpec((width, width // 4), lambda d, b: (0, 0)),
        ],
        out_specs=[
            pl.BlockSpec((1, 1, rows, width), lambda d, b: (d, b, 0, 0)),
            pl.BlockSpec((1, 1, rows // 2, width // 2), lambda d, b: (d, b, 0, 0)),
            pl.BlockSpec((1, 1, rows // 4, width // 4), lambda d, b: (d, b, 0, 0)),
        ],
        out_shape=out_shape,
        scratch_shapes=[pltpu.VMEM((depth, width), jnp.float32)],
    )(extended, band, zs, hs, qs, halve, both)


def smooth(level, clear):
    values = level.astype(jnp.float32)
    dates = values.shape[0]
    clear4 = clear[:, None]
    weight = 0.1 + 0.9 * clear4
    weighted = jnp.pad(weight * values, ((4, 4), (0, 0), (0, 0), (0, 0)))
    weight_pad = jnp.pad(weight, ((4, 4), (0, 0), (0, 0), (0, 0)))
    numer = jnp.zeros_like(values)
    denom = jnp.zeros_like(weight)
    for k in range(9):
        numer = numer + gap_weights[k] * weighted[k : k + dates]
        denom = denom + gap_weights[k] * weight_pad[k : k + dates]
    filled = clear4 * values + (1.0 - clear4) * (numer / denom)
    edged = jnp.pad(filled, ((4, 4), (0, 0), (0, 0), (0, 0)), mode="edge")
    result = jnp.zeros_like(values)
    for k in range(9):
        result = result + savgol_coeffs[k] * edged[k : k + dates]
    return result.astype(jnp.bfloat16)


def expand_mask(clear_mask, row_rep, col_rep):
    grown = jnp.repeat(jnp.repeat(clear_mask, row_rep, axis=1), col_rep, axis=2)
    return grown.astype(jnp.float32)


def expand_mask(clear_mask, row_rep, col_rep):
    grown = jnp.repeat(jnp.repeat(clear_mask, row_rep, axis=1), col_rep, axis=2)
    return grown.astype(jnp.float32)


def local(scenes, resample_taps, clear_mask):
    rows = scenes.shape[2]
    band_index = lax.axis_index("row")
    total_rows = rows * lax.axis_size("row")
    extended = padded(scenes, (("row", 2),), 6)
    extended = jnp.pad(extended, ((0, 0), (0, 0), (0, 4), (0, 0)))
    level_zero, level_one, level_two = pyramid(extended, resample_taps, band_index, total_rows)
    clear_fine = expand_mask(clear_mask, 4, 128)
    clear_half = expand_mask(clear_mask, 2, 64)
    clear_quarter = expand_mask(clear_mask, 1, 32)
    smooth_fine = smooth(
        lax.all_to_all(level_zero, "date", split_axis=2, concat_axis=0, tiled=True), clear_fine
    )
    smooth_half = smooth(
        lax.all_to_all(level_one, "date", split_axis=2, concat_axis=0, tiled=True), clear_half
    )
    smooth_quarter = smooth(
        lax.all_to_all(level_two, "date", split_axis=2, concat_axis=0, tiled=True), clear_quarter
    )
    return (smooth_fine, smooth_half, smooth_quarter)


def solution(mesh):
    in_specs = (P(("groups", "date"), None, "row", None), P(), P("groups", ("row", "date"), None))
    out_specs = (
        P("groups", None, ("row", "date"), None),
        P("groups", None, ("row", "date"), None),
        P("groups", None, ("row", "date"), None),
    )
    return jax.shard_map(local, mesh=mesh, in_specs=in_specs, out_specs=out_specs, check_vma=False)
```

```python
import math

import jax
import jax.numpy as jnp
from jax import lax
from jax.sharding import PartitionSpec as P
from jax.experimental import pallas as pl
from jax.experimental.pallas import tpu as pltpu

gap_weights = [math.exp(-((k - 4) ** 2) / 8.0) for k in range(9)]
savgol_coeffs = [c / 231.0 for c in [-21.0, 14.0, 39.0, 54.0, 59.0, 54.0, 39.0, 14.0, -21.0]]
pyramid_filter = [0.125, 0.375, 0.375, 0.125]


def padded(block, sides, width):
    for axis, dim in sides:
        count = lax.axis_size(axis)
        forward = [(i, i + 1) for i in range(count - 1)]
        backward = [(target, source) for source, target in forward]
        low = lax.ppermute(
            lax.slice_in_dim(block, block.shape[dim] - width, None, axis=dim), axis, forward
        )
        high = lax.ppermute(lax.slice_in_dim(block, 0, width, axis=dim), axis, backward)
        block = jnp.concatenate([low, block, high], axis=dim)
    return block


def inside_rows(count, first, valid, total):
    at = lax.iota(jnp.int32, count)
    places = first + at
    keep = (places >= 0) & (places < total) & (at < valid)
    return keep.astype(jnp.float32)[:, None]


def split_two(a):
    high = a.astype(jnp.bfloat16)
    low = (a - high.astype(jnp.float32)).astype(jnp.bfloat16)
    return high, low


def mm(a, b):
    return jnp.dot(a, b, preferred_element_type=jnp.float32)


def band_table(rows, cols, shift, taps):
    step, weights = taps
    s_at = lax.broadcasted_iota(jnp.int32, (rows, cols), 0)
    c_at = lax.broadcasted_iota(jnp.int32, (rows, cols), 1)
    place = s_at - step * c_at - shift
    total = jnp.zeros((rows, cols), jnp.float32)
    for k, w in enumerate(weights):
        total = total + jnp.where(place == k, w, 0.0)
    return total


def halve_columns(values, table, out_ref):
    width = values.shape[1]
    high, low = split_two(values)
    for j in range(width // 256):
        lo = max(256 * j - 128, 0)
        hi_col = min(256 * j + 384, width)
        first = lo - (256 * j - 128)
        last = first + (hi_col - lo)
        part = table[first:last]
        out_ref[j] = mm(high[:, lo:hi_col], part) + mm(low[:, lo:hi_col], part)


def halve_rows(source_ref, count):
    total = pyramid_filter[0] * source_ref[:, pl.ds(0, count, stride=2), :]
    for p in range(1, 4):
        total = total + pyramid_filter[p] * source_ref[:, pl.ds(p, count, stride=2), :]
    return jnp.concatenate([total[j] for j in range(total.shape[0])], axis=1)


def pyramid_kernel(taps_ref, x_ref, keep_wide_ref, keep_half_ref, o0_ref, o1_ref, o2_ref,
                   across_ref, wide_ref, half_ref, quarter_ref):
    b = pl.program_id(1)
    x = x_ref[0, 0]
    used = x.shape[0]
    width = x.shape[1]
    tiles = width // 128
    column = [taps_ref[0, b, k] for k in range(7)]
    row = [taps_ref[1, b, k] for k in range(7)]
    table = band_table(3 * 128, 128, 125, (1, column))
    t_high = table.astype(jnp.bfloat16)
    rest = table - t_high.astype(jnp.float32)
    t_mid = rest.astype(jnp.bfloat16)
    t_low = (rest - t_mid.astype(jnp.float32)).astype(jnp.bfloat16)
    for j in range(tiles):
        lo = max(j - 1, 0) * 128
        hi_col = min(j + 2, tiles) * 128
        first = lo - (j - 1) * 128
        last = first + (hi_col - lo)
        window = x[:, lo:hi_col]
        acc = mm(window, t_high[first:last]) + mm(window, t_mid[first:last]) + mm(window, t_low[first:last])
        across_ref[0:used, j * 128 : (j + 1) * 128] = acc
    depth = across_ref.shape[0]
    across_ref[used:depth, :] = jnp.zeros((depth - used, width), jnp.float32)
    n_wide = wide_ref.shape[1]
    total = row[0] * across_ref[pl.ds(0, n_wide), :]
    for k in range(1, 7):
        total = total + row[k] * across_ref[pl.ds(k, n_wide), :]
    total = total * keep_wide_ref[...]
    for j in range(tiles):
        wide_ref[j] = total[:, 128 * j : 128 * (j + 1)]
    rows = o0_ref.shape[2]
    for j in range(tiles):
        o0_ref[0, 0, :, 128 * j : 128 * (j + 1)] = wide_ref[j, pl.ds(3, rows), :].astype(o0_ref.dtype)
    n_half = keep_half_ref.shape[0]
    halves = halve_rows(wide_ref, n_half) * keep_half_ref[...]
    down = band_table(512, 128, 127, (2, pyramid_filter)).astype(jnp.bfloat16)
    halve_columns(halves, down, half_ref)
    for j in range(tiles // 2):
        o1_ref[0, 0, :, 128 * j : 128 * (j + 1)] = half_ref[j, pl.ds(1, rows // 2), :].astype(o1_ref.dtype)
    quarters = halve_rows(half_ref, rows // 4)
    halve_columns(quarters, down, quarter_ref)
    for j in range(tiles // 4):
        o2_ref[0, 0, :, 128 * j : 128 * (j + 1)] = quarter_ref[j].astype(o2_ref.dtype)


def pyramid(extended, resample_taps, band_index, total_rows):
    dates, bands, used, width = extended.shape
    rows = used - 16
    n_wide = rows + 24
    n_half = rows // 2 + 8
    depth = n_wide + 8
    keep_wide = inside_rows(n_wide, band_index * rows - 3, rows + 6, total_rows)
    keep_half = inside_rows(n_half, band_index * (rows // 2) - 1, rows // 2 + 2, total_rows // 2)
    out_shape = (
        jax.ShapeDtypeStruct((dates, bands, rows, width), jnp.bfloat16),
        jax.ShapeDtypeStruct((dates, bands, rows // 2, width // 2), jnp.bfloat16),
        jax.ShapeDtypeStruct((dates, bands, rows // 4, width // 4), jnp.bfloat16),
    )
    return pl.pallas_call(
        pyramid_kernel,
        grid=(dates, bands),
        in_specs=[
            pl.BlockSpec(memory_space=pltpu.SMEM),
            pl.BlockSpec((1, 1, used, width), lambda d, b: (d, b, 0, 0)),
            pl.BlockSpec((n_wide, 1), lambda d, b: (0, 0)),
            pl.BlockSpec((n_half, 1), lambda d, b: (0, 0)),
        ],
        out_specs=[
            pl.BlockSpec((1, 1, rows, width), lambda d, b: (d, b, 0, 0)),
            pl.BlockSpec((1, 1, rows // 2, width // 2), lambda d, b: (d, b, 0, 0)),
            pl.BlockSpec((1, 1, rows // 4, width // 4), lambda d, b: (d, b, 0, 0)),
        ],
        out_shape=out_shape,
        scratch_shapes=[
            pltpu.VMEM((depth, width), jnp.float32),
            pltpu.VMEM((width // 128, n_wide, 128), jnp.float32),
            pltpu.VMEM((width // 256, n_half, 128), jnp.float32),
            pltpu.VMEM((width // 512, rows // 4, 128), jnp.float32),
        ],
    )(resample_taps, extended, keep_wide, keep_half)


def smooth(level, clear):
    values = level.astype(jnp.float32)
    dates = values.shape[0]
    clear4 = clear[:, None]
    weight = 0.1 + 0.9 * clear4
    weighted = jnp.pad(weight * values, ((4, 4), (0, 0), (0, 0), (0, 0)))
    weight_pad = jnp.pad(weight, ((4, 4), (0, 0), (0, 0), (0, 0)))
    numer = jnp.zeros_like(values)
    denom = jnp.zeros_like(weight)
    for k in range(9):
        numer = numer + gap_weights[k] * weighted[k : k + dates]
        denom = denom + gap_weights[k] * weight_pad[k : k + dates]
    filled = clear4 * values + (1.0 - clear4) * (numer / denom)
    edged = jnp.pad(filled, ((4, 4), (0, 0), (0, 0), (0, 0)), mode="edge")
    result = jnp.zeros_like(values)
    for k in range(9):
        result = result + savgol_coeffs[k] * edged[k : k + dates]
    return result.astype(jnp.bfloat16)


def expand_mask(clear_mask, row_rep, col_rep):
    grown = jnp.repeat(jnp.repeat(clear_mask, row_rep, axis=1), col_rep, axis=2)
    return grown.astype(jnp.float32)


def expand_mask(clear_mask, row_rep, col_rep):
    grown = jnp.repeat(jnp.repeat(clear_mask, row_rep, axis=1), col_rep, axis=2)
    return grown.astype(jnp.float32)


def local(scenes, resample_taps, clear_mask):
    rows = scenes.shape[2]
    band_index = lax.axis_index("row")
    total_rows = rows * lax.axis_size("row")
    extended = padded(scenes, (("row", 2),), 6)
    extended = jnp.pad(extended, ((0, 0), (0, 0), (0, 4), (0, 0)))
    level_zero, level_one, level_two = pyramid(extended, resample_taps, band_index, total_rows)
    clear_fine = expand_mask(clear_mask, 4, 128)
    clear_half = expand_mask(clear_mask, 2, 64)
    clear_quarter = expand_mask(clear_mask, 1, 32)
    smooth_fine = smooth(
        lax.all_to_all(level_zero, "date", split_axis=2, concat_axis=0, tiled=True), clear_fine
    )
    smooth_half = smooth(
        lax.all_to_all(level_one, "date", split_axis=2, concat_axis=0, tiled=True), clear_half
    )
    smooth_quarter = smooth(
        lax.all_to_all(level_two, "date", split_axis=2, concat_axis=0, tiled=True), clear_quarter
    )
    return (smooth_fine, smooth_half, smooth_quarter)


def solution(mesh):
    in_specs = (P(("groups", "date"), None, "row", None), P(), P("groups", ("row", "date"), None))
    out_specs = (
        P("groups", None, ("row", "date"), None),
        P("groups", None, ("row", "date"), None),
        P("groups", None, ("row", "date"), None),
    )
    return jax.shard_map(local, mesh=mesh, in_specs=in_specs, out_specs=out_specs, check_vma=False)
```

```python
import math

import jax
import jax.numpy as jnp
from jax import lax
from jax.sharding import PartitionSpec as P
from jax.experimental import pallas as pl
from jax.experimental.pallas import tpu as pltpu

gap_weights = [math.exp(-((k - 4) ** 2) / 8.0) for k in range(9)]
savgol_coeffs = [c / 231.0 for c in [-21.0, 14.0, 39.0, 54.0, 59.0, 54.0, 39.0, 14.0, -21.0]]
pyramid_filter = [0.125, 0.375, 0.375, 0.125]


def padded(block, sides, width):
    for axis, dim in sides:
        count = lax.axis_size(axis)
        forward = [(i, i + 1) for i in range(count - 1)]
        backward = [(target, source) for source, target in forward]
        low = lax.ppermute(
            lax.slice_in_dim(block, block.shape[dim] - width, None, axis=dim), axis, forward
        )
        high = lax.ppermute(lax.slice_in_dim(block, 0, width, axis=dim), axis, backward)
        block = jnp.concatenate([low, block, high], axis=dim)
    return block


def inside_rows(count, first, valid, total):
    at = lax.iota(jnp.int32, count)
    places = first + at
    keep = (places >= 0) & (places < total) & (at < valid)
    return keep.astype(jnp.float32)[:, None]


def split_two(a):
    high = a.astype(jnp.bfloat16)
    low = (a - high.astype(jnp.float32)).astype(jnp.bfloat16)
    return high, low


def mm(a, b):
    return jnp.dot(a, b, preferred_element_type=jnp.float32)


def band_table(rows, cols, shift, taps):
    step, weights = taps
    s_at = lax.broadcasted_iota(jnp.int32, (rows, cols), 0)
    c_at = lax.broadcasted_iota(jnp.int32, (rows, cols), 1)
    place = s_at - step * c_at - shift
    total = jnp.zeros((rows, cols), jnp.float32)
    for k, w in enumerate(weights):
        total = total + jnp.where(place == k, w, 0.0)
    return total


def halve_columns(values, table, out_ref):
    width = values.shape[1]
    high, low = split_two(values)
    for j in range(width // 256):
        lo = max(256 * j - 128, 0)
        hi_col = min(256 * j + 384, width)
        first = lo - (256 * j - 128)
        last = first + (hi_col - lo)
        part = table[first:last]
        out_ref[j] = mm(high[:, lo:hi_col], part) + mm(low[:, lo:hi_col], part)


def halve_rows(source_ref, count):
    total = pyramid_filter[0] * source_ref[:, pl.ds(0, count, stride=2), :]
    for p in range(1, 4):
        total = total + pyramid_filter[p] * source_ref[:, pl.ds(p, count, stride=2), :]
    return jnp.concatenate([total[j] for j in range(total.shape[0])], axis=1)


def pyramid_kernel(taps_ref, x_ref, keep_wide_ref, keep_half_ref, o0_ref, o1_ref, o2_ref,
                   across_ref, wide_ref, half_ref, quarter_ref):
    b = pl.program_id(1)
    x = x_ref[0, 0]
    used = x.shape[0]
    width = x.shape[1]
    tiles = width // 128
    column = [taps_ref[0, b, k] for k in range(7)]
    row = [taps_ref[1, b, k] for k in range(7)]
    table = band_table(3 * 128, 128, 125, (1, column))
    t_high = table.astype(jnp.bfloat16)
    rest = table - t_high.astype(jnp.float32)
    t_mid = rest.astype(jnp.bfloat16)
    t_low = (rest - t_mid.astype(jnp.float32)).astype(jnp.bfloat16)
    for j in range(tiles):
        lo = max(j - 1, 0) * 128
        hi_col = min(j + 2, tiles) * 128
        first = lo - (j - 1) * 128
        last = first + (hi_col - lo)
        window = x[:, lo:hi_col]
        acc = mm(window, t_high[first:last]) + mm(window, t_mid[first:last]) + mm(window, t_low[first:last])
        across_ref[0:used, j * 128 : (j + 1) * 128] = acc
    depth = across_ref.shape[0]
    across_ref[used:depth, :] = jnp.zeros((depth - used, width), jnp.float32)
    n_wide = wide_ref.shape[1]
    total = row[0] * across_ref[pl.ds(0, n_wide), :]
    for k in range(1, 7):
        total = total + row[k] * across_ref[pl.ds(k, n_wide), :]
    total = total * keep_wide_ref[...]
    for j in range(tiles):
        wide_ref[j] = total[:, 128 * j : 128 * (j + 1)]
    rows = o0_ref.shape[2]
    for j in range(tiles):
        o0_ref[0, 0, :, 128 * j : 128 * (j + 1)] = wide_ref[j, pl.ds(3, rows), :].astype(o0_ref.dtype)
    n_half = keep_half_ref.shape[0]
    halves = halve_rows(wide_ref, n_half) * keep_half_ref[...]
    down = band_table(512, 128, 127, (2, pyramid_filter)).astype(jnp.bfloat16)
    halve_columns(halves, down, half_ref)
    for j in range(tiles // 2):
        o1_ref[0, 0, :, 128 * j : 128 * (j + 1)] = half_ref[j, pl.ds(1, rows // 2), :].astype(o1_ref.dtype)
    quarters = halve_rows(half_ref, rows // 4)
    halve_columns(quarters, down, quarter_ref)
    for j in range(tiles // 4):
        o2_ref[0, 0, :, 128 * j : 128 * (j + 1)] = quarter_ref[j].astype(o2_ref.dtype)


def pyramid(extended, resample_taps, band_index, total_rows):
    dates, bands, used, width = extended.shape
    rows = used - 16
    n_wide = rows + 24
    n_half = rows // 2 + 8
    depth = n_wide + 8
    keep_wide = inside_rows(n_wide, band_index * rows - 3, rows + 6, total_rows)
    keep_half = inside_rows(n_half, band_index * (rows // 2) - 1, rows // 2 + 2, total_rows // 2)
    out_shape = (
        jax.ShapeDtypeStruct((dates, bands, rows, width), jnp.bfloat16),
        jax.ShapeDtypeStruct((dates, bands, rows // 2, width // 2), jnp.bfloat16),
        jax.ShapeDtypeStruct((dates, bands, rows // 4, width // 4), jnp.bfloat16),
    )
    return pl.pallas_call(
        pyramid_kernel,
        grid=(dates, bands),
        in_specs=[
            pl.BlockSpec(memory_space=pltpu.SMEM),
            pl.BlockSpec((1, 1, used, width), lambda d, b: (d, b, 0, 0)),
            pl.BlockSpec((n_wide, 1), lambda d, b: (0, 0)),
            pl.BlockSpec((n_half, 1), lambda d, b: (0, 0)),
        ],
        out_specs=[
            pl.BlockSpec((1, 1, rows, width), lambda d, b: (d, b, 0, 0)),
            pl.BlockSpec((1, 1, rows // 2, width // 2), lambda d, b: (d, b, 0, 0)),
            pl.BlockSpec((1, 1, rows // 4, width // 4), lambda d, b: (d, b, 0, 0)),
        ],
        out_shape=out_shape,
        scratch_shapes=[
            pltpu.VMEM((depth, width), jnp.float32),
            pltpu.VMEM((width // 128, n_wide, 128), jnp.float32),
            pltpu.VMEM((width // 256, n_half, 128), jnp.float32),
            pltpu.VMEM((width // 512, rows // 4, 128), jnp.float32),
        ],
    )(resample_taps, extended, keep_wide, keep_half)


def smooth(level, clear):
    values = level.astype(jnp.float32)
    dates = values.shape[0]
    clear4 = clear[:, None]
    weight = 0.1 + 0.9 * clear4
    weighted = jnp.pad(weight * values, ((4, 4), (0, 0), (0, 0), (0, 0)))
    weight_pad = jnp.pad(weight, ((4, 4), (0, 0), (0, 0), (0, 0)))
    numer = jnp.zeros_like(values)
    denom = jnp.zeros_like(weight)
    for k in range(9):
        numer = numer + gap_weights[k] * weighted[k : k + dates]
        denom = denom + gap_weights[k] * weight_pad[k : k + dates]
    filled = clear4 * values + (1.0 - clear4) * (numer / denom)
    edged = jnp.pad(filled, ((4, 4), (0, 0), (0, 0), (0, 0)), mode="edge")
    result = jnp.zeros_like(values)
    for k in range(9):
        result = result + savgol_coeffs[k] * edged[k : k + dates]
    return result.astype(jnp.bfloat16)


def expand_mask(clear_mask, row_rep, col_rep):
    grown = jnp.repeat(jnp.repeat(clear_mask, row_rep, axis=1), col_rep, axis=2)
    return grown.astype(jnp.float32)


def expand_mask(clear_mask, row_rep, col_rep):
    grown = jnp.repeat(jnp.repeat(clear_mask, row_rep, axis=1), col_rep, axis=2)
    return grown.astype(jnp.float32)


def local(scenes, resample_taps, clear_mask):
    rows = scenes.shape[2]
    band_index = lax.axis_index("row")
    total_rows = rows * lax.axis_size("row")
    extended = padded(scenes, (("row", 2),), 6)
    extended = jnp.pad(extended, ((0, 0), (0, 0), (0, 4), (0, 0)))
    level_zero, level_one, level_two = pyramid(extended, resample_taps, band_index, total_rows)
    ndate = lax.axis_size("date")
    levels = (level_zero, level_one, level_two)
    pieces = []
    for level in levels:
        dates, bands, count, width = level.shape
        block = level.reshape(dates, bands, ndate, count // ndate, width)
        pieces.append(jnp.moveaxis(block, 2, 0).reshape(ndate, dates, bands, -1))
    packed = jnp.concatenate(pieces, axis=3)
    got = lax.all_to_all(packed, "date", split_axis=0, concat_axis=0, tiled=True)
    masks = (
        expand_mask(clear_mask, 4, 128),
        expand_mask(clear_mask, 2, 64),
        expand_mask(clear_mask, 1, 32),
    )
    outs = []
    start = 0
    for level, piece, clear in zip(levels, pieces, masks):
        dates, bands, count, width = level.shape
        size = piece.shape[3]
        part = got[:, :, :, start : start + size].reshape(ndate * dates, bands, count // ndate, width)
        start += size
        outs.append(smooth(part, clear))
    return tuple(outs)


def solution(mesh):
    in_specs = (P(("groups", "date"), None, "row", None), P(), P("groups", ("row", "date"), None))
    out_specs = (
        P("groups", None, ("row", "date"), None),
        P("groups", None, ("row", "date"), None),
        P("groups", None, ("row", "date"), None),
    )
    return jax.shard_map(local, mesh=mesh, in_specs=in_specs, out_specs=out_specs, check_vma=False)
```

```python
import math

import jax
import numpy as np
import jax.numpy as jnp
from jax import lax
from jax.sharding import PartitionSpec as P
from jax.experimental import pallas as pl
from jax.experimental.pallas import tpu as pltpu

gap_weights = [math.exp(-((k - 4) ** 2) / 8.0) for k in range(9)]
savgol_coeffs = [c / 231.0 for c in [-21.0, 14.0, 39.0, 54.0, 59.0, 54.0, 39.0, 14.0, -21.0]]
pyramid_filter = [0.125, 0.375, 0.375, 0.125]


def padded(block, sides, width):
    for axis, dim in sides:
        count = lax.axis_size(axis)
        forward = [(i, i + 1) for i in range(count - 1)]
        backward = [(target, source) for source, target in forward]
        low = lax.ppermute(
            lax.slice_in_dim(block, block.shape[dim] - width, None, axis=dim), axis, forward
        )
        high = lax.ppermute(lax.slice_in_dim(block, 0, width, axis=dim), axis, backward)
        block = jnp.concatenate([low, block, high], axis=dim)
    return block


def inside_rows(count, first, valid, total):
    at = lax.iota(jnp.int32, count)
    places = first + at
    keep = (places >= 0) & (places < total) & (at < valid)
    return keep.astype(jnp.float32)[:, None]


def split_two(a):
    high = a.astype(jnp.bfloat16)
    low = (a - high.astype(jnp.float32)).astype(jnp.bfloat16)
    return high, low


def mm(a, b):
    return jnp.dot(a, b, preferred_element_type=jnp.float32)


def band_table(rows, cols, shift, taps):
    step, weights = taps
    s_at = lax.broadcasted_iota(jnp.int32, (rows, cols), 0)
    c_at = lax.broadcasted_iota(jnp.int32, (rows, cols), 1)
    place = s_at - step * c_at - shift
    total = jnp.zeros((rows, cols), jnp.float32)
    for k, w in enumerate(weights):
        total = total + jnp.where(place == k, w, 0.0)
    return total


def halve_columns(values, table, out_ref):
    width = values.shape[1]
    high, low = split_two(values)
    for j in range(width // 256):
        lo = max(256 * j - 128, 0)
        hi_col = min(256 * j + 384, width)
        first = lo - (256 * j - 128)
        last = first + (hi_col - lo)
        part = table[first:last]
        out_ref[j] = mm(high[:, lo:hi_col], part) + mm(low[:, lo:hi_col], part)


def halve_rows(source_ref, count):
    total = pyramid_filter[0] * source_ref[:, pl.ds(0, count, stride=2), :]
    for p in range(1, 4):
        total = total + pyramid_filter[p] * source_ref[:, pl.ds(p, count, stride=2), :]
    return jnp.concatenate([total[j] for j in range(total.shape[0])], axis=1)


def pyramid_kernel(taps_ref, x_ref, keep_wide_ref, keep_half_ref, o0_ref, o1_ref, o2_ref,
                   across_ref, wide_ref, half_ref, quarter_ref):
    b = pl.program_id(1)
    x = x_ref[0, 0]
    used = x.shape[0]
    width = x.shape[1]
    tiles = width // 128
    column = [taps_ref[0, b, k] for k in range(7)]
    row = [taps_ref[1, b, k] for k in range(7)]
    table = band_table(3 * 128, 128, 125, (1, column))
    t_high = table.astype(jnp.bfloat16)
    rest = table - t_high.astype(jnp.float32)
    t_mid = rest.astype(jnp.bfloat16)
    t_low = (rest - t_mid.astype(jnp.float32)).astype(jnp.bfloat16)
    for j in range(tiles):
        lo = max(j - 1, 0) * 128
        hi_col = min(j + 2, tiles) * 128
        first = lo - (j - 1) * 128
        last = first + (hi_col - lo)
        window = x[:, lo:hi_col]
        acc = mm(window, t_high[first:last]) + mm(window, t_mid[first:last]) + mm(window, t_low[first:last])
        across_ref[0:used, j * 128 : (j + 1) * 128] = acc
    depth = across_ref.shape[0]
    across_ref[used:depth, :] = jnp.zeros((depth - used, width), jnp.float32)
    n_wide = wide_ref.shape[1]
    total = row[0] * across_ref[pl.ds(0, n_wide), :]
    for k in range(1, 7):
        total = total + row[k] * across_ref[pl.ds(k, n_wide), :]
    total = total * keep_wide_ref[...]
    for j in range(tiles):
        wide_ref[j] = total[:, 128 * j : 128 * (j + 1)]
    rows = o0_ref.shape[2]
    for j in range(tiles):
        o0_ref[0, 0, :, 128 * j : 128 * (j + 1)] = wide_ref[j, pl.ds(3, rows), :].astype(o0_ref.dtype)
    n_half = keep_half_ref.shape[0]
    halves = halve_rows(wide_ref, n_half) * keep_half_ref[...]
    down = band_table(512, 128, 127, (2, pyramid_filter)).astype(jnp.bfloat16)
    halve_columns(halves, down, half_ref)
    for j in range(tiles // 2):
        o1_ref[0, 0, :, 128 * j : 128 * (j + 1)] = half_ref[j, pl.ds(1, rows // 2), :].astype(o1_ref.dtype)
    quarters = halve_rows(half_ref, rows // 4)
    halve_columns(quarters, down, quarter_ref)
    for j in range(tiles // 4):
        o2_ref[0, 0, :, 128 * j : 128 * (j + 1)] = quarter_ref[j].astype(o2_ref.dtype)


def pyramid(extended, resample_taps, band_index, total_rows):
    dates, bands, used, width = extended.shape
    rows = used - 16
    n_wide = rows + 24
    n_half = rows // 2 + 8
    depth = n_wide + 8
    keep_wide = inside_rows(n_wide, band_index * rows - 3, rows + 6, total_rows)
    keep_half = inside_rows(n_half, band_index * (rows // 2) - 1, rows // 2 + 2, total_rows // 2)
    out_shape = (
        jax.ShapeDtypeStruct((dates, bands, rows, width), jnp.bfloat16),
        jax.ShapeDtypeStruct((dates, bands, rows // 2, width // 2), jnp.bfloat16),
        jax.ShapeDtypeStruct((dates, bands, rows // 4, width // 4), jnp.bfloat16),
    )
    return pl.pallas_call(
        pyramid_kernel,
        grid=(dates, bands),
        in_specs=[
            pl.BlockSpec(memory_space=pltpu.SMEM),
            pl.BlockSpec((1, 1, used, width), lambda d, b: (d, b, 0, 0)),
            pl.BlockSpec((n_wide, 1), lambda d, b: (0, 0)),
            pl.BlockSpec((n_half, 1), lambda d, b: (0, 0)),
        ],
        out_specs=[
            pl.BlockSpec((1, 1, rows, width), lambda d, b: (d, b, 0, 0)),
            pl.BlockSpec((1, 1, rows // 2, width // 2), lambda d, b: (d, b, 0, 0)),
            pl.BlockSpec((1, 1, rows // 4, width // 4), lambda d, b: (d, b, 0, 0)),
        ],
        out_shape=out_shape,
        scratch_shapes=[
            pltpu.VMEM((depth, width), jnp.float32),
            pltpu.VMEM((width // 128, n_wide, 128), jnp.float32),
            pltpu.VMEM((width // 256, n_half, 128), jnp.float32),
            pltpu.VMEM((width // 512, rows // 4, 128), jnp.float32),
        ],
    )(resample_taps, extended, keep_wide, keep_half)


def smooth_operator(dates):
    clamp = np.zeros((dates, dates), np.float64)
    near = np.zeros((dates, dates), np.float64)
    for t in range(dates):
        for k in range(9):
            clamp[t, min(max(t + k - 4, 0), dates - 1)] += savgol_coeffs[k]
            if 0 <= t + k - 4 < dates:
                near[t, t + k - 4] = gap_weights[k]
    return clamp.astype(np.float32), near.astype(np.float32)


def smooth_coefficients(clear):
    dates = clear.shape[0]
    clamp, near = smooth_operator(dates)
    hi = lax.Precision.HIGHEST
    weight = 0.1 + 0.9 * clear
    denom = jnp.einsum("su,uxy->sxy", near, weight, precision=hi)
    gap = (1.0 - clear) / denom
    fill = near[:, :, None, None] * weight[None, :] * gap[:, None]
    fill = fill + np.eye(dates, dtype=np.float32)[:, :, None, None] * clear[None, :]
    return jnp.einsum("ts,suxy->tuxy", clamp, fill, precision=hi)


def smooth_kernel(level_ref, coeff_ref, out_ref):
    dates = level_ref.shape[0]
    rows = level_ref.shape[2]
    width = level_ref.shape[3]
    mask_cols = coeff_ref.shape[3]
    span = width // mask_cols
    per_tile = 128 // span
    lane_group = lax.broadcasted_iota(jnp.int32, (rows, 128), 1) // span
    for j in range(width // 128):
        values = [level_ref[u, 0, :, 128 * j : 128 * (j + 1)].astype(jnp.float32) for u in range(dates)]

        def one_date(t, carry):
            acc = jnp.zeros((rows, 128), jnp.float32)
            for u in range(dates):
                c = coeff_ref[t, u]
                tile = jnp.broadcast_to(c[:, per_tile * j : per_tile * j + 1], (rows, 128))
                for g in range(1, per_tile):
                    m = per_tile * j + g
                    tile = jnp.where(lane_group == g, jnp.broadcast_to(c[:, m : m + 1], (rows, 128)), tile)
                acc = acc + tile * values[u]
            out_ref[t, 0, :, 128 * j : 128 * (j + 1)] = acc.astype(out_ref.dtype)
            return carry

        lax.fori_loop(0, dates, one_date, 0)


def smooth(level, coeff):
    dates, bands, rows, width = level.shape
    grown = jnp.repeat(coeff, rows // coeff.shape[2], axis=2)
    return pl.pallas_call(
        smooth_kernel,
        grid=(bands,),
        in_specs=[
            pl.BlockSpec((dates, 1, rows, width), lambda b: (0, b, 0, 0)),
            pl.BlockSpec(grown.shape, lambda b: (0, 0, 0, 0)),
        ],
        out_specs=pl.BlockSpec((dates, 1, rows, width), lambda b: (0, b, 0, 0)),
        out_shape=jax.ShapeDtypeStruct(level.shape, jnp.bfloat16),
    )(level, grown)


def local(scenes, resample_taps, clear_mask):
    rows = scenes.shape[2]
    band_index = lax.axis_index("row")
    total_rows = rows * lax.axis_size("row")
    extended = padded(scenes, (("row", 2),), 6)
    extended = jnp.pad(extended, ((0, 0), (0, 0), (0, 4), (0, 0)))
    levels = pyramid(extended, resample_taps, band_index, total_rows)
    coeff = smooth_coefficients(clear_mask.astype(jnp.float32))
    return tuple(
        smooth(lax.all_to_all(level, "date", split_axis=2, concat_axis=0, tiled=True), coeff)
        for level in levels
    )


def solution(mesh):
    in_specs = (P(("groups", "date"), None, "row", None), P(), P("groups", ("row", "date"), None))
    out_specs = (
        P("groups", None, ("row", "date"), None),
        P("groups", None, ("row", "date"), None),
        P("groups", None, ("row", "date"), None),
    )
    return jax.shard_map(local, mesh=mesh, in_specs=in_specs, out_specs=out_specs, check_vma=False)
```

```python
import math

import jax
import numpy as np
import jax.numpy as jnp
from jax import lax
from jax.sharding import PartitionSpec as P
from jax.experimental import pallas as pl
from jax.experimental.pallas import tpu as pltpu

gap_weights = [math.exp(-((k - 4) ** 2) / 8.0) for k in range(9)]
savgol_coeffs = [c / 231.0 for c in [-21.0, 14.0, 39.0, 54.0, 59.0, 54.0, 39.0, 14.0, -21.0]]
pyramid_filter = [0.125, 0.375, 0.375, 0.125]


def padded(block, sides, width):
    for axis, dim in sides:
        count = lax.axis_size(axis)
        forward = [(i, i + 1) for i in range(count - 1)]
        backward = [(target, source) for source, target in forward]
        low = lax.ppermute(
            lax.slice_in_dim(block, block.shape[dim] - width, None, axis=dim), axis, forward
        )
        high = lax.ppermute(lax.slice_in_dim(block, 0, width, axis=dim), axis, backward)
        block = jnp.concatenate([low, block, high], axis=dim)
    return block


def inside_rows(count, first, valid, total):
    at = lax.iota(jnp.int32, count)
    places = first + at
    keep = (places >= 0) & (places < total) & (at < valid)
    return keep.astype(jnp.float32)[:, None]


def split_two(a):
    high = a.astype(jnp.bfloat16)
    low = (a - high.astype(jnp.float32)).astype(jnp.bfloat16)
    return high, low


def mm(a, b):
    return jnp.dot(a, b, preferred_element_type=jnp.float32)


def band_table(rows, cols, shift, taps):
    step, weights = taps
    s_at = lax.broadcasted_iota(jnp.int32, (rows, cols), 0)
    c_at = lax.broadcasted_iota(jnp.int32, (rows, cols), 1)
    place = s_at - step * c_at - shift
    total = jnp.zeros((rows, cols), jnp.float32)
    for k, w in enumerate(weights):
        total = total + jnp.where(place == k, w, 0.0)
    return total


def halve_columns(values, table, out_ref):
    width = values.shape[1]
    high, low = split_two(values)
    for j in range(width // 256):
        lo = max(256 * j - 128, 0)
        hi_col = min(256 * j + 384, width)
        first = lo - (256 * j - 128)
        last = first + (hi_col - lo)
        part = table[first:last]
        out_ref[j] = mm(high[:, lo:hi_col], part) + mm(low[:, lo:hi_col], part)


def halve_rows(source_ref, count):
    total = pyramid_filter[0] * source_ref[:, pl.ds(0, count, stride=2), :]
    for p in range(1, 4):
        total = total + pyramid_filter[p] * source_ref[:, pl.ds(p, count, stride=2), :]
    return jnp.concatenate([total[j] for j in range(total.shape[0])], axis=1)


def pyramid_kernel(taps_ref, x_ref, keep_wide_ref, keep_half_ref, o0_ref, o1_ref, o2_ref,
                   across_ref, wide_ref, half_ref, quarter_ref):
    b = pl.program_id(1)
    x = x_ref[0, 0]
    used = x.shape[0]
    width = x.shape[1]
    tiles = width // 128
    column = [taps_ref[0, b, k] for k in range(7)]
    row = [taps_ref[1, b, k] for k in range(7)]
    table = band_table(3 * 128, 128, 125, (1, column))
    t_high = table.astype(jnp.bfloat16)
    rest = table - t_high.astype(jnp.float32)
    t_mid = rest.astype(jnp.bfloat16)
    t_low = (rest - t_mid.astype(jnp.float32)).astype(jnp.bfloat16)
    for j in range(tiles):
        lo = max(j - 1, 0) * 128
        hi_col = min(j + 2, tiles) * 128
        first = lo - (j - 1) * 128
        last = first + (hi_col - lo)
        window = x[:, lo:hi_col]
        acc = mm(window, t_high[first:last]) + mm(window, t_mid[first:last]) + mm(window, t_low[first:last])
        across_ref[0:used, j * 128 : (j + 1) * 128] = acc
    depth = across_ref.shape[0]
    across_ref[used:depth, :] = jnp.zeros((depth - used, width), jnp.float32)
    n_wide = wide_ref.shape[1]
    total = row[0] * across_ref[pl.ds(0, n_wide), :]
    for k in range(1, 7):
        total = total + row[k] * across_ref[pl.ds(k, n_wide), :]
    total = total * keep_wide_ref[...]
    for j in range(tiles):
        wide_ref[j] = total[:, 128 * j : 128 * (j + 1)]
    rows = o0_ref.shape[2]
    for j in range(tiles):
        o0_ref[0, 0, :, 128 * j : 128 * (j + 1)] = wide_ref[j, pl.ds(3, rows), :].astype(o0_ref.dtype)
    n_half = keep_half_ref.shape[0]
    halves = halve_rows(wide_ref, n_half) * keep_half_ref[...]
    down = band_table(512, 128, 127, (2, pyramid_filter)).astype(jnp.bfloat16)
    halve_columns(halves, down, half_ref)
    for j in range(tiles // 2):
        o1_ref[0, 0, :, 128 * j : 128 * (j + 1)] = half_ref[j, pl.ds(1, rows // 2), :].astype(o1_ref.dtype)
    quarters = halve_rows(half_ref, rows // 4)
    halve_columns(quarters, down, quarter_ref)
    for j in range(tiles // 4):
        o2_ref[0, 0, :, 128 * j : 128 * (j + 1)] = quarter_ref[j].astype(o2_ref.dtype)


def pyramid(extended, resample_taps, band_index, total_rows):
    dates, bands, used, width = extended.shape
    rows = used - 16
    n_wide = rows + 24
    n_half = rows // 2 + 8
    depth = n_wide + 8
    keep_wide = inside_rows(n_wide, band_index * rows - 3, rows + 6, total_rows)
    keep_half = inside_rows(n_half, band_index * (rows // 2) - 1, rows // 2 + 2, total_rows // 2)
    out_shape = (
        jax.ShapeDtypeStruct((dates, bands, rows, width), jnp.bfloat16),
        jax.ShapeDtypeStruct((dates, bands, rows // 2, width // 2), jnp.bfloat16),
        jax.ShapeDtypeStruct((dates, bands, rows // 4, width // 4), jnp.bfloat16),
    )
    return pl.pallas_call(
        pyramid_kernel,
        grid=(dates, bands),
        in_specs=[
            pl.BlockSpec(memory_space=pltpu.SMEM),
            pl.BlockSpec((1, 1, used, width), lambda d, b: (d, b, 0, 0)),
            pl.BlockSpec((n_wide, 1), lambda d, b: (0, 0)),
            pl.BlockSpec((n_half, 1), lambda d, b: (0, 0)),
        ],
        out_specs=[
            pl.BlockSpec((1, 1, rows, width), lambda d, b: (d, b, 0, 0)),
            pl.BlockSpec((1, 1, rows // 2, width // 2), lambda d, b: (d, b, 0, 0)),
            pl.BlockSpec((1, 1, rows // 4, width // 4), lambda d, b: (d, b, 0, 0)),
        ],
        out_shape=out_shape,
        scratch_shapes=[
            pltpu.VMEM((depth, width), jnp.float32),
            pltpu.VMEM((width // 128, n_wide, 128), jnp.float32),
            pltpu.VMEM((width // 256, n_half, 128), jnp.float32),
            pltpu.VMEM((width // 512, rows // 4, 128), jnp.float32),
        ],
    )(resample_taps, extended, keep_wide, keep_half)


def smooth_operator(dates):
    clamp = np.zeros((dates, dates), np.float64)
    near = np.zeros((dates, dates), np.float64)
    for t in range(dates):
        for k in range(9):
            clamp[t, min(max(t + k - 4, 0), dates - 1)] += savgol_coeffs[k]
            if 0 <= t + k - 4 < dates:
                near[t, t + k - 4] = gap_weights[k]
    return clamp.astype(np.float32), near.astype(np.float32)


def smooth_coefficients(clear):
    dates = clear.shape[0]
    clamp, near = smooth_operator(dates)
    hi = lax.Precision.HIGHEST
    weight = 0.1 + 0.9 * clear
    denom = jnp.einsum("su,uxy->sxy", near, weight, precision=hi)
    gap = (1.0 - clear) / denom
    fill = near[:, :, None, None] * weight[None, :] * gap[:, None]
    fill = fill + np.eye(dates, dtype=np.float32)[:, :, None, None] * clear[None, :]
    return jnp.einsum("ts,suxy->tuxy", clamp, fill, precision=hi)


def smooth_kernel(level_ref, coeff_ref, out_ref, values_ref):
    dates, bands, rows, width = level_ref.shape
    mask_cols = coeff_ref.shape[3]
    span = width // mask_cols
    per_tile = 128 // span
    lane_group = lax.broadcasted_iota(jnp.int32, (rows, 128), 1) // span
    for j in range(width // 128):
        values_ref[...] = level_ref[:, :, :, 128 * j : 128 * (j + 1)].astype(jnp.float32)

        def one_date(t, carry):
            tiles = []
            for u in range(dates):
                c = coeff_ref[t, u]
                tile = jnp.broadcast_to(c[:, per_tile * j : per_tile * j + 1], (rows, 128))
                for g in range(1, per_tile):
                    m = per_tile * j + g
                    tile = jnp.where(lane_group == g, jnp.broadcast_to(c[:, m : m + 1], (rows, 128)), tile)
                tiles.append(tile)
            for band in range(bands):
                acc = tiles[0] * values_ref[0, band]
                for u in range(1, dates):
                    acc = acc + tiles[u] * values_ref[u, band]
                out_ref[t, band, :, 128 * j : 128 * (j + 1)] = acc.astype(out_ref.dtype)
            return carry

        lax.fori_loop(0, dates, one_date, 0)


def smooth(level, coeff):
    dates, bands, rows, width = level.shape
    grown = jnp.repeat(coeff, rows // coeff.shape[2], axis=2)
    return pl.pallas_call(
        smooth_kernel,
        in_specs=[
            pl.BlockSpec(level.shape, lambda: (0, 0, 0, 0)),
            pl.BlockSpec(grown.shape, lambda: (0, 0, 0, 0)),
        ],
        out_specs=pl.BlockSpec(level.shape, lambda: (0, 0, 0, 0)),
        out_shape=jax.ShapeDtypeStruct(level.shape, jnp.bfloat16),
        scratch_shapes=[pltpu.VMEM((dates, bands, rows, 128), jnp.float32)],
    )(level, grown)


def local(scenes, resample_taps, clear_mask):
    rows = scenes.shape[2]
    band_index = lax.axis_index("row")
    total_rows = rows * lax.axis_size("row")
    extended = padded(scenes, (("row", 2),), 6)
    extended = jnp.pad(extended, ((0, 0), (0, 0), (0, 4), (0, 0)))
    levels = pyramid(extended, resample_taps, band_index, total_rows)
    coeff = smooth_coefficients(clear_mask.astype(jnp.float32))
    return tuple(
        smooth(lax.all_to_all(level, "date", split_axis=2, concat_axis=0, tiled=True), coeff)
        for level in levels
    )


def solution(mesh):
    in_specs = (P(("groups", "date"), None, "row", None), P(), P("groups", ("row", "date"), None))
    out_specs = (
        P("groups", None, ("row", "date"), None),
        P("groups", None, ("row", "date"), None),
        P("groups", None, ("row", "date"), None),
    )
    return jax.shard_map(local, mesh=mesh, in_specs=in_specs, out_specs=out_specs, check_vma=False)
```

```python
import functools
import math

import jax
import numpy as np
import jax.numpy as jnp
from jax import lax
from jax.sharding import PartitionSpec as P
from jax.experimental import pallas as pl
from jax.experimental.pallas import tpu as pltpu

gap_weights = [math.exp(-((k - 4) ** 2) / 8.0) for k in range(9)]
savgol_coeffs = [c / 231.0 for c in [-21.0, 14.0, 39.0, 54.0, 59.0, 54.0, 39.0, 14.0, -21.0]]
pyramid_filter = [0.125, 0.375, 0.375, 0.125]


def padded(block, sides, width):
    for axis, dim in sides:
        count = lax.axis_size(axis)
        forward = [(i, i + 1) for i in range(count - 1)]
        backward = [(target, source) for source, target in forward]
        low = lax.ppermute(
            lax.slice_in_dim(block, block.shape[dim] - width, None, axis=dim), axis, forward
        )
        high = lax.ppermute(lax.slice_in_dim(block, 0, width, axis=dim), axis, backward)
        block = jnp.concatenate([low, block, high], axis=dim)
    return block


def inside_rows(count, first, valid, total):
    at = lax.iota(jnp.int32, count)
    places = first + at
    keep = (places >= 0) & (places < total) & (at < valid)
    return keep.astype(jnp.float32)[:, None]


def split_two(a):
    high = a.astype(jnp.bfloat16)
    low = (a - high.astype(jnp.float32)).astype(jnp.bfloat16)
    return high, low


def mm(a, b):
    return jnp.dot(a, b, preferred_element_type=jnp.float32)


def band_table(rows, cols, shift, taps):
    step, weights = taps
    s_at = lax.broadcasted_iota(jnp.int32, (rows, cols), 0)
    c_at = lax.broadcasted_iota(jnp.int32, (rows, cols), 1)
    place = s_at - step * c_at - shift
    total = jnp.zeros((rows, cols), jnp.float32)
    for k, w in enumerate(weights):
        total = total + jnp.where(place == k, w, 0.0)
    return total


def halve_columns(values, table, out_ref):
    width = values.shape[1]
    high, low = split_two(values)
    for j in range(width // 256):
        lo = max(256 * j - 128, 0)
        hi_col = min(256 * j + 384, width)
        first = lo - (256 * j - 128)
        last = first + (hi_col - lo)
        part = table[first:last]
        out_ref[j, 0 : values.shape[0]] = mm(high[:, lo:hi_col], part) + mm(low[:, lo:hi_col], part)


def halve_rows(source_ref, count):
    total = pyramid_filter[0] * source_ref[:, pl.ds(0, count, stride=2), :]
    for p in range(1, 4):
        total = total + pyramid_filter[p] * source_ref[:, pl.ds(p, count, stride=2), :]
    return jnp.concatenate([total[j] for j in range(total.shape[0])], axis=1)


def piece_rows(rows, ndate):
    fine = rows // ndate
    return (fine, max(fine // 2, 8), max(fine // 4, 8))


def pyramid_kernel(ndate, taps_ref, x_ref, keep_wide_ref, keep_half_ref, packed_ref,
                   across_ref, wide_ref, half_ref, quarter_ref):
    b = pl.program_id(1)
    x = x_ref[0, 0]
    used = x.shape[0]
    width = x.shape[1]
    tiles = width // 128
    rows = used - 16
    column = [taps_ref[0, b, k] for k in range(7)]
    row = [taps_ref[1, b, k] for k in range(7)]
    table = band_table(3 * 128, 128, 125, (1, column))
    t_high = table.astype(jnp.bfloat16)
    rest = table - t_high.astype(jnp.float32)
    t_mid = rest.astype(jnp.bfloat16)
    t_low = (rest - t_mid.astype(jnp.float32)).astype(jnp.bfloat16)
    for j in range(tiles):
        lo = max(j - 1, 0) * 128
        hi_col = min(j + 2, tiles) * 128
        first = lo - (j - 1) * 128
        last = first + (hi_col - lo)
        window = x[:, lo:hi_col]
        acc = mm(window, t_high[first:last]) + mm(window, t_mid[first:last]) + mm(window, t_low[first:last])
        across_ref[0:used, j * 128 : (j + 1) * 128] = acc
    depth = across_ref.shape[0]
    across_ref[used:depth, :] = jnp.zeros((depth - used, width), jnp.float32)
    n_wide = wide_ref.shape[1]
    total = row[0] * across_ref[pl.ds(0, n_wide), :]
    for k in range(1, 7):
        total = total + row[k] * across_ref[pl.ds(k, n_wide), :]
    total = total * keep_wide_ref[...]
    for j in range(tiles):
        wide_ref[j] = total[:, 128 * j : 128 * (j + 1)]
    n_half = keep_half_ref.shape[0]
    halves = halve_rows(wide_ref, n_half) * keep_half_ref[...]
    down = band_table(512, 128, 127, (2, pyramid_filter)).astype(jnp.bfloat16)
    halve_columns(halves, down, half_ref)
    quarters = halve_rows(half_ref, rows // 4)
    n_quarter = quarter_ref.shape[1]
    quarter_ref[:, rows // 4 : n_quarter, :] = jnp.zeros((tiles // 4, n_quarter - rows // 4, 128), jnp.float32)
    halve_columns(quarters, down, quarter_ref)
    fine, p_half, p_quarter = piece_rows(rows, ndate)
    for q in range(ndate):
        parts = [wide_ref[j, pl.ds(3 + fine * q, fine), :] for j in range(tiles)]
        parts += [half_ref[j, pl.ds(1 + (fine // 2) * q, p_half), :] for j in range(tiles // 2)]
        parts += [quarter_ref[j, pl.ds((fine // 4) * q, p_quarter), :] for j in range(tiles // 4)]
        packed_ref[q, 0, 0] = jnp.concatenate(parts, axis=0).astype(packed_ref.dtype)


def pyramid(extended, resample_taps, band_index, total_rows, ndate):
    dates, bands, used, width = extended.shape
    rows = used - 16
    n_wide = rows + 24
    n_half = rows // 2 + 8
    depth = n_wide + 8
    fine, p_half, p_quarter = piece_rows(rows, ndate)
    count = (width // 128) * fine + (width // 256) * p_half + (width // 512) * p_quarter
    keep_wide = inside_rows(n_wide, band_index * rows - 3, rows + 6, total_rows)
    keep_half = inside_rows(n_half, band_index * (rows // 2) - 1, rows // 2 + 2, total_rows // 2)
    return pl.pallas_call(
        functools.partial(pyramid_kernel, ndate),
        grid=(dates, bands),
        in_specs=[
            pl.BlockSpec(memory_space=pltpu.SMEM),
            pl.BlockSpec((1, 1, used, width), lambda d, b: (d, b, 0, 0)),
            pl.BlockSpec((n_wide, 1), lambda d, b: (0, 0)),
            pl.BlockSpec((n_half, 1), lambda d, b: (0, 0)),
        ],
        out_specs=pl.BlockSpec((ndate, 1, 1, count, 128), lambda d, b: (0, d, b, 0, 0)),
        out_shape=jax.ShapeDtypeStruct((ndate, dates, bands, count, 128), jnp.bfloat16),
        scratch_shapes=[
            pltpu.VMEM((depth, width), jnp.float32),
            pltpu.VMEM((width // 128, n_wide, 128), jnp.float32),
            pltpu.VMEM((width // 256, n_half, 128), jnp.float32),
            pltpu.VMEM((width // 512, rows // 4 + 8, 128), jnp.float32),
        ],
    )(resample_taps, extended, keep_wide, keep_half)


def smooth_operator(dates):
    clamp = np.zeros((dates, dates), np.float64)
    near = np.zeros((dates, dates), np.float64)
    for t in range(dates):
        for k in range(9):
            clamp[t, min(max(t + k - 4, 0), dates - 1)] += savgol_coeffs[k]
            if 0 <= t + k - 4 < dates:
                near[t, t + k - 4] = gap_weights[k]
    return clamp.astype(np.float32), near.astype(np.float32)


def smooth_coefficients(clear):
    dates = clear.shape[0]
    clamp, near = smooth_operator(dates)
    hi = lax.Precision.HIGHEST
    weight = 0.1 + 0.9 * clear
    denom = jnp.einsum("su,uxy->sxy", near, weight, precision=hi)
    gap = (1.0 - clear) / denom
    fill = near[:, :, None, None] * weight[None, :] * gap[:, None]
    fill = fill + np.eye(dates, dtype=np.float32)[:, :, None, None] * clear[None, :]
    return jnp.einsum("ts,suxy->tuxy", clamp, fill, precision=hi)


def smooth_level(got_ref, start, piece, coeff_ref, out_ref, section_ref):
    dates, bands, rows, width = out_ref.shape
    tiles = width // 128
    mask_cols = coeff_ref.shape[3]
    span = width // mask_cols
    per_tile = 128 // span
    lane_group = lax.broadcasted_iota(jnp.int32, (rows, 128), 1) // span
    section_ref[...] = got_ref[:, :, start : start + tiles * piece, :].astype(jnp.float32)
    for j in range(tiles):

        def one_date(t, carry):
            coeffs = []
            for u in range(dates):
                c = coeff_ref[t, u]
                tile = jnp.broadcast_to(c[:, per_tile * j : per_tile * j + 1], (rows, 128))
                for g in range(1, per_tile):
                    m = per_tile * j + g
                    tile = jnp.where(lane_group == g, jnp.broadcast_to(c[:, m : m + 1], (rows, 128)), tile)
                coeffs.append(tile)
            for band in range(bands):
                acc = coeffs[0] * section_ref[0, band, j * piece : j * piece + rows, :]
                for u in range(1, dates):
                    acc = acc + coeffs[u] * section_ref[u, band, j * piece : j * piece + rows, :]
                out_ref[t, band, :, 128 * j : 128 * (j + 1)] = acc.astype(out_ref.dtype)
            return carry

        lax.fori_loop(0, dates, one_date, 0)


def smooth_kernel(pieces, got_ref, c0_ref, c1_ref, c2_ref, o0_ref, o1_ref, o2_ref, s0_ref, s1_ref, s2_ref):
    start = 0
    for piece, c_ref, o_ref, s_ref in zip(pieces, (c0_ref, c1_ref, c2_ref), (o0_ref, o1_ref, o2_ref), (s0_ref, s1_ref, s2_ref)):
        smooth_level(got_ref, start, piece, c_ref, o_ref, s_ref)
        start += (o_ref.shape[3] // 128) * piece


def smooth_all(got, coeff, shapes, pieces):
    dates, bands = got.shape[:2]
    grown = [jnp.repeat(coeff, shape[2] // coeff.shape[2], axis=2) for shape in shapes]
    full = lambda a: pl.BlockSpec(a.shape, lambda: (0,) * len(a.shape))
    outs = [jax.ShapeDtypeStruct(shape, jnp.bfloat16) for shape in shapes]
    return pl.pallas_call(
        functools.partial(smooth_kernel, pieces),
        in_specs=[full(got)] + [full(g) for g in grown],
        out_specs=[full(o) for o in outs],
        out_shape=outs,
        scratch_shapes=[
            pltpu.VMEM((dates, bands, (shape[3] // 128) * piece, 128), jnp.float32)
            for shape, piece in zip(shapes, pieces)
        ],
    )(got, *grown)


def local(scenes, resample_taps, clear_mask):
    dates, bands, rows, width = scenes.shape
    band_index = lax.axis_index("row")
    total_rows = rows * lax.axis_size("row")
    ndate = lax.axis_size("date")
    extended = padded(scenes, (("row", 2),), 6)
    extended = jnp.pad(extended, ((0, 0), (0, 0), (0, 4), (0, 0)))
    packed = pyramid(extended, resample_taps, band_index, total_rows, ndate)
    coeff = smooth_coefficients(clear_mask.astype(jnp.float32))
    got = lax.all_to_all(packed, "date", split_axis=0, concat_axis=0, tiled=True)
    got = got.reshape((ndate * dates,) + got.shape[2:])
    fine = rows // ndate
    total = ndate * dates
    shapes = (
        (total, bands, fine, width),
        (total, bands, fine // 2, width // 2),
        (total, bands, fine // 4, width // 4),
    )
    return tuple(smooth_all(got, coeff, shapes, piece_rows(rows, ndate)))


def solution(mesh):
    in_specs = (P(("groups", "date"), None, "row", None), P(), P("groups", ("row", "date"), None))
    out_specs = (
        P("groups", None, ("row", "date"), None),
        P("groups", None, ("row", "date"), None),
        P("groups", None, ("row", "date"), None),
    )
    return jax.shard_map(local, mesh=mesh, in_specs=in_specs, out_specs=out_specs, check_vma=False)
```

```python
import functools
import math

import jax
import numpy as np
import jax.numpy as jnp
from jax import lax
from jax.sharding import PartitionSpec as P
from jax.experimental import pallas as pl
from jax.experimental.pallas import tpu as pltpu

gap_weights = [math.exp(-((k - 4) ** 2) / 8.0) for k in range(9)]
savgol_coeffs = [c / 231.0 for c in [-21.0, 14.0, 39.0, 54.0, 59.0, 54.0, 39.0, 14.0, -21.0]]
pyramid_filter = [0.125, 0.375, 0.375, 0.125]


def padded(block, sides, width):
    for axis, dim in sides:
        count = lax.axis_size(axis)
        forward = [(i, i + 1) for i in range(count - 1)]
        backward = [(target, source) for source, target in forward]
        low = lax.ppermute(
            lax.slice_in_dim(block, block.shape[dim] - width, None, axis=dim), axis, forward
        )
        high = lax.ppermute(lax.slice_in_dim(block, 0, width, axis=dim), axis, backward)
        block = jnp.concatenate([low, block, high], axis=dim)
    return block


def inside_rows(count, first, valid, total):
    at = lax.iota(jnp.int32, count)
    places = first + at
    keep = (places >= 0) & (places < total) & (at < valid)
    return keep.astype(jnp.float32)[:, None]


def split_two(a):
    high = a.astype(jnp.bfloat16)
    low = (a - high.astype(jnp.float32)).astype(jnp.bfloat16)
    return high, low


def mm(a, b):
    return jnp.dot(a, b, preferred_element_type=jnp.float32)


def band_table(rows, cols, shift, taps):
    step, weights = taps
    s_at = lax.broadcasted_iota(jnp.int32, (rows, cols), 0)
    c_at = lax.broadcasted_iota(jnp.int32, (rows, cols), 1)
    place = s_at - step * c_at - shift
    total = jnp.zeros((rows, cols), jnp.float32)
    for k, w in enumerate(weights):
        total = total + jnp.where(place == k, w, 0.0)
    return total


def halve_columns(values, table, out_ref):
    width = values.shape[1]
    high, low = split_two(values)
    for j in range(width // 256):
        lo = max(256 * j - 128, 0)
        hi_col = min(256 * j + 384, width)
        first = lo - (256 * j - 128)
        last = first + (hi_col - lo)
        part = table[first:last]
        out_ref[j, 0 : values.shape[0]] = mm(high[:, lo:hi_col], part) + mm(low[:, lo:hi_col], part)


def halve_rows(source_ref, count):
    total = pyramid_filter[0] * source_ref[:, pl.ds(0, count, stride=2), :]
    for p in range(1, 4):
        total = total + pyramid_filter[p] * source_ref[:, pl.ds(p, count, stride=2), :]
    return jnp.concatenate([total[j] for j in range(total.shape[0])], axis=1)


def piece_rows(rows, ndate):
    fine = rows // ndate
    return (fine, max(fine // 2, 8), max(fine // 4, 8))


def pyramid_kernel(ndate, taps_ref, x_ref, keep_wide_ref, keep_half_ref, packed_ref,
                   across_ref, wide_ref, half_ref, quarter_ref):
    b = pl.program_id(1)
    x = x_ref[0, 0]
    used = x.shape[0]
    width = x.shape[1]
    tiles = width // 128
    rows = used - 16
    column = [taps_ref[0, b, k] for k in range(7)]
    row = [taps_ref[1, b, k] for k in range(7)]
    table = band_table(3 * 128, 128, 125, (1, column))
    t_high = table.astype(jnp.bfloat16)
    rest = table - t_high.astype(jnp.float32)
    t_mid = rest.astype(jnp.bfloat16)
    t_low = (rest - t_mid.astype(jnp.float32)).astype(jnp.bfloat16)
    for j in range(tiles):
        lo = max(j - 1, 0) * 128
        hi_col = min(j + 2, tiles) * 128
        first = lo - (j - 1) * 128
        last = first + (hi_col - lo)
        window = x[:, lo:hi_col]
        acc = mm(window, t_high[first:last]) + mm(window, t_mid[first:last]) + mm(window, t_low[first:last])
        across_ref[0:used, j * 128 : (j + 1) * 128] = acc
    depth = across_ref.shape[0]
    across_ref[used:depth, :] = jnp.zeros((depth - used, width), jnp.float32)
    n_wide = wide_ref.shape[1]
    total = row[0] * across_ref[pl.ds(0, n_wide), :]
    for k in range(1, 7):
        total = total + row[k] * across_ref[pl.ds(k, n_wide), :]
    total = total * keep_wide_ref[...]
    for j in range(tiles):
        wide_ref[j] = total[:, 128 * j : 128 * (j + 1)]
    n_half = keep_half_ref.shape[0]
    halves = halve_rows(wide_ref, n_half) * keep_half_ref[...]
    down = band_table(512, 128, 127, (2, pyramid_filter)).astype(jnp.bfloat16)
    halve_columns(halves, down, half_ref)
    quarters = halve_rows(half_ref, rows // 4)
    n_quarter = quarter_ref.shape[1]
    quarter_ref[:, rows // 4 : n_quarter, :] = jnp.zeros((tiles // 4, n_quarter - rows // 4, 128), jnp.float32)
    halve_columns(quarters, down, quarter_ref)
    fine, p_half, p_quarter = piece_rows(rows, ndate)
    for q in range(ndate):
        parts = [wide_ref[j, pl.ds(3 + fine * q, fine), :] for j in range(tiles)]
        parts += [half_ref[j, pl.ds(1 + (fine // 2) * q, p_half), :] for j in range(tiles // 2)]
        parts += [quarter_ref[j, pl.ds((fine // 4) * q, p_quarter), :] for j in range(tiles // 4)]
        packed_ref[q, 0, 0] = jnp.concatenate(parts, axis=0).astype(packed_ref.dtype)


def pyramid(extended, resample_taps, band_index, total_rows, ndate):
    dates, bands, used, width = extended.shape
    rows = used - 16
    n_wide = rows + 24
    n_half = rows // 2 + 8
    depth = n_wide + 8
    fine, p_half, p_quarter = piece_rows(rows, ndate)
    count = (width // 128) * fine + (width // 256) * p_half + (width // 512) * p_quarter
    keep_wide = inside_rows(n_wide, band_index * rows - 3, rows + 6, total_rows)
    keep_half = inside_rows(n_half, band_index * (rows // 2) - 1, rows // 2 + 2, total_rows // 2)
    return pl.pallas_call(
        functools.partial(pyramid_kernel, ndate),
        grid=(dates, bands),
        in_specs=[
            pl.BlockSpec(memory_space=pltpu.SMEM),
            pl.BlockSpec((1, 1, used, width), lambda d, b: (d, b, 0, 0)),
            pl.BlockSpec((n_wide, 1), lambda d, b: (0, 0)),
            pl.BlockSpec((n_half, 1), lambda d, b: (0, 0)),
        ],
        out_specs=pl.BlockSpec((ndate, 1, 1, count, 128), lambda d, b: (0, d, b, 0, 0)),
        out_shape=jax.ShapeDtypeStruct((ndate, dates, bands, count, 128), jnp.bfloat16),
        scratch_shapes=[
            pltpu.VMEM((depth, width), jnp.float32),
            pltpu.VMEM((width // 128, n_wide, 128), jnp.float32),
            pltpu.VMEM((width // 256, n_half, 128), jnp.float32),
            pltpu.VMEM((width // 512, rows // 4 + 8, 128), jnp.float32),
        ],
    )(resample_taps, extended, keep_wide, keep_half)


def smooth_operator(dates):
    clamp = np.zeros((dates, dates), np.float64)
    near = np.zeros((dates, dates), np.float64)
    for t in range(dates):
        for k in range(9):
            clamp[t, min(max(t + k - 4, 0), dates - 1)] += savgol_coeffs[k]
            if 0 <= t + k - 4 < dates:
                near[t, t + k - 4] = gap_weights[k]
    return clamp.astype(np.float32), near.astype(np.float32)


def smooth_coefficients(clear):
    dates = clear.shape[0]
    clamp, near = smooth_operator(dates)
    hi = lax.Precision.HIGHEST
    weight = 0.1 + 0.9 * clear
    denom = jnp.einsum("su,uxy->sxy", near, weight, precision=hi)
    gap = (1.0 - clear) / denom
    fill = near[:, :, None, None] * weight[None, :] * gap[:, None]
    fill = fill + np.eye(dates, dtype=np.float32)[:, :, None, None] * clear[None, :]
    return jnp.einsum("ts,suxy->tuxy", clamp, fill, precision=hi)


def smooth_level(got_ref, start, piece, coeff_ref, out_ref, section_ref):
    dates, bands, rows, width = out_ref.shape
    tiles = width // 128
    mask_cols = coeff_ref.shape[3]
    span = width // mask_cols
    per_tile = 128 // span
    lane_group = lax.broadcasted_iota(jnp.int32, (rows, 128), 1) // span
    section_ref[...] = got_ref[:, :, start : start + tiles * piece, :].astype(jnp.float32)
    for j in range(tiles):

        def one_date(t, carry):
            coeffs = []
            for u in range(dates):
                c = coeff_ref[t, u]
                tile = jnp.broadcast_to(c[:, per_tile * j : per_tile * j + 1], (rows, 128))
                for g in range(1, per_tile):
                    m = per_tile * j + g
                    tile = jnp.where(lane_group == g, jnp.broadcast_to(c[:, m : m + 1], (rows, 128)), tile)
                coeffs.append(tile)
            for band in range(bands):
                acc = coeffs[0] * section_ref[0, band, j * piece : j * piece + rows, :]
                for u in range(1, dates):
                    acc = acc + coeffs[u] * section_ref[u, band, j * piece : j * piece + rows, :]
                out_ref[t, band, :, 128 * j : 128 * (j + 1)] = acc.astype(out_ref.dtype)
            return carry

        lax.fori_loop(0, dates, one_date, 0)


def smooth_kernel(pieces, got_ref, c0_ref, c1_ref, c2_ref, *rest):
    o0_ref, o1_ref, o2_ref, s0_ref, s1_ref, s2_ref = rest[-6:]
    start = 0
    for piece, c_ref, o_ref, s_ref in zip(pieces, (c0_ref, c1_ref, c2_ref), (o0_ref, o1_ref, o2_ref), (s0_ref, s1_ref, s2_ref)):
        smooth_level(got_ref, start, piece, c_ref, o_ref, s_ref)
        start += (o_ref.shape[3] // 128) * piece


def smooth_all(got, grown, shapes, pieces, chunk, previous):
    dates, bands = got.shape[:2]
    full = lambda a: pl.BlockSpec(a.shape, lambda i: (0,) * len(a.shape))
    outs = [jax.ShapeDtypeStruct(shape, jnp.bfloat16) for shape in shapes]
    out_specs = [pl.BlockSpec((dates, bands) + shape[2:], lambda i: (0, chunk, 0, 0)) for shape in shapes]
    in_specs = [full(got)] + [full(g) for g in grown]
    args = [got] + list(grown)
    aliases = {}
    if previous is not None:
        for i, prev in enumerate(previous):
            aliases[len(args)] = i
            in_specs.append(pl.BlockSpec(memory_space=pl.ANY))
            args.append(prev)
    return pl.pallas_call(
        functools.partial(smooth_kernel, pieces),
        grid=(1,),
        in_specs=in_specs,
        out_specs=out_specs,
        out_shape=outs,
        input_output_aliases=aliases,
        scratch_shapes=[
            pltpu.VMEM((dates, bands, (shape[3] // 128) * piece, 128), jnp.float32)
            for shape, piece in zip(shapes, pieces)
        ],
    )(*args)


def local(scenes, resample_taps, clear_mask):
    dates, bands, rows, width = scenes.shape
    band_index = lax.axis_index("row")
    total_rows = rows * lax.axis_size("row")
    ndate = lax.axis_size("date")
    extended = padded(scenes, (("row", 2),), 6)
    extended = jnp.pad(extended, ((0, 0), (0, 0), (0, 4), (0, 0)))
    coeff = smooth_coefficients(clear_mask.astype(jnp.float32))
    fine = rows // ndate
    total = ndate * dates
    shapes = (
        (total, bands, fine, width),
        (total, bands, fine // 2, width // 2),
        (total, bands, fine // 4, width // 4),
    )
    grown = [jnp.repeat(coeff, shape[2] // coeff.shape[2], axis=2) for shape in shapes]
    chunks = 2 if bands % 2 == 0 else 1
    step = bands // chunks
    outs = None
    for chunk in range(chunks):
        part = slice(chunk * step, (chunk + 1) * step)
        packed = pyramid(extended[:, part], resample_taps[:, part], band_index, total_rows, ndate)
        got = lax.all_to_all(packed, "date", split_axis=0, concat_axis=0, tiled=True)
        got = got.reshape((total,) + got.shape[2:])
        outs = smooth_all(got, grown, shapes, piece_rows(rows, ndate), chunk, outs)
    return tuple(outs)


def solution(mesh):
    in_specs = (P(("groups", "date"), None, "row", None), P(), P("groups", ("row", "date"), None))
    out_specs = (
        P("groups", None, ("row", "date"), None),
        P("groups", None, ("row", "date"), None),
        P("groups", None, ("row", "date"), None),
    )
    return jax.shard_map(local, mesh=mesh, in_specs=in_specs, out_specs=out_specs, check_vma=False)
```

```python
import functools
import math

import jax
import numpy as np
import jax.numpy as jnp
from jax import lax
from jax.sharding import PartitionSpec as P
from jax.experimental import pallas as pl
from jax.experimental.pallas import tpu as pltpu

gap_weights = [math.exp(-((k - 4) ** 2) / 8.0) for k in range(9)]
savgol_coeffs = [c / 231.0 for c in [-21.0, 14.0, 39.0, 54.0, 59.0, 54.0, 39.0, 14.0, -21.0]]
pyramid_filter = [0.125, 0.375, 0.375, 0.125]


def padded(block, sides, width):
    for axis, dim in sides:
        count = lax.axis_size(axis)
        forward = [(i, i + 1) for i in range(count - 1)]
        backward = [(target, source) for source, target in forward]
        low = lax.ppermute(
            lax.slice_in_dim(block, block.shape[dim] - width, None, axis=dim), axis, forward
        )
        high = lax.ppermute(lax.slice_in_dim(block, 0, width, axis=dim), axis, backward)
        block = jnp.concatenate([low, block, high], axis=dim)
    return block


def inside_rows(count, first, valid, total):
    at = lax.iota(jnp.int32, count)
    places = first + at
    keep = (places >= 0) & (places < total) & (at < valid)
    return keep.astype(jnp.float32)[:, None]


def split_two(a):
    high = a.astype(jnp.bfloat16)
    low = (a - high.astype(jnp.float32)).astype(jnp.bfloat16)
    return high, low


def mm(a, b):
    return jnp.dot(a, b, preferred_element_type=jnp.float32)


def band_table(rows, cols, shift, taps):
    step, weights = taps
    s_at = lax.broadcasted_iota(jnp.int32, (rows, cols), 0)
    c_at = lax.broadcasted_iota(jnp.int32, (rows, cols), 1)
    place = s_at - step * c_at - shift
    total = jnp.zeros((rows, cols), jnp.float32)
    for k, w in enumerate(weights):
        total = total + jnp.where(place == k, w, 0.0)
    return total


def halve_columns(values, table, out_ref):
    width = values.shape[1]
    high, low = split_two(values)
    for j in range(width // 256):
        lo = max(256 * j - 128, 0)
        hi_col = min(256 * j + 384, width)
        first = lo - (256 * j - 128)
        last = first + (hi_col - lo)
        part = table[first:last]
        out_ref[j, 0 : values.shape[0]] = mm(high[:, lo:hi_col], part) + mm(low[:, lo:hi_col], part)


def halve_rows(source_ref, count):
    total = pyramid_filter[0] * source_ref[:, pl.ds(0, count, stride=2), :]
    for p in range(1, 4):
        total = total + pyramid_filter[p] * source_ref[:, pl.ds(p, count, stride=2), :]
    return jnp.concatenate([total[j] for j in range(total.shape[0])], axis=1)


def piece_rows(rows, ndate):
    fine = rows // ndate
    return (fine, max(fine // 2, 8), max(fine // 4, 8))


def pyramid_kernel(ndate, taps_ref, x_ref, keep_wide_ref, keep_half_ref, packed_ref,
                   across_ref, wide_ref, half_ref, quarter_ref):
    b = pl.program_id(1)
    x = x_ref[0, 0]
    used = x.shape[0]
    width = x.shape[1]
    tiles = width // 128
    rows = used - 16
    column = [taps_ref[0, b, k] for k in range(7)]
    row = [taps_ref[1, b, k] for k in range(7)]
    table = band_table(3 * 128, 128, 125, (1, column))
    t_high = table.astype(jnp.bfloat16)
    rest = table - t_high.astype(jnp.float32)
    t_mid = rest.astype(jnp.bfloat16)
    t_low = (rest - t_mid.astype(jnp.float32)).astype(jnp.bfloat16)
    for j in range(tiles):
        lo = max(j - 1, 0) * 128
        hi_col = min(j + 2, tiles) * 128
        first = lo - (j - 1) * 128
        last = first + (hi_col - lo)
        window = x[:, lo:hi_col]
        acc = mm(window, t_high[first:last]) + mm(window, t_mid[first:last]) + mm(window, t_low[first:last])
        across_ref[0:used, j * 128 : (j + 1) * 128] = acc
    depth = across_ref.shape[0]
    across_ref[used:depth, :] = jnp.zeros((depth - used, width), jnp.float32)
    n_wide = wide_ref.shape[1]
    total = row[0] * across_ref[pl.ds(0, n_wide), :]
    for k in range(1, 7):
        total = total + row[k] * across_ref[pl.ds(k, n_wide), :]
    total = total * keep_wide_ref[...]
    for j in range(tiles):
        wide_ref[j] = total[:, 128 * j : 128 * (j + 1)]
    n_half = keep_half_ref.shape[0]
    halves = halve_rows(wide_ref, n_half) * keep_half_ref[...]
    down = band_table(512, 128, 127, (2, pyramid_filter)).astype(jnp.bfloat16)
    halve_columns(halves, down, half_ref)
    quarters = halve_rows(half_ref, rows // 4)
    n_quarter = quarter_ref.shape[1]
    quarter_ref[:, rows // 4 : n_quarter, :] = jnp.zeros((tiles // 4, n_quarter - rows // 4, 128), jnp.float32)
    halve_columns(quarters, down, quarter_ref)
    fine, p_half, p_quarter = piece_rows(rows, ndate)
    for q in range(ndate):
        parts = [wide_ref[j, pl.ds(3 + fine * q, fine), :] for j in range(tiles)]
        parts += [half_ref[j, pl.ds(1 + (fine // 2) * q, p_half), :] for j in range(tiles // 2)]
        parts += [quarter_ref[j, pl.ds((fine // 4) * q, p_quarter), :] for j in range(tiles // 4)]
        packed_ref[q, 0, 0] = jnp.concatenate(parts, axis=0).astype(packed_ref.dtype)


def pyramid(extended, resample_taps, band_index, total_rows, ndate):
    dates, bands, used, width = extended.shape
    rows = used - 16
    n_wide = rows + 24
    n_half = rows // 2 + 8
    depth = n_wide + 8
    fine, p_half, p_quarter = piece_rows(rows, ndate)
    count = (width // 128) * fine + (width // 256) * p_half + (width // 512) * p_quarter
    keep_wide = inside_rows(n_wide, band_index * rows - 3, rows + 6, total_rows)
    keep_half = inside_rows(n_half, band_index * (rows // 2) - 1, rows // 2 + 2, total_rows // 2)
    return pl.pallas_call(
        functools.partial(pyramid_kernel, ndate),
        grid=(dates, bands),
        in_specs=[
            pl.BlockSpec(memory_space=pltpu.SMEM),
            pl.BlockSpec((1, 1, used, width), lambda d, b: (d, b, 0, 0)),
            pl.BlockSpec((n_wide, 1), lambda d, b: (0, 0)),
            pl.BlockSpec((n_half, 1), lambda d, b: (0, 0)),
        ],
        out_specs=pl.BlockSpec((ndate, 1, 1, count, 128), lambda d, b: (0, d, b, 0, 0)),
        out_shape=jax.ShapeDtypeStruct((ndate, dates, bands, count, 128), jnp.bfloat16),
        scratch_shapes=[
            pltpu.VMEM((depth, width), jnp.float32),
            pltpu.VMEM((width // 128, n_wide, 128), jnp.float32),
            pltpu.VMEM((width // 256, n_half, 128), jnp.float32),
            pltpu.VMEM((width // 512, rows // 4 + 8, 128), jnp.float32),
        ],
    )(resample_taps, extended, keep_wide, keep_half)


def smooth_operator(dates):
    clamp = np.zeros((dates, dates), np.float64)
    near = np.zeros((dates, dates), np.float64)
    for t in range(dates):
        for k in range(9):
            clamp[t, min(max(t + k - 4, 0), dates - 1)] += savgol_coeffs[k]
            if 0 <= t + k - 4 < dates:
                near[t, t + k - 4] = gap_weights[k]
    return clamp.astype(np.float32), near.astype(np.float32)


def smooth_coefficients(clear):
    dates = clear.shape[0]
    clamp, near = smooth_operator(dates)
    hi = lax.Precision.HIGHEST
    weight = 0.1 + 0.9 * clear
    denom = jnp.einsum("su,uxy->sxy", near, weight, precision=hi)
    gap = (1.0 - clear) / denom
    fill = near[:, :, None, None] * weight[None, :] * gap[:, None]
    fill = fill + np.eye(dates, dtype=np.float32)[:, :, None, None] * clear[None, :]
    return jnp.einsum("ts,suxy->tuxy", clamp, fill, precision=hi)


def smooth_kernel(got_ref, coeff_ref, *rest):
    out_ref = rest[-1]
    dates, bands, rows = out_ref.shape[:3]

    def one_date(t, carry):
        accs = [None] * bands
        for u in range(dates):
            c = coeff_ref[t, u]
            for band in range(bands):
                term = c * got_ref[u, band, 0:rows, :].astype(jnp.float32)
                accs[band] = term if accs[band] is None else accs[band] + term
        for band in range(bands):
            out_ref[t, band] = accs[band].astype(out_ref.dtype)
        return carry

    lax.fori_loop(0, dates, one_date, 0)


def smooth_level(got, grown, shape, piece, first, chunk, previous):
    dates, bands = got.shape[:2]
    rows = shape[2]
    tiles = shape[3] // 128
    in_specs = [
        pl.BlockSpec((dates, bands, piece, 128), lambda j: (0, 0, first + j, 0)),
        pl.BlockSpec((dates, dates, rows, 128), lambda j: (0, 0, 0, j)),
    ]
    args = [got, grown]
    aliases = {}
    if previous is not None:
        aliases[2] = 0
        in_specs.append(pl.BlockSpec(memory_space=pl.ANY))
        args.append(previous)
    return pl.pallas_call(
        smooth_kernel,
        grid=(tiles,),
        in_specs=in_specs,
        out_specs=pl.BlockSpec((dates, bands, rows, 128), lambda j: (0, chunk, 0, j)),
        out_shape=jax.ShapeDtypeStruct(shape, jnp.bfloat16),
        input_output_aliases=aliases,
    )(*args)


def expand(coeff, rows, width):
    dates, _, mask_rows, mask_cols = coeff.shape
    grown = jnp.broadcast_to(
        coeff[:, :, :, None, :, None],
        (dates, dates, mask_rows, rows // mask_rows, mask_cols, width // mask_cols),
    )
    return grown.reshape(dates, dates, rows, width)


def local(scenes, resample_taps, clear_mask):
    dates, bands, rows, width = scenes.shape
    band_index = lax.axis_index("row")
    total_rows = rows * lax.axis_size("row")
    ndate = lax.axis_size("date")
    extended = padded(scenes, (("row", 2),), 6)
    extended = jnp.pad(extended, ((0, 0), (0, 0), (0, 4), (0, 0)))
    coeff = smooth_coefficients(clear_mask.astype(jnp.float32))
    fine = rows // ndate
    total = ndate * dates
    shapes = (
        (total, bands, fine, width),
        (total, bands, fine // 2, width // 2),
        (total, bands, fine // 4, width // 4),
    )
    grown = [expand(coeff, shape[2], shape[3]) for shape in shapes]
    pieces = piece_rows(rows, ndate)
    firsts = []
    start = 0
    for shape, piece in zip(shapes, pieces):
        firsts.append(start // piece)
        start += (shape[3] // 128) * piece
    chunks = 2 if bands % 2 == 0 else 1
    step = bands // chunks
    outs = [None, None, None]
    for chunk in range(chunks):
        part = slice(chunk * step, (chunk + 1) * step)
        packed = pyramid(extended[:, part], resample_taps[:, part], band_index, total_rows, ndate)
        got = lax.all_to_all(packed, "date", split_axis=0, concat_axis=0, tiled=True)
        got = got.reshape((total,) + got.shape[2:])
        outs = [
            smooth_level(got, g, shape, piece, first, chunk, prev)
            for g, shape, piece, first, prev in zip(grown, shapes, pieces, firsts, outs)
        ]
    return tuple(outs)


def solution(mesh):
    in_specs = (P(("groups", "date"), None, "row", None), P(), P("groups", ("row", "date"), None))
    out_specs = (
        P("groups", None, ("row", "date"), None),
        P("groups", None, ("row", "date"), None),
        P("groups", None, ("row", "date"), None),
    )
    return jax.shard_map(local, mesh=mesh, in_specs=in_specs, out_specs=out_specs, check_vma=False)
```

```python
import functools
import math

import jax
import numpy as np
import jax.numpy as jnp
from jax import lax
from jax.sharding import PartitionSpec as P
from jax.experimental import pallas as pl
from jax.experimental.pallas import tpu as pltpu

gap_weights = [math.exp(-((k - 4) ** 2) / 8.0) for k in range(9)]
savgol_coeffs = [c / 231.0 for c in [-21.0, 14.0, 39.0, 54.0, 59.0, 54.0, 39.0, 14.0, -21.0]]
pyramid_filter = [0.125, 0.375, 0.375, 0.125]


def padded(block, sides, width):
    for axis, dim in sides:
        count = lax.axis_size(axis)
        forward = [(i, i + 1) for i in range(count - 1)]
        backward = [(target, source) for source, target in forward]
        low = lax.ppermute(
            lax.slice_in_dim(block, block.shape[dim] - width, None, axis=dim), axis, forward
        )
        high = lax.ppermute(lax.slice_in_dim(block, 0, width, axis=dim), axis, backward)
        block = jnp.concatenate([low, block, high], axis=dim)
    return block


def inside_rows(count, first, valid, total):
    at = lax.iota(jnp.int32, count)
    places = first + at
    keep = (places >= 0) & (places < total) & (at < valid)
    return keep.astype(jnp.float32)[:, None]


def split_two(a):
    high = a.astype(jnp.bfloat16)
    low = (a - high.astype(jnp.float32)).astype(jnp.bfloat16)
    return high, low


def mm(a, b):
    return jnp.dot(a, b, preferred_element_type=jnp.float32)


def band_table(rows, cols, shift, taps):
    step, weights = taps
    s_at = lax.broadcasted_iota(jnp.int32, (rows, cols), 0)
    c_at = lax.broadcasted_iota(jnp.int32, (rows, cols), 1)
    place = s_at - step * c_at - shift
    total = jnp.zeros((rows, cols), jnp.float32)
    for k, w in enumerate(weights):
        total = total + jnp.where(place == k, w, 0.0)
    return total


def halve_columns(values, table, out_ref):
    width = values.shape[1]
    high, low = split_two(values)
    for j in range(width // 256):
        lo = max(256 * j - 128, 0)
        hi_col = min(256 * j + 384, width)
        first = lo - (256 * j - 128)
        last = first + (hi_col - lo)
        part = table[first:last]
        out_ref[j, 0 : values.shape[0]] = mm(high[:, lo:hi_col], part) + mm(low[:, lo:hi_col], part)


def halve_rows(source_ref, count):
    total = pyramid_filter[0] * source_ref[:, pl.ds(0, count, stride=2), :]
    for p in range(1, 4):
        total = total + pyramid_filter[p] * source_ref[:, pl.ds(p, count, stride=2), :]
    return jnp.concatenate([total[j] for j in range(total.shape[0])], axis=1)


def piece_rows(rows, ndate):
    fine = rows // ndate
    return (fine, max(fine // 2, 8), max(fine // 4, 8))


def pyramid_kernel(ndate, taps_ref, x_ref, keep_wide_ref, keep_half_ref, packed_ref,
                   across_ref, wide_ref, half_ref, quarter_ref):
    b = pl.program_id(1)
    x = x_ref[0, 0]
    used = x.shape[0]
    width = x.shape[1]
    tiles = width // 128
    rows = used - 16
    column = [taps_ref[0, b, k] for k in range(7)]
    row = [taps_ref[1, b, k] for k in range(7)]
    table = band_table(3 * 128, 128, 125, (1, column))
    t_high = table.astype(jnp.bfloat16)
    rest = table - t_high.astype(jnp.float32)
    t_mid = rest.astype(jnp.bfloat16)
    t_low = (rest - t_mid.astype(jnp.float32)).astype(jnp.bfloat16)
    for j in range(tiles):
        lo = max(j - 1, 0) * 128
        hi_col = min(j + 2, tiles) * 128
        first = lo - (j - 1) * 128
        last = first + (hi_col - lo)
        window = x[:, lo:hi_col]
        acc = mm(window, t_high[first:last]) + mm(window, t_mid[first:last]) + mm(window, t_low[first:last])
        across_ref[0:used, j * 128 : (j + 1) * 128] = acc
    depth = across_ref.shape[0]
    across_ref[used:depth, :] = jnp.zeros((depth - used, width), jnp.float32)
    n_wide = wide_ref.shape[1]
    total = row[0] * across_ref[pl.ds(0, n_wide), :]
    for k in range(1, 7):
        total = total + row[k] * across_ref[pl.ds(k, n_wide), :]
    total = total * keep_wide_ref[...]
    for j in range(tiles):
        wide_ref[j] = total[:, 128 * j : 128 * (j + 1)]
    n_half = keep_half_ref.shape[0]
    halves = halve_rows(wide_ref, n_half) * keep_half_ref[...]
    down = band_table(512, 128, 127, (2, pyramid_filter)).astype(jnp.bfloat16)
    halve_columns(halves, down, half_ref)
    quarters = halve_rows(half_ref, rows // 4)
    n_quarter = quarter_ref.shape[1]
    quarter_ref[:, rows // 4 : n_quarter, :] = jnp.zeros((tiles // 4, n_quarter - rows // 4, 128), jnp.float32)
    halve_columns(quarters, down, quarter_ref)
    fine, p_half, p_quarter = piece_rows(rows, ndate)
    for q in range(ndate):
        parts = [wide_ref[j, pl.ds(3 + fine * q, fine), :] for j in range(tiles)]
        parts += [half_ref[j, pl.ds(1 + (fine // 2) * q, p_half), :] for j in range(tiles // 2)]
        parts += [quarter_ref[j, pl.ds((fine // 4) * q, p_quarter), :] for j in range(tiles // 4)]
        packed_ref[q, 0, 0] = jnp.concatenate(parts, axis=0).astype(packed_ref.dtype)


def pyramid(extended, resample_taps, band_index, total_rows, ndate):
    dates, bands, used, width = extended.shape
    rows = used - 16
    n_wide = rows + 24
    n_half = rows // 2 + 8
    depth = n_wide + 8
    fine, p_half, p_quarter = piece_rows(rows, ndate)
    count = (width // 128) * fine + (width // 256) * p_half + (width // 512) * p_quarter
    keep_wide = inside_rows(n_wide, band_index * rows - 3, rows + 6, total_rows)
    keep_half = inside_rows(n_half, band_index * (rows // 2) - 1, rows // 2 + 2, total_rows // 2)
    return pl.pallas_call(
        functools.partial(pyramid_kernel, ndate),
        grid=(dates, bands),
        in_specs=[
            pl.BlockSpec(memory_space=pltpu.SMEM),
            pl.BlockSpec((1, 1, used, width), lambda d, b: (d, b, 0, 0)),
            pl.BlockSpec((n_wide, 1), lambda d, b: (0, 0)),
            pl.BlockSpec((n_half, 1), lambda d, b: (0, 0)),
        ],
        out_specs=pl.BlockSpec((ndate, 1, 1, count, 128), lambda d, b: (0, d, b, 0, 0)),
        out_shape=jax.ShapeDtypeStruct((ndate, dates, bands, count, 128), jnp.bfloat16),
        scratch_shapes=[
            pltpu.VMEM((depth, width), jnp.float32),
            pltpu.VMEM((width // 128, n_wide, 128), jnp.float32),
            pltpu.VMEM((width // 256, n_half, 128), jnp.float32),
            pltpu.VMEM((width // 512, rows // 4 + 8, 128), jnp.float32),
        ],
    )(resample_taps, extended, keep_wide, keep_half)


def smooth_operator(dates):
    clamp = np.zeros((dates, dates), np.float64)
    near = np.zeros((dates, dates), np.float64)
    for t in range(dates):
        for k in range(9):
            clamp[t, min(max(t + k - 4, 0), dates - 1)] += savgol_coeffs[k]
            if 0 <= t + k - 4 < dates:
                near[t, t + k - 4] = gap_weights[k]
    return clamp.astype(np.float32), near.astype(np.float32)


def smooth_coefficients(clear):
    dates = clear.shape[0]
    clamp, near = smooth_operator(dates)
    hi = lax.Precision.HIGHEST
    weight = 0.1 + 0.9 * clear
    denom = jnp.einsum("su,uxy->sxy", near, weight, precision=hi)
    gap = (1.0 - clear) / denom
    fill = near[:, :, None, None] * weight[None, :] * gap[:, None]
    fill = fill + np.eye(dates, dtype=np.float32)[:, :, None, None] * clear[None, :]
    return jnp.einsum("ts,suxy->tuxy", clamp, fill, precision=hi)


def split_three(a):
    high = a.astype(jnp.bfloat16)
    rest = a - high.astype(jnp.float32)
    mid = rest.astype(jnp.bfloat16)
    low = (rest - mid.astype(jnp.float32)).astype(jnp.bfloat16)
    return high, mid, low


def smooth_level(mask_cols, got_ref, start, piece, coeff_ref, out_ref, section_ref, tiles_ref):
    dates, bands, rows, width = out_ref.shape
    tiles = width // 128
    span = width // mask_cols
    section_ref[...] = got_ref[:, :, start : start + tiles * piece, :].astype(jnp.float32)
    parts = split_three(coeff_ref[...])
    m_at = lax.broadcasted_iota(jnp.int32, (128, 128), 0)
    lane = lax.broadcasted_iota(jnp.int32, (128, 128), 1)
    for j in range(tiles):
        pick = (m_at == (128 * j + lane) // span).astype(jnp.bfloat16)
        grown = mm(parts[0], pick) + mm(parts[1], pick) + mm(parts[2], pick)
        tiles_ref[...] = grown.reshape(tiles_ref.shape)

        def one_date(t, carry):
            for band in range(bands):
                acc = tiles_ref[t, 0] * section_ref[0, band, j * piece : j * piece + rows, :]
                for u in range(1, dates):
                    acc = acc + tiles_ref[t, u] * section_ref[u, band, j * piece : j * piece + rows, :]
                out_ref[t, band, :, 128 * j : 128 * (j + 1)] = acc.astype(out_ref.dtype)
            return carry

        lax.fori_loop(0, dates, one_date, 0)


def smooth_kernel(mask_cols, pieces, got_ref, c0_ref, c1_ref, c2_ref, o0_ref, o1_ref, o2_ref,
                  s0_ref, s1_ref, s2_ref, t0_ref, t1_ref, t2_ref):
    start = 0
    levels = zip(pieces, (c0_ref, c1_ref, c2_ref), (o0_ref, o1_ref, o2_ref), (s0_ref, s1_ref, s2_ref), (t0_ref, t1_ref, t2_ref))
    for piece, c_ref, o_ref, s_ref, t_ref in levels:
        smooth_level(mask_cols, got_ref, start, piece, c_ref, o_ref, s_ref, t_ref)
        start += (o_ref.shape[3] // 128) * piece


def smooth_all(got, coeff, shapes, pieces):
    dates, bands = got.shape[:2]
    mask_cols = coeff.shape[3]
    flat = []
    for shape in shapes:
        grown = jnp.repeat(coeff, shape[2] // coeff.shape[2], axis=2)
        grown = grown.reshape(-1, mask_cols)
        flat.append(jnp.pad(grown, ((0, 0), (0, 128 - mask_cols))))
    full = lambda a: pl.BlockSpec(a.shape, lambda: (0,) * len(a.shape))
    outs = [jax.ShapeDtypeStruct(shape, jnp.bfloat16) for shape in shapes]
    return pl.pallas_call(
        functools.partial(smooth_kernel, mask_cols, pieces),
        in_specs=[full(got)] + [full(g) for g in flat],
        out_specs=[full(o) for o in outs],
        out_shape=outs,
        scratch_shapes=[
            pltpu.VMEM((dates, bands, (shape[3] // 128) * piece, 128), jnp.float32)
            for shape, piece in zip(shapes, pieces)
        ]
        + [pltpu.VMEM((dates, dates, shape[2], 128), jnp.float32) for shape in shapes],
    )(got, *flat)


def local(scenes, resample_taps, clear_mask):
    dates, bands, rows, width = scenes.shape
    band_index = lax.axis_index("row")
    total_rows = rows * lax.axis_size("row")
    ndate = lax.axis_size("date")
    extended = padded(scenes, (("row", 2),), 6)
    extended = jnp.pad(extended, ((0, 0), (0, 0), (0, 4), (0, 0)))
    packed = pyramid(extended, resample_taps, band_index, total_rows, ndate)
    coeff = smooth_coefficients(clear_mask.astype(jnp.float32))
    got = lax.all_to_all(packed, "date", split_axis=0, concat_axis=0, tiled=True)
    got = got.reshape((ndate * dates,) + got.shape[2:])
    fine = rows // ndate
    total = ndate * dates
    shapes = (
        (total, bands, fine, width),
        (total, bands, fine // 2, width // 2),
        (total, bands, fine // 4, width // 4),
    )
    return tuple(smooth_all(got, coeff, shapes, piece_rows(rows, ndate)))


def solution(mesh):
    in_specs = (P(("groups", "date"), None, "row", None), P(), P("groups", ("row", "date"), None))
    out_specs = (
        P("groups", None, ("row", "date"), None),
        P("groups", None, ("row", "date"), None),
        P("groups", None, ("row", "date"), None),
    )
    return jax.shard_map(local, mesh=mesh, in_specs=in_specs, out_specs=out_specs, check_vma=False)
```

```python
import functools
import math

import jax
import numpy as np
import jax.numpy as jnp
from jax import lax
from jax.sharding import PartitionSpec as P
from jax.experimental import pallas as pl
from jax.experimental.pallas import tpu as pltpu

gap_weights = [math.exp(-((k - 4) ** 2) / 8.0) for k in range(9)]
savgol_coeffs = [c / 231.0 for c in [-21.0, 14.0, 39.0, 54.0, 59.0, 54.0, 39.0, 14.0, -21.0]]
pyramid_filter = [0.125, 0.375, 0.375, 0.125]


def padded(block, sides, width):
    for axis, dim in sides:
        count = lax.axis_size(axis)
        forward = [(i, i + 1) for i in range(count - 1)]
        backward = [(target, source) for source, target in forward]
        low = lax.ppermute(
            lax.slice_in_dim(block, block.shape[dim] - width, None, axis=dim), axis, forward
        )
        high = lax.ppermute(lax.slice_in_dim(block, 0, width, axis=dim), axis, backward)
        block = jnp.concatenate([low, block, high], axis=dim)
    return block


def inside_rows(count, first, valid, total):
    at = lax.iota(jnp.int32, count)
    places = first + at
    keep = (places >= 0) & (places < total) & (at < valid)
    return keep.astype(jnp.float32)[:, None]


def split_two(a):
    high = a.astype(jnp.bfloat16)
    low = (a - high.astype(jnp.float32)).astype(jnp.bfloat16)
    return high, low


def mm(a, b):
    return jnp.dot(a, b, preferred_element_type=jnp.float32)


def band_table(rows, cols, shift, taps):
    step, weights = taps
    s_at = lax.broadcasted_iota(jnp.int32, (rows, cols), 0)
    c_at = lax.broadcasted_iota(jnp.int32, (rows, cols), 1)
    place = s_at - step * c_at - shift
    total = jnp.zeros((rows, cols), jnp.float32)
    for k, w in enumerate(weights):
        total = total + jnp.where(place == k, w, 0.0)
    return total


def halve_columns(values, table, out_ref):
    width = values.shape[1]
    high, low = split_two(values)
    for j in range(width // 256):
        lo = max(256 * j - 128, 0)
        hi_col = min(256 * j + 384, width)
        first = lo - (256 * j - 128)
        last = first + (hi_col - lo)
        part = table[first:last]
        out_ref[j, 0 : values.shape[0]] = mm(high[:, lo:hi_col], part) + mm(low[:, lo:hi_col], part)


def halve_rows(source_ref, count):
    total = pyramid_filter[0] * source_ref[:, pl.ds(0, count, stride=2), :]
    for p in range(1, 4):
        total = total + pyramid_filter[p] * source_ref[:, pl.ds(p, count, stride=2), :]
    return jnp.concatenate([total[j] for j in range(total.shape[0])], axis=1)


def piece_rows(rows, ndate):
    fine = rows // ndate
    return (fine, max(fine // 2, 8), max(fine // 4, 8))


def pyramid_kernel(ndate, taps_ref, x_ref, keep_wide_ref, keep_half_ref, packed_ref,
                   across_ref, wide_ref, half_ref, quarter_ref):
    b = pl.program_id(1)
    x = x_ref[0, 0]
    used = x.shape[0]
    width = x.shape[1]
    tiles = width // 128
    rows = used - 16
    column = [taps_ref[0, b, k] for k in range(7)]
    row = [taps_ref[1, b, k] for k in range(7)]
    table = band_table(3 * 128, 128, 125, (1, column))
    t_high = table.astype(jnp.bfloat16)
    rest = table - t_high.astype(jnp.float32)
    t_mid = rest.astype(jnp.bfloat16)
    t_low = (rest - t_mid.astype(jnp.float32)).astype(jnp.bfloat16)
    for j in range(tiles):
        lo = max(j - 1, 0) * 128
        hi_col = min(j + 2, tiles) * 128
        first = lo - (j - 1) * 128
        last = first + (hi_col - lo)
        window = x[:, lo:hi_col]
        acc = mm(window, t_high[first:last]) + mm(window, t_mid[first:last]) + mm(window, t_low[first:last])
        across_ref[0:used, j * 128 : (j + 1) * 128] = acc
    depth = across_ref.shape[0]
    across_ref[used:depth, :] = jnp.zeros((depth - used, width), jnp.float32)
    n_wide = wide_ref.shape[1]
    total = row[0] * across_ref[pl.ds(0, n_wide), :]
    for k in range(1, 7):
        total = total + row[k] * across_ref[pl.ds(k, n_wide), :]
    total = total * keep_wide_ref[...]
    for j in range(tiles):
        wide_ref[j] = total[:, 128 * j : 128 * (j + 1)]
    n_half = keep_half_ref.shape[0]
    halves = halve_rows(wide_ref, n_half) * keep_half_ref[...]
    down = band_table(512, 128, 127, (2, pyramid_filter)).astype(jnp.bfloat16)
    halve_columns(halves, down, half_ref)
    quarters = halve_rows(half_ref, rows // 4)
    n_quarter = quarter_ref.shape[1]
    quarter_ref[:, rows // 4 : n_quarter, :] = jnp.zeros((tiles // 4, n_quarter - rows // 4, 128), jnp.float32)
    halve_columns(quarters, down, quarter_ref)
    fine, p_half, p_quarter = piece_rows(rows, ndate)
    for q in range(ndate):
        parts = [wide_ref[j, pl.ds(3 + fine * q, fine), :] for j in range(tiles)]
        parts += [half_ref[j, pl.ds(1 + (fine // 2) * q, p_half), :] for j in range(tiles // 2)]
        parts += [quarter_ref[j, pl.ds((fine // 4) * q, p_quarter), :] for j in range(tiles // 4)]
        packed_ref[q, 0, 0] = jnp.concatenate(parts, axis=0).astype(packed_ref.dtype)


def pyramid(extended, resample_taps, band_index, total_rows, ndate):
    dates, bands, used, width = extended.shape
    rows = used - 16
    n_wide = rows + 24
    n_half = rows // 2 + 8
    depth = n_wide + 8
    fine, p_half, p_quarter = piece_rows(rows, ndate)
    count = (width // 128) * fine + (width // 256) * p_half + (width // 512) * p_quarter
    keep_wide = inside_rows(n_wide, band_index * rows - 3, rows + 6, total_rows)
    keep_half = inside_rows(n_half, band_index * (rows // 2) - 1, rows // 2 + 2, total_rows // 2)
    return pl.pallas_call(
        functools.partial(pyramid_kernel, ndate),
        grid=(dates, bands),
        in_specs=[
            pl.BlockSpec(memory_space=pltpu.SMEM),
            pl.BlockSpec((1, 1, used, width), lambda d, b: (d, b, 0, 0)),
            pl.BlockSpec((n_wide, 1), lambda d, b: (0, 0)),
            pl.BlockSpec((n_half, 1), lambda d, b: (0, 0)),
        ],
        out_specs=pl.BlockSpec((ndate, 1, 1, count, 128), lambda d, b: (0, d, b, 0, 0)),
        out_shape=jax.ShapeDtypeStruct((ndate, dates, bands, count, 128), jnp.bfloat16),
        scratch_shapes=[
            pltpu.VMEM((depth, width), jnp.float32),
            pltpu.VMEM((width // 128, n_wide, 128), jnp.float32),
            pltpu.VMEM((width // 256, n_half, 128), jnp.float32),
            pltpu.VMEM((width // 512, rows // 4 + 8, 128), jnp.float32),
        ],
    )(resample_taps, extended, keep_wide, keep_half)


def smooth_operator(dates):
    clamp = np.zeros((dates, dates), np.float64)
    near = np.zeros((dates, dates), np.float64)
    for t in range(dates):
        for k in range(9):
            clamp[t, min(max(t + k - 4, 0), dates - 1)] += savgol_coeffs[k]
            if 0 <= t + k - 4 < dates:
                near[t, t + k - 4] = gap_weights[k]
    return clamp.astype(np.float32), near.astype(np.float32)


def smooth_coefficients(clear):
    dates = clear.shape[0]
    clamp, near = smooth_operator(dates)
    hi = lax.Precision.HIGHEST
    weight = 0.1 + 0.9 * clear
    denom = jnp.einsum("su,uxy->sxy", near, weight, precision=hi)
    gap = (1.0 - clear) / denom
    fill = near[:, :, None, None] * weight[None, :] * gap[:, None]
    fill = fill + np.eye(dates, dtype=np.float32)[:, :, None, None] * clear[None, :]
    return jnp.einsum("ts,suxy->tuxy", clamp, fill, precision=hi)


def split_three(a):
    high = a.astype(jnp.bfloat16)
    rest = a - high.astype(jnp.float32)
    mid = rest.astype(jnp.bfloat16)
    low = (rest - mid.astype(jnp.float32)).astype(jnp.bfloat16)
    return high, mid, low


def smooth_level(mask_cols, got_ref, start, piece, coeff_ref, out_ref, section_ref, tiles_ref):
    dates, bands, rows, width = out_ref.shape
    tiles = width // 128
    span = width // mask_cols
    section_ref[...] = got_ref[:, :, start : start + tiles * piece, :].astype(jnp.float32)
    parts = split_three(coeff_ref[...])
    m_at = lax.broadcasted_iota(jnp.int32, (128, 128), 0)
    lane = lax.broadcasted_iota(jnp.int32, (128, 128), 1)
    for j in range(tiles):
        pick = (m_at == (128 * j + lane) // span).astype(jnp.bfloat16)
        grown = mm(parts[0], pick) + mm(parts[1], pick) + mm(parts[2], pick)
        tiles_ref[...] = grown.reshape(tiles_ref.shape)

        step = min(rows, 8)

        def one_block(r, carry):
            r0 = pl.multiple_of(r * step, step)
            values = [
                [section_ref[u, band, pl.ds(j * piece + r0, step), :] for band in range(bands)]
                for u in range(dates)
            ]
            for t in range(dates):
                weights = [tiles_ref[t, u, pl.ds(r0, step), :] for u in range(dates)]
                for band in range(bands):
                    acc = weights[0] * values[0][band]
                    for u in range(1, dates):
                        acc = acc + weights[u] * values[u][band]
                    out_ref[t, band, pl.ds(r0, step), 128 * j : 128 * (j + 1)] = acc.astype(out_ref.dtype)
            return carry

        lax.fori_loop(0, rows // step, one_block, 0)


def smooth_kernel(mask_cols, pieces, got_ref, c0_ref, c1_ref, c2_ref, o0_ref, o1_ref, o2_ref,
                  s0_ref, s1_ref, s2_ref, t0_ref, t1_ref, t2_ref):
    start = 0
    levels = zip(pieces, (c0_ref, c1_ref, c2_ref), (o0_ref, o1_ref, o2_ref), (s0_ref, s1_ref, s2_ref), (t0_ref, t1_ref, t2_ref))
    for piece, c_ref, o_ref, s_ref, t_ref in levels:
        smooth_level(mask_cols, got_ref, start, piece, c_ref, o_ref, s_ref, t_ref)
        start += (o_ref.shape[3] // 128) * piece


def smooth_all(got, coeff, shapes, pieces):
    dates, bands = got.shape[:2]
    mask_cols = coeff.shape[3]
    flat = []
    for shape in shapes:
        grown = jnp.repeat(coeff, shape[2] // coeff.shape[2], axis=2)
        grown = grown.reshape(-1, mask_cols)
        flat.append(jnp.pad(grown, ((0, 0), (0, 128 - mask_cols))))
    full = lambda a: pl.BlockSpec(a.shape, lambda: (0,) * len(a.shape))
    outs = [jax.ShapeDtypeStruct(shape, jnp.bfloat16) for shape in shapes]
    return pl.pallas_call(
        functools.partial(smooth_kernel, mask_cols, pieces),
        in_specs=[full(got)] + [full(g) for g in flat],
        out_specs=[full(o) for o in outs],
        out_shape=outs,
        scratch_shapes=[
            pltpu.VMEM((dates, bands, (shape[3] // 128) * piece, 128), jnp.float32)
            for shape, piece in zip(shapes, pieces)
        ]
        + [pltpu.VMEM((dates, dates, shape[2], 128), jnp.float32) for shape in shapes],
    )(got, *flat)


def local(scenes, resample_taps, clear_mask):
    dates, bands, rows, width = scenes.shape
    band_index = lax.axis_index("row")
    total_rows = rows * lax.axis_size("row")
    ndate = lax.axis_size("date")
    extended = padded(scenes, (("row", 2),), 6)
    extended = jnp.pad(extended, ((0, 0), (0, 0), (0, 4), (0, 0)))
    packed = pyramid(extended, resample_taps, band_index, total_rows, ndate)
    coeff = smooth_coefficients(clear_mask.astype(jnp.float32))
    got = lax.all_to_all(packed, "date", split_axis=0, concat_axis=0, tiled=True)
    got = got.reshape((ndate * dates,) + got.shape[2:])
    fine = rows // ndate
    total = ndate * dates
    shapes = (
        (total, bands, fine, width),
        (total, bands, fine // 2, width // 2),
        (total, bands, fine // 4, width // 4),
    )
    return tuple(smooth_all(got, coeff, shapes, piece_rows(rows, ndate)))


def solution(mesh):
    in_specs = (P(("groups", "date"), None, "row", None), P(), P("groups", ("row", "date"), None))
    out_specs = (
        P("groups", None, ("row", "date"), None),
        P("groups", None, ("row", "date"), None),
        P("groups", None, ("row", "date"), None),
    )
    return jax.shard_map(local, mesh=mesh, in_specs=in_specs, out_specs=out_specs, check_vma=False)
```

```python
import functools
import math

import jax
import numpy as np
import jax.numpy as jnp
from jax import lax
from jax.sharding import PartitionSpec as P
from jax.experimental import pallas as pl
from jax.experimental.pallas import tpu as pltpu

gap_weights = [math.exp(-((k - 4) ** 2) / 8.0) for k in range(9)]
savgol_coeffs = [c / 231.0 for c in [-21.0, 14.0, 39.0, 54.0, 59.0, 54.0, 39.0, 14.0, -21.0]]
pyramid_filter = [0.125, 0.375, 0.375, 0.125]


def split_two(a):
    high = a.astype(jnp.bfloat16)
    low = (a - high.astype(jnp.float32)).astype(jnp.bfloat16)
    return high, low


def mm(a, b):
    return jnp.dot(a, b, preferred_element_type=jnp.float32)


def band_table(rows, cols, shift, taps):
    step, weights = taps
    s_at = lax.broadcasted_iota(jnp.int32, (rows, cols), 0)
    c_at = lax.broadcasted_iota(jnp.int32, (rows, cols), 1)
    place = s_at - step * c_at - shift
    total = jnp.zeros((rows, cols), jnp.float32)
    for k, w in enumerate(weights):
        total = total + jnp.where(place == k, w, 0.0)
    return total


def halve_columns(values, table, out_ref):
    width = values.shape[1]
    high, low = split_two(values)
    for j in range(width // 256):
        lo = max(256 * j - 128, 0)
        hi_col = min(256 * j + 384, width)
        first = lo - (256 * j - 128)
        last = first + (hi_col - lo)
        part = table[first:last]
        out_ref[j, 0 : values.shape[0]] = mm(high[:, lo:hi_col], part) + mm(low[:, lo:hi_col], part)


def halve_rows(source_ref, count):
    total = pyramid_filter[0] * source_ref[:, pl.ds(0, count, stride=2), :]
    for p in range(1, 4):
        total = total + pyramid_filter[p] * source_ref[:, pl.ds(p, count, stride=2), :]
    return jnp.concatenate([total[j] for j in range(total.shape[0])], axis=1)


def piece_rows(rows, ndate):
    fine = rows // ndate
    return (fine, max(fine // 2, 8), max(fine // 4, 8))


def pyramid_kernel(ndate, total_rows, taps_ref, where_ref, low_ref, x_ref, high_ref, packed_ref,
                   across_ref, wide_ref, half_ref, quarter_ref):
    b = pl.program_id(1)
    rows = x_ref.shape[2]
    width = x_ref.shape[3]
    edge = low_ref.shape[2]
    tiles = width // 128
    column = [taps_ref[0, b, k] for k in range(7)]
    row = [taps_ref[1, b, k] for k in range(7)]
    table = band_table(3 * 128, 128, 125, (1, column))
    t_high = table.astype(jnp.bfloat16)
    rest = table - t_high.astype(jnp.float32)
    t_mid = rest.astype(jnp.bfloat16)
    t_low = (rest - t_mid.astype(jnp.float32)).astype(jnp.bfloat16)
    sources = ((low_ref, 0), (x_ref, edge), (high_ref, edge + rows))
    for source_ref, at in sources:
        x = source_ref[0, 0]
        count = x.shape[0]
        for j in range(tiles):
            lo = max(j - 1, 0) * 128
            hi_col = min(j + 2, tiles) * 128
            first = lo - (j - 1) * 128
            last = first + (hi_col - lo)
            window = x[:, lo:hi_col]
            acc = mm(window, t_high[first:last]) + mm(window, t_mid[first:last]) + mm(window, t_low[first:last])
            across_ref[at : at + count, j * 128 : (j + 1) * 128] = acc
    used = 2 * edge + rows
    depth = across_ref.shape[0]
    across_ref[used:depth, :] = jnp.zeros((depth - used, width), jnp.float32)
    band_index = where_ref[0]
    n_wide = wide_ref.shape[1]
    wide_at = lax.broadcasted_iota(jnp.int32, (n_wide, 128), 0)
    wide_row = band_index * rows - 3 + wide_at
    keep_wide = ((wide_row >= 0) & (wide_row < total_rows) & (wide_at < rows + 6)).astype(jnp.float32)
    shift = edge - 6
    for j in range(tiles):
        cols = slice(128 * j, 128 * (j + 1))
        total = row[0] * across_ref[pl.ds(shift, n_wide), cols]
        for k in range(1, 7):
            total = total + row[k] * across_ref[pl.ds(shift + k, n_wide), cols]
        wide_ref[j] = total * keep_wide
    n_half = half_ref.shape[1]
    half_at = lax.broadcasted_iota(jnp.int32, (n_half, 1), 0)
    half_row = band_index * (rows // 2) - 1 + half_at
    keep_half = ((half_row >= 0) & (half_row < total_rows // 2) & (half_at < rows // 2 + 2)).astype(jnp.float32)
    halves = halve_rows(wide_ref, n_half) * keep_half
    down = band_table(512, 128, 127, (2, pyramid_filter)).astype(jnp.bfloat16)
    halve_columns(halves, down, half_ref)
    quarters = halve_rows(half_ref, rows // 4)
    n_quarter = quarter_ref.shape[1]
    quarter_ref[:, rows // 4 : n_quarter, :] = jnp.zeros((tiles // 4, n_quarter - rows // 4, 128), jnp.float32)
    halve_columns(quarters, down, quarter_ref)
    fine, p_half, p_quarter = piece_rows(rows, ndate)
    for q in range(ndate):
        parts = [wide_ref[j, pl.ds(3 + fine * q, fine), :] for j in range(tiles)]
        parts += [half_ref[j, pl.ds(1 + (fine // 2) * q, p_half), :] for j in range(tiles // 2)]
        parts += [quarter_ref[j, pl.ds((fine // 4) * q, p_quarter), :] for j in range(tiles // 4)]
        packed_ref[q, 0, 0] = jnp.concatenate(parts, axis=0).astype(packed_ref.dtype)


def pyramid(low, scenes, high, resample_taps, band_index, total_rows, ndate):
    dates, bands, rows, width = scenes.shape
    edge = low.shape[2]
    n_wide = rows + 24
    n_half = rows // 2 + 8
    depth = max(n_wide + 8, 2 * edge + rows)
    fine, p_half, p_quarter = piece_rows(rows, ndate)
    count = (width // 128) * fine + (width // 256) * p_half + (width // 512) * p_quarter
    where = jnp.reshape(band_index, (1,)).astype(jnp.int32)
    return pl.pallas_call(
        functools.partial(pyramid_kernel, ndate, total_rows),
        grid=(dates, bands),
        in_specs=[
            pl.BlockSpec(memory_space=pltpu.SMEM),
            pl.BlockSpec(memory_space=pltpu.SMEM),
            pl.BlockSpec((1, 1, edge, width), lambda d, b: (d, b, 0, 0)),
            pl.BlockSpec((1, 1, rows, width), lambda d, b: (d, b, 0, 0)),
            pl.BlockSpec((1, 1, edge, width), lambda d, b: (d, b, 0, 0)),
        ],
        out_specs=pl.BlockSpec((ndate, 1, 1, count, 128), lambda d, b: (0, d, b, 0, 0)),
        out_shape=jax.ShapeDtypeStruct((ndate, dates, bands, count, 128), jnp.bfloat16),
        scratch_shapes=[
            pltpu.VMEM((depth, width), jnp.float32),
            pltpu.VMEM((width // 128, n_wide, 128), jnp.float32),
            pltpu.VMEM((width // 256, n_half, 128), jnp.float32),
            pltpu.VMEM((width // 512, rows // 4 + 8, 128), jnp.float32),
        ],
    )(resample_taps, where, low, scenes, high)


def smooth_operator(dates):
    clamp = np.zeros((dates, dates), np.float64)
    near = np.zeros((dates, dates), np.float64)
    for t in range(dates):
        for k in range(9):
            clamp[t, min(max(t + k - 4, 0), dates - 1)] += savgol_coeffs[k]
            if 0 <= t + k - 4 < dates:
                near[t, t + k - 4] = gap_weights[k]
    return clamp.astype(np.float32), near.astype(np.float32)


def smooth_coefficients(clear):
    dates = clear.shape[0]
    clamp, near = smooth_operator(dates)
    hi = lax.Precision.HIGHEST
    weight = 0.1 + 0.9 * clear
    denom = jnp.einsum("su,uxy->sxy", near, weight, precision=hi)
    gap = (1.0 - clear) / denom
    fill = near[:, :, None, None] * weight[None, :] * gap[:, None]
    fill = fill + np.eye(dates, dtype=np.float32)[:, :, None, None] * clear[None, :]
    return jnp.einsum("ts,suxy->tuxy", clamp, fill, precision=hi)


def split_three(a):
    high = a.astype(jnp.bfloat16)
    rest = a - high.astype(jnp.float32)
    mid = rest.astype(jnp.bfloat16)
    low = (rest - mid.astype(jnp.float32)).astype(jnp.bfloat16)
    return high, mid, low


def smooth_level(mask_cols, got_ref, start, piece, coeff_ref, out_ref, section_ref, tiles_ref):
    dates, bands, rows, width = out_ref.shape
    tiles = width // 128
    span = width // mask_cols
    section_ref[...] = got_ref[:, :, start : start + tiles * piece, :].astype(jnp.float32)
    parts = split_three(coeff_ref[...])
    m_at = lax.broadcasted_iota(jnp.int32, (128, 128), 0)
    lane = lax.broadcasted_iota(jnp.int32, (128, 128), 1)
    for j in range(tiles):
        pick = (m_at == (128 * j + lane) // span).astype(jnp.bfloat16)
        grown = mm(parts[0], pick) + mm(parts[1], pick) + mm(parts[2], pick)
        tiles_ref[...] = grown.reshape(tiles_ref.shape)

        step = min(rows, 8)

        def one_block(r, carry):
            r0 = pl.multiple_of(r * step, step)
            values = [
                [section_ref[u, band, pl.ds(j * piece + r0, step), :] for band in range(bands)]
                for u in range(dates)
            ]
            for t in range(dates):
                weights = [tiles_ref[t, u, pl.ds(r0, step), :] for u in range(dates)]
                for band in range(bands):
                    acc = weights[0] * values[0][band]
                    for u in range(1, dates):
                        acc = acc + weights[u] * values[u][band]
                    out_ref[t, band, pl.ds(r0, step), 128 * j : 128 * (j + 1)] = acc.astype(out_ref.dtype)
            return carry

        lax.fori_loop(0, rows // step, one_block, 0)


def smooth_kernel(mask_cols, pieces, got_ref, c0_ref, c1_ref, c2_ref, o0_ref, o1_ref, o2_ref,
                  s0_ref, s1_ref, s2_ref, t0_ref, t1_ref, t2_ref):
    start = 0
    levels = zip(pieces, (c0_ref, c1_ref, c2_ref), (o0_ref, o1_ref, o2_ref), (s0_ref, s1_ref, s2_ref), (t0_ref, t1_ref, t2_ref))
    for piece, c_ref, o_ref, s_ref, t_ref in levels:
        smooth_level(mask_cols, got_ref, start, piece, c_ref, o_ref, s_ref, t_ref)
        start += (o_ref.shape[3] // 128) * piece


def smooth_all(got, coeff, shapes, pieces):
    dates, bands = got.shape[:2]
    mask_cols = coeff.shape[3]
    flat = []
    for shape in shapes:
        grown = jnp.repeat(coeff, shape[2] // coeff.shape[2], axis=2)
        grown = grown.reshape(-1, mask_cols)
        flat.append(jnp.pad(grown, ((0, 0), (0, 128 - mask_cols))))
    full = lambda a: pl.BlockSpec(a.shape, lambda: (0,) * len(a.shape))
    outs = [jax.ShapeDtypeStruct(shape, jnp.bfloat16) for shape in shapes]
    return pl.pallas_call(
        functools.partial(smooth_kernel, mask_cols, pieces),
        in_specs=[full(got)] + [full(g) for g in flat],
        out_specs=[full(o) for o in outs],
        out_shape=outs,
        scratch_shapes=[
            pltpu.VMEM((dates, bands, (shape[3] // 128) * piece, 128), jnp.float32)
            for shape, piece in zip(shapes, pieces)
        ]
        + [pltpu.VMEM((dates, dates, shape[2], 128), jnp.float32) for shape in shapes],
    )(got, *flat)


def local(scenes, resample_taps, clear_mask):
    dates, bands, rows, width = scenes.shape
    band_index = lax.axis_index("row")
    total_rows = rows * lax.axis_size("row")
    ndate = lax.axis_size("date")
    count = lax.axis_size("row")
    forward = [(i, i + 1) for i in range(count - 1)]
    backward = [(target, source) for source, target in forward]
    low = lax.ppermute(scenes[:, :, rows - 8 :], "row", forward)
    high = lax.ppermute(scenes[:, :, :8], "row", backward)
    packed = pyramid(low, scenes, high, resample_taps, band_index, total_rows, ndate)
    coeff = smooth_coefficients(clear_mask.astype(jnp.float32))
    got = lax.all_to_all(packed, "date", split_axis=0, concat_axis=0, tiled=True)
    got = got.reshape((ndate * dates,) + got.shape[2:])
    fine = rows // ndate
    total = ndate * dates
    shapes = (
        (total, bands, fine, width),
        (total, bands, fine // 2, width // 2),
        (total, bands, fine // 4, width // 4),
    )
    return tuple(smooth_all(got, coeff, shapes, piece_rows(rows, ndate)))


def solution(mesh):
    in_specs = (P(("groups", "date"), None, "row", None), P(), P("groups", ("row", "date"), None))
    out_specs = (
        P("groups", None, ("row", "date"), None),
        P("groups", None, ("row", "date"), None),
        P("groups", None, ("row", "date"), None),
    )
    return jax.shard_map(local, mesh=mesh, in_specs=in_specs, out_specs=out_specs, check_vma=False)
```

```python
import functools
import math

import jax
import numpy as np
import jax.numpy as jnp
from jax import lax
from jax.sharding import PartitionSpec as P
from jax.experimental import pallas as pl
from jax.experimental.pallas import tpu as pltpu

gap_weights = [math.exp(-((k - 4) ** 2) / 8.0) for k in range(9)]
savgol_coeffs = [c / 231.0 for c in [-21.0, 14.0, 39.0, 54.0, 59.0, 54.0, 39.0, 14.0, -21.0]]
pyramid_filter = [0.125, 0.375, 0.375, 0.125]


def split_two(a):
    high = a.astype(jnp.bfloat16)
    low = (a - high.astype(jnp.float32)).astype(jnp.bfloat16)
    return high, low


def mm(a, b):
    return jnp.dot(a, b, preferred_element_type=jnp.float32)


def band_table(rows, cols, shift, taps):
    step, weights = taps
    s_at = lax.broadcasted_iota(jnp.int32, (rows, cols), 0)
    c_at = lax.broadcasted_iota(jnp.int32, (rows, cols), 1)
    place = s_at - step * c_at - shift
    total = jnp.zeros((rows, cols), jnp.float32)
    for k, w in enumerate(weights):
        total = total + jnp.where(place == k, w, 0.0)
    return total


def halve_columns(values, table, out_ref):
    width = values.shape[1]
    high, low = split_two(values)
    for j in range(width // 256):
        lo = max(256 * j - 128, 0)
        hi_col = min(256 * j + 384, width)
        first = lo - (256 * j - 128)
        last = first + (hi_col - lo)
        part = table[first:last]
        out_ref[j, 0 : values.shape[0]] = mm(high[:, lo:hi_col], part) + mm(low[:, lo:hi_col], part)


def halve_rows(source_ref, count):
    total = pyramid_filter[0] * source_ref[:, pl.ds(0, count, stride=2), :]
    for p in range(1, 4):
        total = total + pyramid_filter[p] * source_ref[:, pl.ds(p, count, stride=2), :]
    return jnp.concatenate([total[j] for j in range(total.shape[0])], axis=1)


def piece_rows(rows, ndate):
    fine = rows // ndate
    return (fine, max(fine // 2, 8), max(fine // 4, 8))


def pyramid_kernel(ndate, total_rows, taps_ref, where_ref, low_ref, x_ref, high_ref, packed_ref,
                   across_ref, wide_ref, half_ref, quarter_ref):
    b = pl.program_id(1)
    rows = x_ref.shape[2]
    width = x_ref.shape[3]
    edge = low_ref.shape[2]
    tiles = width // 128
    column = [taps_ref[0, b, k] for k in range(7)]
    row = [taps_ref[1, b, k] for k in range(7)]
    table = band_table(3 * 128, 128, 125, (1, column))
    t_high = table.astype(jnp.bfloat16)
    rest = table - t_high.astype(jnp.float32)
    t_mid = rest.astype(jnp.bfloat16)
    t_low = (rest - t_mid.astype(jnp.float32)).astype(jnp.bfloat16)
    sources = ((low_ref, 0), (x_ref, edge), (high_ref, edge + rows))
    for source_ref, at in sources:
        x = source_ref[0, 0]
        count = x.shape[0]
        for j in range(tiles):
            lo = max(j - 1, 0) * 128
            hi_col = min(j + 2, tiles) * 128
            first = lo - (j - 1) * 128
            last = first + (hi_col - lo)
            window = x[:, lo:hi_col]
            acc = mm(window, t_high[first:last]) + mm(window, t_mid[first:last]) + mm(window, t_low[first:last])
            across_ref[at : at + count, j * 128 : (j + 1) * 128] = acc
    used = 2 * edge + rows
    depth = across_ref.shape[0]
    across_ref[used:depth, :] = jnp.zeros((depth - used, width), jnp.float32)
    band_index = where_ref[0]
    n_wide = wide_ref.shape[1]
    wide_at = lax.broadcasted_iota(jnp.int32, (n_wide, 128), 0)
    wide_row = band_index * rows - 3 + wide_at
    keep_wide = ((wide_row >= 0) & (wide_row < total_rows) & (wide_at < rows + 6)).astype(jnp.float32)
    shift = edge - 6
    for j in range(tiles):
        cols = slice(128 * j, 128 * (j + 1))
        total = row[0] * across_ref[pl.ds(shift, n_wide), cols]
        for k in range(1, 7):
            total = total + row[k] * across_ref[pl.ds(shift + k, n_wide), cols]
        wide_ref[j] = total * keep_wide
    n_half = half_ref.shape[1]
    half_at = lax.broadcasted_iota(jnp.int32, (n_half, 1), 0)
    half_row = band_index * (rows // 2) - 1 + half_at
    keep_half = ((half_row >= 0) & (half_row < total_rows // 2) & (half_at < rows // 2 + 2)).astype(jnp.float32)
    halves = halve_rows(wide_ref, n_half) * keep_half
    down = band_table(512, 128, 127, (2, pyramid_filter)).astype(jnp.bfloat16)
    halve_columns(halves, down, half_ref)
    quarters = halve_rows(half_ref, rows // 4)
    n_quarter = quarter_ref.shape[1]
    quarter_ref[:, rows // 4 : n_quarter, :] = jnp.zeros((tiles // 4, n_quarter - rows // 4, 128), jnp.float32)
    halve_columns(quarters, down, quarter_ref)
    fine, p_half, p_quarter = piece_rows(rows, ndate)
    for q in range(ndate):
        parts = [wide_ref[j, pl.ds(3 + fine * q, fine), :] for j in range(tiles)]
        parts += [half_ref[j, pl.ds(1 + (fine // 2) * q, p_half), :] for j in range(tiles // 2)]
        parts += [quarter_ref[j, pl.ds((fine // 4) * q, p_quarter), :] for j in range(tiles // 4)]
        packed_ref[q, 0, 0] = jnp.concatenate(parts, axis=0).astype(packed_ref.dtype)


def pyramid(low, scenes, high, resample_taps, band_index, total_rows, ndate):
    dates, bands, rows, width = scenes.shape
    edge = low.shape[2]
    n_wide = rows + 24
    n_half = rows // 2 + 8
    depth = max(n_wide + 8, 2 * edge + rows)
    fine, p_half, p_quarter = piece_rows(rows, ndate)
    count = (width // 128) * fine + (width // 256) * p_half + (width // 512) * p_quarter
    where = jnp.reshape(band_index, (1,)).astype(jnp.int32)
    return pl.pallas_call(
        functools.partial(pyramid_kernel, ndate, total_rows),
        grid=(dates, bands),
        in_specs=[
            pl.BlockSpec(memory_space=pltpu.SMEM),
            pl.BlockSpec(memory_space=pltpu.SMEM),
            pl.BlockSpec((1, 1, edge, width), lambda d, b: (d, b, 0, 0)),
            pl.BlockSpec((1, 1, rows, width), lambda d, b: (d, b, 0, 0)),
            pl.BlockSpec((1, 1, edge, width), lambda d, b: (d, b, 0, 0)),
        ],
        out_specs=pl.BlockSpec((ndate, 1, 1, count, 128), lambda d, b: (0, d, b, 0, 0)),
        out_shape=jax.ShapeDtypeStruct((ndate, dates, bands, count, 128), jnp.bfloat16),
        scratch_shapes=[
            pltpu.VMEM((depth, width), jnp.float32),
            pltpu.VMEM((width // 128, n_wide, 128), jnp.float32),
            pltpu.VMEM((width // 256, n_half, 128), jnp.float32),
            pltpu.VMEM((width // 512, rows // 4 + 8, 128), jnp.float32),
        ],
    )(resample_taps, where, low, scenes, high)


def smooth_operator(dates):
    clamp = np.zeros((dates, dates), np.float64)
    near = np.zeros((dates, dates), np.float64)
    for t in range(dates):
        for k in range(9):
            clamp[t, min(max(t + k - 4, 0), dates - 1)] += savgol_coeffs[k]
            if 0 <= t + k - 4 < dates:
                near[t, t + k - 4] = gap_weights[k]
    return clamp.astype(np.float32), near.astype(np.float32)


def smooth_coefficients(clear):
    dates = clear.shape[0]
    clamp, near = smooth_operator(dates)
    hi = lax.Precision.HIGHEST
    weight = 0.1 + 0.9 * clear
    denom = jnp.einsum("su,uxy->sxy", near, weight, precision=hi)
    gap = (1.0 - clear) / denom
    fill = near[:, :, None, None] * weight[None, :] * gap[:, None]
    fill = fill + np.eye(dates, dtype=np.float32)[:, :, None, None] * clear[None, :]
    return jnp.einsum("ts,suxy->tuxy", clamp, fill, precision=hi)


def split_three(a):
    high = a.astype(jnp.bfloat16)
    rest = a - high.astype(jnp.float32)
    mid = rest.astype(jnp.bfloat16)
    low = (rest - mid.astype(jnp.float32)).astype(jnp.bfloat16)
    return high, mid, low


def smooth_level(mask_cols, got_ref, start, piece, coeff_ref, out_ref, section_ref, tiles_ref):
    dates, bands, rows, width = out_ref.shape
    tiles = width // 128
    span = width // mask_cols
    section_ref[...] = got_ref[:, :, start : start + tiles * piece, :].astype(jnp.float32)
    parts = split_three(coeff_ref[...])
    m_at = lax.broadcasted_iota(jnp.int32, (128, 128), 0)
    lane = lax.broadcasted_iota(jnp.int32, (128, 128), 1)
    for j in range(tiles):
        pick = (m_at == (128 * j + lane) // span).astype(jnp.bfloat16)
        grown = mm(parts[0], pick) + mm(parts[1], pick) + mm(parts[2], pick)
        tiles_ref[...] = grown.reshape(tiles_ref.shape)

        step = min(rows, 8)

        def one_block(r, carry):
            r0 = pl.multiple_of(r * step, step)
            values = [
                [section_ref[u, band, pl.ds(j * piece + r0, step), :] for band in range(bands)]
                for u in range(dates)
            ]
            for t in range(dates):
                weights = [tiles_ref[t, u, pl.ds(r0, step), :] for u in range(dates)]
                for band in range(bands):
                    acc = weights[0] * values[0][band]
                    for u in range(1, dates):
                        acc = acc + weights[u] * values[u][band]
                    out_ref[t, band, pl.ds(r0, step), 128 * j : 128 * (j + 1)] = acc.astype(out_ref.dtype)
            return carry

        lax.fori_loop(0, rows // step, one_block, 0)


def smooth_kernel(mask_cols, pieces, got_ref, c0_ref, c1_ref, c2_ref, *rest):
    o0_ref, o1_ref, o2_ref, s0_ref, s1_ref, s2_ref, t0_ref, t1_ref, t2_ref = rest[-9:]
    start = 0
    levels = zip(pieces, (c0_ref, c1_ref, c2_ref), (o0_ref, o1_ref, o2_ref), (s0_ref, s1_ref, s2_ref), (t0_ref, t1_ref, t2_ref))
    for piece, c_ref, o_ref, s_ref, t_ref in levels:
        smooth_level(mask_cols, got_ref, start, piece, c_ref, o_ref, s_ref, t_ref)
        start += (o_ref.shape[3] // 128) * piece


def smooth_all(got, flat, shapes, pieces, mask_cols, chunk, previous):
    dates, bands = got.shape[:2]
    full = lambda a: pl.BlockSpec(a.shape, lambda i: (0,) * len(a.shape))
    outs = [jax.ShapeDtypeStruct(shape, jnp.bfloat16) for shape in shapes]
    out_specs = [pl.BlockSpec((dates, bands) + shape[2:], lambda i: (0, chunk, 0, 0)) for shape in shapes]
    in_specs = [full(got)] + [full(g) for g in flat]
    args = [got] + list(flat)
    aliases = {}
    if previous is not None:
        for i, prev in enumerate(previous):
            aliases[len(args)] = i
            in_specs.append(pl.BlockSpec(memory_space=pl.ANY))
            args.append(prev)
    return pl.pallas_call(
        functools.partial(smooth_kernel, mask_cols, pieces),
        grid=(1,),
        in_specs=in_specs,
        out_specs=out_specs,
        out_shape=outs,
        input_output_aliases=aliases,
        scratch_shapes=[
            pltpu.VMEM((dates, bands, (shape[3] // 128) * piece, 128), jnp.float32)
            for shape, piece in zip(shapes, pieces)
        ]
        + [pltpu.VMEM((dates, dates, shape[2], 128), jnp.float32) for shape in shapes],
    )(*args)


def local(scenes, resample_taps, clear_mask):
    dates, bands, rows, width = scenes.shape
    band_index = lax.axis_index("row")
    total_rows = rows * lax.axis_size("row")
    ndate = lax.axis_size("date")
    count = lax.axis_size("row")
    forward = [(i, i + 1) for i in range(count - 1)]
    backward = [(target, source) for source, target in forward]
    low = lax.ppermute(scenes[:, :, rows - 8 :], "row", forward)
    high = lax.ppermute(scenes[:, :, :8], "row", backward)
    coeff = smooth_coefficients(clear_mask.astype(jnp.float32))
    fine = rows // ndate
    total = ndate * dates
    shapes = (
        (total, bands, fine, width),
        (total, bands, fine // 2, width // 2),
        (total, bands, fine // 4, width // 4),
    )
    mask_cols = coeff.shape[3]
    flat = []
    for shape in shapes:
        grown = jnp.repeat(coeff, shape[2] // coeff.shape[2], axis=2).reshape(-1, mask_cols)
        flat.append(jnp.pad(grown, ((0, 0), (0, 128 - mask_cols))))
    pieces = piece_rows(rows, ndate)
    chunks = 2 if bands % 2 == 0 else 1
    step = bands // chunks
    outs = None
    for chunk in range(chunks):
        part = slice(chunk * step, (chunk + 1) * step)
        packed = pyramid(low[:, part], scenes[:, part], high[:, part], resample_taps[:, part],
                         band_index, total_rows, ndate)
        got = lax.all_to_all(packed, "date", split_axis=0, concat_axis=0, tiled=True)
        got = got.reshape((total,) + got.shape[2:])
        outs = smooth_all(got, flat, shapes, pieces, mask_cols, chunk, outs)
    return tuple(outs)


def solution(mesh):
    in_specs = (P(("groups", "date"), None, "row", None), P(), P("groups", ("row", "date"), None))
    out_specs = (
        P("groups", None, ("row", "date"), None),
        P("groups", None, ("row", "date"), None),
        P("groups", None, ("row", "date"), None),
    )
    return jax.shard_map(local, mesh=mesh, in_specs=in_specs, out_specs=out_specs, check_vma=False)
```

```python
import functools
import math

import jax
import numpy as np
import jax.numpy as jnp
from jax import lax
from jax.sharding import PartitionSpec as P
from jax.experimental import pallas as pl
from jax.experimental.pallas import tpu as pltpu

gap_weights = [math.exp(-((k - 4) ** 2) / 8.0) for k in range(9)]
savgol_coeffs = [c / 231.0 for c in [-21.0, 14.0, 39.0, 54.0, 59.0, 54.0, 39.0, 14.0, -21.0]]
pyramid_filter = [0.125, 0.375, 0.375, 0.125]


def split_two(a):
    high = a.astype(jnp.bfloat16)
    low = (a - high.astype(jnp.float32)).astype(jnp.bfloat16)
    return high, low


def mm(a, b):
    return jnp.dot(a, b, preferred_element_type=jnp.float32)


def band_table(rows, cols, shift, taps):
    step, weights = taps
    s_at = lax.broadcasted_iota(jnp.int32, (rows, cols), 0)
    c_at = lax.broadcasted_iota(jnp.int32, (rows, cols), 1)
    place = s_at - step * c_at - shift
    total = jnp.zeros((rows, cols), jnp.float32)
    for k, w in enumerate(weights):
        total = total + jnp.where(place == k, w, 0.0)
    return total


def halve_columns(values, table, out_ref):
    width = values.shape[1]
    high, low = split_two(values)
    for j in range(width // 256):
        lo = max(256 * j - 128, 0)
        hi_col = min(256 * j + 384, width)
        first = lo - (256 * j - 128)
        last = first + (hi_col - lo)
        part = table[first:last]
        out_ref[j, 0 : values.shape[0]] = mm(high[:, lo:hi_col], part) + mm(low[:, lo:hi_col], part)


def halve_rows(source_ref, count):
    total = pyramid_filter[0] * source_ref[:, pl.ds(0, count, stride=2), :]
    for p in range(1, 4):
        total = total + pyramid_filter[p] * source_ref[:, pl.ds(p, count, stride=2), :]
    return jnp.concatenate([total[j] for j in range(total.shape[0])], axis=1)


def piece_rows(rows, ndate):
    fine = rows // ndate
    return (fine, max(fine // 2, 8), max(fine // 4, 8))


def pyramid_kernel(ndate, total_rows, taps_ref, where_ref, low_ref, x_ref, high_ref, packed_ref,
                   across_ref, wide_ref, half_ref, quarter_ref):
    b = pl.program_id(1)
    rows = x_ref.shape[2]
    width = x_ref.shape[3]
    edge = low_ref.shape[2]
    tiles = width // 128
    column = [taps_ref[0, b, k] for k in range(7)]
    row = [taps_ref[1, b, k] for k in range(7)]
    table = band_table(3 * 128, 128, 125, (1, column))
    t_high = table.astype(jnp.bfloat16)
    rest = table - t_high.astype(jnp.float32)
    t_mid = rest.astype(jnp.bfloat16)
    t_low = (rest - t_mid.astype(jnp.float32)).astype(jnp.bfloat16)
    sources = ((low_ref, 0), (x_ref, edge), (high_ref, edge + rows))
    for source_ref, at in sources:
        x = source_ref[0, 0]
        count = x.shape[0]
        for j in range(tiles):
            lo = max(j - 1, 0) * 128
            hi_col = min(j + 2, tiles) * 128
            first = lo - (j - 1) * 128
            last = first + (hi_col - lo)
            window = x[:, lo:hi_col]
            acc = mm(window, t_high[first:last]) + mm(window, t_mid[first:last]) + mm(window, t_low[first:last])
            across_ref[at : at + count, j * 128 : (j + 1) * 128] = acc
    used = 2 * edge + rows
    depth = across_ref.shape[0]
    across_ref[used:depth, :] = jnp.zeros((depth - used, width), jnp.float32)
    band_index = where_ref[0]
    n_wide = wide_ref.shape[1]
    wide_at = lax.broadcasted_iota(jnp.int32, (n_wide, 128), 0)
    wide_row = band_index * rows - 3 + wide_at
    keep_wide = ((wide_row >= 0) & (wide_row < total_rows) & (wide_at < rows + 6)).astype(jnp.float32)
    shift = edge - 6
    for j in range(tiles):
        cols = slice(128 * j, 128 * (j + 1))
        total = row[0] * across_ref[pl.ds(shift, n_wide), cols]
        for k in range(1, 7):
            total = total + row[k] * across_ref[pl.ds(shift + k, n_wide), cols]
        wide_ref[j] = total * keep_wide
    n_half = half_ref.shape[1]
    half_at = lax.broadcasted_iota(jnp.int32, (n_half, 1), 0)
    half_row = band_index * (rows // 2) - 1 + half_at
    keep_half = ((half_row >= 0) & (half_row < total_rows // 2) & (half_at < rows // 2 + 2)).astype(jnp.float32)
    halves = halve_rows(wide_ref, n_half) * keep_half
    down = band_table(512, 128, 127, (2, pyramid_filter)).astype(jnp.bfloat16)
    halve_columns(halves, down, half_ref)
    quarters = halve_rows(half_ref, rows // 4)
    n_quarter = quarter_ref.shape[1]
    quarter_ref[:, rows // 4 : n_quarter, :] = jnp.zeros((tiles // 4, n_quarter - rows // 4, 128), jnp.float32)
    halve_columns(quarters, down, quarter_ref)
    fine, p_half, p_quarter = piece_rows(rows, ndate)
    for q in range(ndate):
        parts = [wide_ref[j, pl.ds(3 + fine * q, fine), :] for j in range(tiles)]
        parts += [half_ref[j, pl.ds(1 + (fine // 2) * q, p_half), :] for j in range(tiles // 2)]
        parts += [quarter_ref[j, pl.ds((fine // 4) * q, p_quarter), :] for j in range(tiles // 4)]
        packed_ref[q, 0, 0] = jnp.concatenate(parts, axis=0).astype(packed_ref.dtype)


def pyramid(low, scenes, high, resample_taps, band_index, total_rows, ndate):
    dates, bands, rows, width = scenes.shape
    edge = low.shape[2]
    n_wide = rows + 24
    n_half = rows // 2 + 8
    depth = max(n_wide + 8, 2 * edge + rows)
    fine, p_half, p_quarter = piece_rows(rows, ndate)
    count = (width // 128) * fine + (width // 256) * p_half + (width // 512) * p_quarter
    where = jnp.reshape(band_index, (1,)).astype(jnp.int32)
    return pl.pallas_call(
        functools.partial(pyramid_kernel, ndate, total_rows),
        grid=(dates, bands),
        in_specs=[
            pl.BlockSpec(memory_space=pltpu.SMEM),
            pl.BlockSpec(memory_space=pltpu.SMEM),
            pl.BlockSpec((1, 1, edge, width), lambda d, b: (d, b, 0, 0)),
            pl.BlockSpec((1, 1, rows, width), lambda d, b: (d, b, 0, 0)),
            pl.BlockSpec((1, 1, edge, width), lambda d, b: (d, b, 0, 0)),
        ],
        out_specs=pl.BlockSpec((ndate, 1, 1, count, 128), lambda d, b: (0, d, b, 0, 0)),
        out_shape=jax.ShapeDtypeStruct((ndate, dates, bands, count, 128), jnp.bfloat16),
        scratch_shapes=[
            pltpu.VMEM((depth, width), jnp.float32),
            pltpu.VMEM((width // 128, n_wide, 128), jnp.float32),
            pltpu.VMEM((width // 256, n_half, 128), jnp.float32),
            pltpu.VMEM((width // 512, rows // 4 + 8, 128), jnp.float32),
        ],
    )(resample_taps, where, low, scenes, high)


def smooth_operator(dates):
    clamp = np.zeros((dates, dates), np.float64)
    near = np.zeros((dates, dates), np.float64)
    for t in range(dates):
        for k in range(9):
            clamp[t, min(max(t + k - 4, 0), dates - 1)] += savgol_coeffs[k]
            if 0 <= t + k - 4 < dates:
                near[t, t + k - 4] = gap_weights[k]
    return clamp.astype(np.float32), near.astype(np.float32)


def smooth_coefficients(clear):
    dates = clear.shape[0]
    clamp, near = smooth_operator(dates)
    hi = lax.Precision.HIGHEST
    weight = 0.1 + 0.9 * clear
    denom = jnp.einsum("su,uxy->sxy", near, weight, precision=hi)
    gap = (1.0 - clear) / denom
    fill = near[:, :, None, None] * weight[None, :] * gap[:, None]
    fill = fill + np.eye(dates, dtype=np.float32)[:, :, None, None] * clear[None, :]
    return jnp.einsum("ts,suxy->tuxy", clamp, fill, precision=hi)


def smooth_level(mask_cols, got_ref, start, piece, coeff_ref, out_ref, section_ref, tiles_ref):
    dates, bands, rows, width = out_ref.shape
    tiles = width // 128
    span = width // mask_cols
    section_ref[...] = got_ref[:, :, start : start + tiles * piece, :].astype(jnp.float32)
    parts = split_two(coeff_ref[...])
    m_at = lax.broadcasted_iota(jnp.int32, (128, 128), 0)
    lane = lax.broadcasted_iota(jnp.int32, (128, 128), 1)
    for j in range(tiles):
        pick = (m_at == (128 * j + lane) // span).astype(jnp.bfloat16)
        grown = mm(parts[0], pick) + mm(parts[1], pick)
        tiles_ref[...] = grown.reshape(tiles_ref.shape)

        step = min(rows, 8)

        def one_block(r, carry):
            r0 = pl.multiple_of(r * step, step)
            values = [
                [section_ref[u, band, pl.ds(j * piece + r0, step), :] for band in range(bands)]
                for u in range(dates)
            ]
            for t in range(dates):
                weights = [tiles_ref[t, u, pl.ds(r0, step), :] for u in range(dates)]
                for band in range(bands):
                    acc = weights[0] * values[0][band]
                    for u in range(1, dates):
                        acc = acc + weights[u] * values[u][band]
                    out_ref[t, band, pl.ds(r0, step), 128 * j : 128 * (j + 1)] = acc.astype(out_ref.dtype)
            return carry

        lax.fori_loop(0, rows // step, one_block, 0)


def smooth_kernel(mask_cols, pieces, got_ref, c0_ref, c1_ref, c2_ref, o0_ref, o1_ref, o2_ref,
                  s0_ref, s1_ref, s2_ref, t0_ref, t1_ref, t2_ref):
    start = 0
    levels = zip(pieces, (c0_ref, c1_ref, c2_ref), (o0_ref, o1_ref, o2_ref), (s0_ref, s1_ref, s2_ref), (t0_ref, t1_ref, t2_ref))
    for piece, c_ref, o_ref, s_ref, t_ref in levels:
        smooth_level(mask_cols, got_ref, start, piece, c_ref, o_ref, s_ref, t_ref)
        start += (o_ref.shape[3] // 128) * piece


def smooth_all(got, coeff, shapes, pieces):
    dates, bands = got.shape[:2]
    mask_cols = coeff.shape[3]
    flat = []
    for shape in shapes:
        grown = jnp.repeat(coeff, shape[2] // coeff.shape[2], axis=2)
        grown = grown.reshape(-1, mask_cols)
        flat.append(jnp.pad(grown, ((0, 0), (0, 128 - mask_cols))))
    full = lambda a: pl.BlockSpec(a.shape, lambda: (0,) * len(a.shape))
    outs = [jax.ShapeDtypeStruct(shape, jnp.bfloat16) for shape in shapes]
    return pl.pallas_call(
        functools.partial(smooth_kernel, mask_cols, pieces),
        in_specs=[full(got)] + [full(g) for g in flat],
        out_specs=[full(o) for o in outs],
        out_shape=outs,
        scratch_shapes=[
            pltpu.VMEM((dates, bands, (shape[3] // 128) * piece, 128), jnp.float32)
            for shape, piece in zip(shapes, pieces)
        ]
        + [pltpu.VMEM((dates, dates, shape[2], 128), jnp.float32) for shape in shapes],
    )(got, *flat)


def local(scenes, resample_taps, clear_mask):
    dates, bands, rows, width = scenes.shape
    band_index = lax.axis_index("row")
    total_rows = rows * lax.axis_size("row")
    ndate = lax.axis_size("date")
    count = lax.axis_size("row")
    forward = [(i, i + 1) for i in range(count - 1)]
    backward = [(target, source) for source, target in forward]
    low = lax.ppermute(scenes[:, :, rows - 8 :], "row", forward)
    high = lax.ppermute(scenes[:, :, :8], "row", backward)
    packed = pyramid(low, scenes, high, resample_taps, band_index, total_rows, ndate)
    coeff = smooth_coefficients(clear_mask.astype(jnp.float32))
    got = lax.all_to_all(packed, "date", split_axis=0, concat_axis=0, tiled=True)
    got = got.reshape((ndate * dates,) + got.shape[2:])
    fine = rows // ndate
    total = ndate * dates
    shapes = (
        (total, bands, fine, width),
        (total, bands, fine // 2, width // 2),
        (total, bands, fine // 4, width // 4),
    )
    return tuple(smooth_all(got, coeff, shapes, piece_rows(rows, ndate)))


def solution(mesh):
    in_specs = (P(("groups", "date"), None, "row", None), P(), P("groups", ("row", "date"), None))
    out_specs = (
        P("groups", None, ("row", "date"), None),
        P("groups", None, ("row", "date"), None),
        P("groups", None, ("row", "date"), None),
    )
    return jax.shard_map(local, mesh=mesh, in_specs=in_specs, out_specs=out_specs, check_vma=False)
```

```python
import functools
import math

import jax
import numpy as np
import jax.numpy as jnp
from jax import lax
from jax.sharding import PartitionSpec as P
from jax.experimental import pallas as pl
from jax.experimental.pallas import tpu as pltpu

gap_weights = [math.exp(-((k - 4) ** 2) / 8.0) for k in range(9)]
savgol_coeffs = [c / 231.0 for c in [-21.0, 14.0, 39.0, 54.0, 59.0, 54.0, 39.0, 14.0, -21.0]]
pyramid_filter = [0.125, 0.375, 0.375, 0.125]


def split_two(a):
    high = a.astype(jnp.bfloat16)
    low = (a - high.astype(jnp.float32)).astype(jnp.bfloat16)
    return high, low


def mm(a, b):
    return jnp.dot(a, b, preferred_element_type=jnp.float32)


def band_table(rows, cols, shift, taps):
    step, weights = taps
    s_at = lax.broadcasted_iota(jnp.int32, (rows, cols), 0)
    c_at = lax.broadcasted_iota(jnp.int32, (rows, cols), 1)
    place = s_at - step * c_at - shift
    total = jnp.zeros((rows, cols), jnp.float32)
    for k, w in enumerate(weights):
        total = total + jnp.where(place == k, w, 0.0)
    return total


def halve_columns(values, table, out_ref):
    width = values.shape[1]
    high, low = split_two(values)
    for j in range(width // 256):
        lo = max(256 * j - 128, 0)
        hi_col = min(256 * j + 384, width)
        first = lo - (256 * j - 128)
        last = first + (hi_col - lo)
        part = table[first:last]
        out_ref[j, 0 : values.shape[0]] = mm(high[:, lo:hi_col], part) + mm(low[:, lo:hi_col], part)


def halve_rows(source_ref, count):
    total = pyramid_filter[0] * source_ref[:, pl.ds(0, count, stride=2), :]
    for p in range(1, 4):
        total = total + pyramid_filter[p] * source_ref[:, pl.ds(p, count, stride=2), :]
    return jnp.concatenate([total[j] for j in range(total.shape[0])], axis=1)


def piece_rows(rows, ndate):
    fine = rows // ndate
    return (fine, max(fine // 2, 8), max(fine // 4, 8))


def pyramid_kernel(ndate, total_rows, taps_ref, where_ref, low_ref, x_ref, high_ref, packed_ref,
                   across_ref, wide_ref, half_ref, quarter_ref):
    b = pl.program_id(1)
    rows = x_ref.shape[2]
    width = x_ref.shape[3]
    edge = low_ref.shape[2]
    tiles = width // 128
    column = [taps_ref[0, b, k] for k in range(7)]
    row = [taps_ref[1, b, k] for k in range(7)]
    table = band_table(3 * 128, 128, 125, (1, column))
    t_high, t_low = split_two(table)
    sources = ((low_ref, 0), (x_ref, edge), (high_ref, edge + rows))
    for source_ref, at in sources:
        x = source_ref[0, 0]
        count = x.shape[0]
        for j in range(tiles):
            lo = max(j - 1, 0) * 128
            hi_col = min(j + 2, tiles) * 128
            first = lo - (j - 1) * 128
            last = first + (hi_col - lo)
            window = x[:, lo:hi_col]
            acc = mm(window, t_high[first:last]) + mm(window, t_low[first:last])
            across_ref[at : at + count, j * 128 : (j + 1) * 128] = acc
    used = 2 * edge + rows
    depth = across_ref.shape[0]
    across_ref[used:depth, :] = jnp.zeros((depth - used, width), jnp.float32)
    band_index = where_ref[0]
    n_wide = wide_ref.shape[1]
    wide_at = lax.broadcasted_iota(jnp.int32, (n_wide, 128), 0)
    wide_row = band_index * rows - 3 + wide_at
    keep_wide = ((wide_row >= 0) & (wide_row < total_rows) & (wide_at < rows + 6)).astype(jnp.float32)
    shift = edge - 6
    for j in range(tiles):
        cols = slice(128 * j, 128 * (j + 1))
        total = row[0] * across_ref[pl.ds(shift, n_wide), cols]
        for k in range(1, 7):
            total = total + row[k] * across_ref[pl.ds(shift + k, n_wide), cols]
        wide_ref[j] = total * keep_wide
    n_half = half_ref.shape[1]
    half_at = lax.broadcasted_iota(jnp.int32, (n_half, 1), 0)
    half_row = band_index * (rows // 2) - 1 + half_at
    keep_half = ((half_row >= 0) & (half_row < total_rows // 2) & (half_at < rows // 2 + 2)).astype(jnp.float32)
    halves = halve_rows(wide_ref, n_half) * keep_half
    down = band_table(512, 128, 127, (2, pyramid_filter)).astype(jnp.bfloat16)
    halve_columns(halves, down, half_ref)
    quarters = halve_rows(half_ref, rows // 4)
    n_quarter = quarter_ref.shape[1]
    quarter_ref[:, rows // 4 : n_quarter, :] = jnp.zeros((tiles // 4, n_quarter - rows // 4, 128), jnp.float32)
    halve_columns(quarters, down, quarter_ref)
    fine, p_half, p_quarter = piece_rows(rows, ndate)
    for q in range(ndate):
        parts = [wide_ref[j, pl.ds(3 + fine * q, fine), :] for j in range(tiles)]
        parts += [half_ref[j, pl.ds(1 + (fine // 2) * q, p_half), :] for j in range(tiles // 2)]
        parts += [quarter_ref[j, pl.ds((fine // 4) * q, p_quarter), :] for j in range(tiles // 4)]
        packed_ref[q, 0, 0] = jnp.concatenate(parts, axis=0).astype(packed_ref.dtype)


def pyramid(low, scenes, high, resample_taps, band_index, total_rows, ndate):
    dates, bands, rows, width = scenes.shape
    edge = low.shape[2]
    n_wide = rows + 24
    n_half = rows // 2 + 8
    depth = max(n_wide + 8, 2 * edge + rows)
    fine, p_half, p_quarter = piece_rows(rows, ndate)
    count = (width // 128) * fine + (width // 256) * p_half + (width // 512) * p_quarter
    where = jnp.reshape(band_index, (1,)).astype(jnp.int32)
    return pl.pallas_call(
        functools.partial(pyramid_kernel, ndate, total_rows),
        grid=(dates, bands),
        in_specs=[
            pl.BlockSpec(memory_space=pltpu.SMEM),
            pl.BlockSpec(memory_space=pltpu.SMEM),
            pl.BlockSpec((1, 1, edge, width), lambda d, b: (d, b, 0, 0)),
            pl.BlockSpec((1, 1, rows, width), lambda d, b: (d, b, 0, 0)),
            pl.BlockSpec((1, 1, edge, width), lambda d, b: (d, b, 0, 0)),
        ],
        out_specs=pl.BlockSpec((ndate, 1, 1, count, 128), lambda d, b: (0, d, b, 0, 0)),
        out_shape=jax.ShapeDtypeStruct((ndate, dates, bands, count, 128), jnp.bfloat16),
        scratch_shapes=[
            pltpu.VMEM((depth, width), jnp.float32),
            pltpu.VMEM((width // 128, n_wide, 128), jnp.float32),
            pltpu.VMEM((width // 256, n_half, 128), jnp.float32),
            pltpu.VMEM((width // 512, rows // 4 + 8, 128), jnp.float32),
        ],
    )(resample_taps, where, low, scenes, high)


def smooth_operator(dates):
    clamp = np.zeros((dates, dates), np.float64)
    near = np.zeros((dates, dates), np.float64)
    for t in range(dates):
        for k in range(9):
            clamp[t, min(max(t + k - 4, 0), dates - 1)] += savgol_coeffs[k]
            if 0 <= t + k - 4 < dates:
                near[t, t + k - 4] = gap_weights[k]
    return clamp.astype(np.float32), near.astype(np.float32)


def smooth_coefficients(clear):
    dates = clear.shape[0]
    clamp, near = smooth_operator(dates)
    hi = lax.Precision.HIGHEST
    weight = 0.1 + 0.9 * clear
    denom = jnp.einsum("su,uxy->sxy", near, weight, precision=hi)
    gap = (1.0 - clear) / denom
    fill = near[:, :, None, None] * weight[None, :] * gap[:, None]
    fill = fill + np.eye(dates, dtype=np.float32)[:, :, None, None] * clear[None, :]
    return jnp.einsum("ts,suxy->tuxy", clamp, fill, precision=hi)


def smooth_level(mask_cols, got_ref, start, piece, coeff_ref, out_ref, section_ref, tiles_ref):
    dates, bands, rows, width = out_ref.shape
    tiles = width // 128
    span = width // mask_cols
    section_ref[...] = got_ref[:, :, start : start + tiles * piece, :].astype(jnp.float32)
    parts = split_two(coeff_ref[...])
    m_at = lax.broadcasted_iota(jnp.int32, (128, 128), 0)
    lane = lax.broadcasted_iota(jnp.int32, (128, 128), 1)
    for j in range(tiles):
        pick = (m_at == (128 * j + lane) // span).astype(jnp.bfloat16)
        grown = mm(parts[0], pick) + mm(parts[1], pick)
        tiles_ref[...] = grown.reshape(tiles_ref.shape)

        step = min(rows, 8)

        def one_block(r, carry):
            r0 = pl.multiple_of(r * step, step)
            values = [
                [section_ref[u, band, pl.ds(j * piece + r0, step), :] for band in range(bands)]
                for u in range(dates)
            ]
            for t in range(dates):
                weights = [tiles_ref[t, u, pl.ds(r0, step), :] for u in range(dates)]
                for band in range(bands):
                    acc = weights[0] * values[0][band]
                    for u in range(1, dates):
                        acc = acc + weights[u] * values[u][band]
                    out_ref[t, band, pl.ds(r0, step), 128 * j : 128 * (j + 1)] = acc.astype(out_ref.dtype)
            return carry

        lax.fori_loop(0, rows // step, one_block, 0)


def smooth_kernel(mask_cols, pieces, got_ref, c0_ref, c1_ref, c2_ref, o0_ref, o1_ref, o2_ref,
                  s0_ref, s1_ref, s2_ref, t0_ref, t1_ref, t2_ref):
    start = 0
    levels = zip(pieces, (c0_ref, c1_ref, c2_ref), (o0_ref, o1_ref, o2_ref), (s0_ref, s1_ref, s2_ref), (t0_ref, t1_ref, t2_ref))
    for piece, c_ref, o_ref, s_ref, t_ref in levels:
        smooth_level(mask_cols, got_ref, start, piece, c_ref, o_ref, s_ref, t_ref)
        start += (o_ref.shape[3] // 128) * piece


def smooth_all(got, coeff, shapes, pieces):
    dates, bands = got.shape[:2]
    mask_cols = coeff.shape[3]
    flat = []
    for shape in shapes:
        grown = jnp.repeat(coeff, shape[2] // coeff.shape[2], axis=2)
        grown = grown.reshape(-1, mask_cols)
        flat.append(jnp.pad(grown, ((0, 0), (0, 128 - mask_cols))))
    full = lambda a: pl.BlockSpec(a.shape, lambda: (0,) * len(a.shape))
    outs = [jax.ShapeDtypeStruct(shape, jnp.bfloat16) for shape in shapes]
    return pl.pallas_call(
        functools.partial(smooth_kernel, mask_cols, pieces),
        in_specs=[full(got)] + [full(g) for g in flat],
        out_specs=[full(o) for o in outs],
        out_shape=outs,
        scratch_shapes=[
            pltpu.VMEM((dates, bands, (shape[3] // 128) * piece, 128), jnp.float32)
            for shape, piece in zip(shapes, pieces)
        ]
        + [pltpu.VMEM((dates, dates, shape[2], 128), jnp.float32) for shape in shapes],
    )(got, *flat)


def local(scenes, resample_taps, clear_mask):
    dates, bands, rows, width = scenes.shape
    band_index = lax.axis_index("row")
    total_rows = rows * lax.axis_size("row")
    ndate = lax.axis_size("date")
    count = lax.axis_size("row")
    forward = [(i, i + 1) for i in range(count - 1)]
    backward = [(target, source) for source, target in forward]
    low = lax.ppermute(scenes[:, :, rows - 8 :], "row", forward)
    high = lax.ppermute(scenes[:, :, :8], "row", backward)
    packed = pyramid(low, scenes, high, resample_taps, band_index, total_rows, ndate)
    coeff = smooth_coefficients(clear_mask.astype(jnp.float32))
    got = lax.all_to_all(packed, "date", split_axis=0, concat_axis=0, tiled=True)
    got = got.reshape((ndate * dates,) + got.shape[2:])
    fine = rows // ndate
    total = ndate * dates
    shapes = (
        (total, bands, fine, width),
        (total, bands, fine // 2, width // 2),
        (total, bands, fine // 4, width // 4),
    )
    return tuple(smooth_all(got, coeff, shapes, piece_rows(rows, ndate)))


def solution(mesh):
    in_specs = (P(("groups", "date"), None, "row", None), P(), P("groups", ("row", "date"), None))
    out_specs = (
        P("groups", None, ("row", "date"), None),
        P("groups", None, ("row", "date"), None),
        P("groups", None, ("row", "date"), None),
    )
    return jax.shard_map(local, mesh=mesh, in_specs=in_specs, out_specs=out_specs, check_vma=False)
```

```python
import functools
import math

import jax
import numpy as np
import jax.numpy as jnp
from jax import lax
from jax.sharding import PartitionSpec as P
from jax.experimental import pallas as pl
from jax.experimental.pallas import tpu as pltpu

gap_weights = [math.exp(-((k - 4) ** 2) / 8.0) for k in range(9)]
savgol_coeffs = [c / 231.0 for c in [-21.0, 14.0, 39.0, 54.0, 59.0, 54.0, 39.0, 14.0, -21.0]]
pyramid_filter = [0.125, 0.375, 0.375, 0.125]


def split_two(a):
    high = a.astype(jnp.bfloat16)
    low = (a - high.astype(jnp.float32)).astype(jnp.bfloat16)
    return high, low


def mm(a, b):
    return jnp.dot(a, b, preferred_element_type=jnp.float32)


def band_table(rows, cols, shift, taps):
    step, weights = taps
    s_at = lax.broadcasted_iota(jnp.int32, (rows, cols), 0)
    c_at = lax.broadcasted_iota(jnp.int32, (rows, cols), 1)
    place = s_at - step * c_at - shift
    total = jnp.zeros((rows, cols), jnp.float32)
    for k, w in enumerate(weights):
        total = total + jnp.where(place == k, w, 0.0)
    return total


def halve_columns(values, table, out_ref):
    width = values.shape[1]
    high, low = split_two(values)
    for j in range(width // 256):
        lo = max(256 * j - 128, 0)
        hi_col = min(256 * j + 384, width)
        first = lo - (256 * j - 128)
        last = first + (hi_col - lo)
        part = table[first:last]
        out_ref[j, 0 : values.shape[0]] = mm(high[:, lo:hi_col], part) + mm(low[:, lo:hi_col], part)


def halve_rows(source_ref, count):
    total = pyramid_filter[0] * source_ref[:, pl.ds(0, count, stride=2), :]
    for p in range(1, 4):
        total = total + pyramid_filter[p] * source_ref[:, pl.ds(p, count, stride=2), :]
    return jnp.concatenate([total[j] for j in range(total.shape[0])], axis=1)


def piece_rows(rows, ndate):
    fine = rows // ndate
    return (fine, max(fine // 2, 8), max(fine // 4, 8))


def pyramid_kernel(ndate, total_rows, taps_ref, where_ref, low_ref, x_ref, high_ref, packed_ref,
                   across_ref, wide_ref, half_ref, quarter_ref):
    b = pl.program_id(1)
    rows = x_ref.shape[2]
    width = x_ref.shape[3]
    edge = low_ref.shape[2]
    tiles = width // 128
    column = [taps_ref[0, b, k] for k in range(7)]
    row = [taps_ref[1, b, k] for k in range(7)]
    table = band_table(3 * 128, 128, 125, (1, column))
    t_high, t_low = split_two(table)
    sources = ((low_ref, 0), (x_ref, edge), (high_ref, edge + rows))
    for source_ref, at in sources:
        x = source_ref[0, 0]
        count = x.shape[0]
        for j in range(tiles):
            lo = max(j - 1, 0) * 128
            hi_col = min(j + 2, tiles) * 128
            first = lo - (j - 1) * 128
            last = first + (hi_col - lo)
            window = x[:, lo:hi_col]
            acc = mm(window, t_high[first:last]) + mm(window, t_low[first:last])
            across_ref[at : at + count, j * 128 : (j + 1) * 128] = acc
    used = 2 * edge + rows
    depth = across_ref.shape[0]
    across_ref[used:depth, :] = jnp.zeros((depth - used, width), jnp.float32)
    band_index = where_ref[0]
    n_wide = wide_ref.shape[1]
    wide_at = lax.broadcasted_iota(jnp.int32, (n_wide, 128), 0)
    wide_row = band_index * rows - 3 + wide_at
    keep_wide = ((wide_row >= 0) & (wide_row < total_rows) & (wide_at < rows + 6)).astype(jnp.float32)
    shift = edge - 6
    for j in range(tiles):
        cols = slice(128 * j, 128 * (j + 1))
        total = row[0] * across_ref[pl.ds(shift, n_wide), cols]
        for k in range(1, 7):
            total = total + row[k] * across_ref[pl.ds(shift + k, n_wide), cols]
        wide_ref[j] = total * keep_wide
    n_half = half_ref.shape[1]
    half_at = lax.broadcasted_iota(jnp.int32, (n_half, 1), 0)
    half_row = band_index * (rows // 2) - 1 + half_at
    keep_half = ((half_row >= 0) & (half_row < total_rows // 2) & (half_at < rows // 2 + 2)).astype(jnp.float32)
    halves = halve_rows(wide_ref, n_half) * keep_half
    down = band_table(512, 128, 127, (2, pyramid_filter)).astype(jnp.bfloat16)
    halve_columns(halves, down, half_ref)
    quarters = halve_rows(half_ref, rows // 4)
    n_quarter = quarter_ref.shape[1]
    quarter_ref[:, rows // 4 : n_quarter, :] = jnp.zeros((tiles // 4, n_quarter - rows // 4, 128), jnp.float32)
    halve_columns(quarters, down, quarter_ref)
    fine, p_half, p_quarter = piece_rows(rows, ndate)
    for q in range(ndate):
        parts = [wide_ref[j, pl.ds(3 + fine * q, fine), :] for j in range(tiles)]
        parts += [half_ref[j, pl.ds(1 + (fine // 2) * q, p_half), :] for j in range(tiles // 2)]
        parts += [quarter_ref[j, pl.ds((fine // 4) * q, p_quarter), :] for j in range(tiles // 4)]
        packed_ref[q, 0, 0] = jnp.concatenate(parts, axis=0).astype(packed_ref.dtype)


def pyramid(low, scenes, high, resample_taps, band_index, total_rows, ndate):
    dates, bands, rows, width = scenes.shape
    edge = low.shape[2]
    n_wide = rows + 24
    n_half = rows // 2 + 8
    depth = max(n_wide + 8, 2 * edge + rows)
    fine, p_half, p_quarter = piece_rows(rows, ndate)
    count = (width // 128) * fine + (width // 256) * p_half + (width // 512) * p_quarter
    where = jnp.reshape(band_index, (1,)).astype(jnp.int32)
    return pl.pallas_call(
        functools.partial(pyramid_kernel, ndate, total_rows),
        grid=(dates, bands),
        in_specs=[
            pl.BlockSpec(memory_space=pltpu.SMEM),
            pl.BlockSpec(memory_space=pltpu.SMEM),
            pl.BlockSpec((1, 1, edge, width), lambda d, b: (d, b, 0, 0)),
            pl.BlockSpec((1, 1, rows, width), lambda d, b: (d, b, 0, 0)),
            pl.BlockSpec((1, 1, edge, width), lambda d, b: (d, b, 0, 0)),
        ],
        out_specs=pl.BlockSpec((ndate, 1, 1, count, 128), lambda d, b: (0, d, b, 0, 0)),
        out_shape=jax.ShapeDtypeStruct((ndate, dates, bands, count, 128), jnp.bfloat16),
        scratch_shapes=[
            pltpu.VMEM((depth, width), jnp.float32),
            pltpu.VMEM((width // 128, n_wide, 128), jnp.float32),
            pltpu.VMEM((width // 256, n_half, 128), jnp.float32),
            pltpu.VMEM((width // 512, rows // 4 + 8, 128), jnp.float32),
        ],
    )(resample_taps, where, low, scenes, high)


def smooth_operator(dates):
    clamp = np.zeros((dates, dates), np.float64)
    near = np.zeros((dates, dates), np.float64)
    for t in range(dates):
        for k in range(9):
            clamp[t, min(max(t + k - 4, 0), dates - 1)] += savgol_coeffs[k]
            if 0 <= t + k - 4 < dates:
                near[t, t + k - 4] = gap_weights[k]
    return clamp.astype(np.float32), near.astype(np.float32)


def smooth_coefficients(clear):
    dates = clear.shape[0]
    clamp, near = smooth_operator(dates)
    hi = lax.Precision.HIGHEST
    weight = 0.1 + 0.9 * clear
    denom = jnp.einsum("su,uxy->sxy", near, weight, precision=hi)
    gap = (1.0 - clear) / denom
    fill = near[:, :, None, None] * weight[None, :] * gap[:, None]
    fill = fill + np.eye(dates, dtype=np.float32)[:, :, None, None] * clear[None, :]
    return jnp.einsum("ts,suxy->tuxy", clamp, fill, precision=hi)


def smooth_level(mask_cols, got_ref, start, piece, coeff_ref, out_ref, section_ref, tiles_ref):
    dates, bands, rows, width = out_ref.shape
    tiles = width // 128
    span = width // mask_cols
    parts = split_two(coeff_ref[...])
    m_at = lax.broadcasted_iota(jnp.int32, (128, 128), 0)
    lane = lax.broadcasted_iota(jnp.int32, (128, 128), 1)
    for j in range(tiles):
        pick = (m_at == (128 * j + lane) // span).astype(jnp.bfloat16)
        grown = mm(parts[0], pick) + mm(parts[1], pick)
        tiles_ref[...] = grown.reshape(tiles_ref.shape)

        step = min(rows, 8)

        def one_block(r, carry):
            r0 = pl.multiple_of(r * step, step)
            values = [
                [got_ref[u, band, pl.ds(start + j * piece + r0, step), :].astype(jnp.float32) for band in range(bands)]
                for u in range(dates)
            ]
            for t in range(dates):
                weights = [tiles_ref[t, u, pl.ds(r0, step), :] for u in range(dates)]
                for band in range(bands):
                    acc = weights[0] * values[0][band]
                    for u in range(1, dates):
                        acc = acc + weights[u] * values[u][band]
                    out_ref[t, band, pl.ds(r0, step), 128 * j : 128 * (j + 1)] = acc.astype(out_ref.dtype)
            return carry

        lax.fori_loop(0, rows // step, one_block, 0)


def smooth_kernel(mask_cols, pieces, got_ref, c0_ref, c1_ref, c2_ref, o0_ref, o1_ref, o2_ref,
                  s0_ref, s1_ref, s2_ref, t0_ref, t1_ref, t2_ref):
    start = 0
    levels = zip(pieces, (c0_ref, c1_ref, c2_ref), (o0_ref, o1_ref, o2_ref), (s0_ref, s1_ref, s2_ref), (t0_ref, t1_ref, t2_ref))
    for piece, c_ref, o_ref, s_ref, t_ref in levels:
        smooth_level(mask_cols, got_ref, start, piece, c_ref, o_ref, s_ref, t_ref)
        start += (o_ref.shape[3] // 128) * piece


def smooth_all(got, coeff, shapes, pieces):
    dates, bands = got.shape[:2]
    mask_cols = coeff.shape[3]
    flat = []
    for shape in shapes:
        grown = jnp.repeat(coeff, shape[2] // coeff.shape[2], axis=2)
        grown = grown.reshape(-1, mask_cols)
        flat.append(jnp.pad(grown, ((0, 0), (0, 128 - mask_cols))))
    full = lambda a: pl.BlockSpec(a.shape, lambda: (0,) * len(a.shape))
    outs = [jax.ShapeDtypeStruct(shape, jnp.bfloat16) for shape in shapes]
    return pl.pallas_call(
        functools.partial(smooth_kernel, mask_cols, pieces),
        in_specs=[full(got)] + [full(g) for g in flat],
        out_specs=[full(o) for o in outs],
        out_shape=outs,
        scratch_shapes=[
            pltpu.VMEM((dates, bands, (shape[3] // 128) * piece, 128), jnp.float32)
            for shape, piece in zip(shapes, pieces)
        ]
        + [pltpu.VMEM((dates, dates, shape[2], 128), jnp.float32) for shape in shapes],
    )(got, *flat)


def local(scenes, resample_taps, clear_mask):
    dates, bands, rows, width = scenes.shape
    band_index = lax.axis_index("row")
    total_rows = rows * lax.axis_size("row")
    ndate = lax.axis_size("date")
    count = lax.axis_size("row")
    forward = [(i, i + 1) for i in range(count - 1)]
    backward = [(target, source) for source, target in forward]
    low = lax.ppermute(scenes[:, :, rows - 8 :], "row", forward)
    high = lax.ppermute(scenes[:, :, :8], "row", backward)
    packed = pyramid(low, scenes, high, resample_taps, band_index, total_rows, ndate)
    coeff = smooth_coefficients(clear_mask.astype(jnp.float32))
    got = lax.all_to_all(packed, "date", split_axis=0, concat_axis=0, tiled=True)
    got = got.reshape((ndate * dates,) + got.shape[2:])
    fine = rows // ndate
    total = ndate * dates
    shapes = (
        (total, bands, fine, width),
        (total, bands, fine // 2, width // 2),
        (total, bands, fine // 4, width // 4),
    )
    return tuple(smooth_all(got, coeff, shapes, piece_rows(rows, ndate)))


def solution(mesh):
    in_specs = (P(("groups", "date"), None, "row", None), P(), P("groups", ("row", "date"), None))
    out_specs = (
        P("groups", None, ("row", "date"), None),
        P("groups", None, ("row", "date"), None),
        P("groups", None, ("row", "date"), None),
    )
    return jax.shard_map(local, mesh=mesh, in_specs=in_specs, out_specs=out_specs, check_vma=False)
```

```python
import functools
import math

import jax
import numpy as np
import jax.numpy as jnp
from jax import lax
from jax.sharding import PartitionSpec as P
from jax.experimental import pallas as pl
from jax.experimental.pallas import tpu as pltpu

gap_weights = [math.exp(-((k - 4) ** 2) / 8.0) for k in range(9)]
savgol_coeffs = [c / 231.0 for c in [-21.0, 14.0, 39.0, 54.0, 59.0, 54.0, 39.0, 14.0, -21.0]]
pyramid_filter = [0.125, 0.375, 0.375, 0.125]


def split_two(a):
    high = a.astype(jnp.bfloat16)
    low = (a - high.astype(jnp.float32)).astype(jnp.bfloat16)
    return high, low


def mm(a, b):
    return jnp.dot(a, b, preferred_element_type=jnp.float32)


def band_table(rows, cols, shift, taps):
    step, weights = taps
    s_at = lax.broadcasted_iota(jnp.int32, (rows, cols), 0)
    c_at = lax.broadcasted_iota(jnp.int32, (rows, cols), 1)
    place = s_at - step * c_at - shift
    total = jnp.zeros((rows, cols), jnp.float32)
    for k, w in enumerate(weights):
        total = total + jnp.where(place == k, w, 0.0)
    return total


def halve_columns(values, table, out_ref):
    width = values.shape[1]
    high, low = split_two(values)
    for j in range(width // 256):
        lo = max(256 * j - 128, 0)
        hi_col = min(256 * j + 384, width)
        first = lo - (256 * j - 128)
        last = first + (hi_col - lo)
        part = table[first:last]
        out_ref[j, 0 : values.shape[0]] = mm(high[:, lo:hi_col], part) + mm(low[:, lo:hi_col], part)


def halve_rows(source_ref, count):
    total = pyramid_filter[0] * source_ref[:, pl.ds(0, count, stride=2), :]
    for p in range(1, 4):
        total = total + pyramid_filter[p] * source_ref[:, pl.ds(p, count, stride=2), :]
    return jnp.concatenate([total[j] for j in range(total.shape[0])], axis=1)


def piece_rows(rows, ndate):
    fine = rows // ndate
    return (fine, max(fine // 2, 8), max(fine // 4, 8))


def pyramid_kernel(ndate, total_rows, taps_ref, where_ref, low_ref, x_ref, high_ref, packed_ref,
                   across_ref, wide_ref, half_ref, quarter_ref):
    b = pl.program_id(1)
    rows = x_ref.shape[2]
    width = x_ref.shape[3]
    edge = low_ref.shape[2]
    tiles = width // 128
    column = [taps_ref[0, b, k] for k in range(7)]
    row = [taps_ref[1, b, k] for k in range(7)]
    table = band_table(3 * 128, 128, 125, (1, column))
    t_high, t_low = split_two(table)
    sources = ((low_ref, 0), (x_ref, edge), (high_ref, edge + rows))
    for source_ref, at in sources:
        x = source_ref[0, 0]
        count = x.shape[0]
        for j in range(tiles):
            lo = max(j - 1, 0) * 128
            hi_col = min(j + 2, tiles) * 128
            first = lo - (j - 1) * 128
            last = first + (hi_col - lo)
            window = x[:, lo:hi_col]
            acc = mm(window, t_high[first:last]) + mm(window, t_low[first:last])
            across_ref[at : at + count, j * 128 : (j + 1) * 128] = acc
    used = 2 * edge + rows
    depth = across_ref.shape[0]
    across_ref[used:depth, :] = jnp.zeros((depth - used, width), jnp.float32)
    band_index = where_ref[0]
    n_wide = wide_ref.shape[1]
    wide_at = lax.broadcasted_iota(jnp.int32, (n_wide, 128), 0)
    wide_row = band_index * rows - 3 + wide_at
    keep_wide = ((wide_row >= 0) & (wide_row < total_rows) & (wide_at < rows + 6)).astype(jnp.float32)
    shift = edge - 6
    for j in range(tiles):
        cols = slice(128 * j, 128 * (j + 1))
        total = row[0] * across_ref[pl.ds(shift, n_wide), cols]
        for k in range(1, 7):
            total = total + row[k] * across_ref[pl.ds(shift + k, n_wide), cols]
        wide_ref[j] = total * keep_wide
    n_half = half_ref.shape[1]
    half_at = lax.broadcasted_iota(jnp.int32, (n_half, 1), 0)
    half_row = band_index * (rows // 2) - 1 + half_at
    keep_half = ((half_row >= 0) & (half_row < total_rows // 2) & (half_at < rows // 2 + 2)).astype(jnp.float32)
    halves = halve_rows(wide_ref, n_half) * keep_half
    down = band_table(512, 128, 127, (2, pyramid_filter)).astype(jnp.bfloat16)
    halve_columns(halves, down, half_ref)
    quarters = halve_rows(half_ref, rows // 4)
    n_quarter = quarter_ref.shape[1]
    quarter_ref[:, rows // 4 : n_quarter, :] = jnp.zeros((tiles // 4, n_quarter - rows // 4, 128), jnp.float32)
    halve_columns(quarters, down, quarter_ref)
    fine, p_half, p_quarter = piece_rows(rows, ndate)
    for q in range(ndate):
        parts = [wide_ref[j, pl.ds(3 + fine * q, fine), :] for j in range(tiles)]
        parts += [half_ref[j, pl.ds(1 + (fine // 2) * q, p_half), :] for j in range(tiles // 2)]
        parts += [quarter_ref[j, pl.ds((fine // 4) * q, p_quarter), :] for j in range(tiles // 4)]
        packed_ref[q, 0, 0] = jnp.concatenate(parts, axis=0).astype(packed_ref.dtype)


def pyramid(low, scenes, high, resample_taps, band_index, total_rows, ndate):
    dates, bands, rows, width = scenes.shape
    edge = low.shape[2]
    n_wide = rows + 24
    n_half = rows // 2 + 8
    depth = max(n_wide + 8, 2 * edge + rows)
    fine, p_half, p_quarter = piece_rows(rows, ndate)
    count = (width // 128) * fine + (width // 256) * p_half + (width // 512) * p_quarter
    where = jnp.reshape(band_index, (1,)).astype(jnp.int32)
    return pl.pallas_call(
        functools.partial(pyramid_kernel, ndate, total_rows),
        grid=(dates, bands),
        in_specs=[
            pl.BlockSpec(memory_space=pltpu.SMEM),
            pl.BlockSpec(memory_space=pltpu.SMEM),
            pl.BlockSpec((1, 1, edge, width), lambda d, b: (d, b, 0, 0)),
            pl.BlockSpec((1, 1, rows, width), lambda d, b: (d, b, 0, 0)),
            pl.BlockSpec((1, 1, edge, width), lambda d, b: (d, b, 0, 0)),
        ],
        out_specs=pl.BlockSpec((ndate, 1, 1, count, 128), lambda d, b: (0, d, b, 0, 0)),
        out_shape=jax.ShapeDtypeStruct((ndate, dates, bands, count, 128), jnp.bfloat16),
        scratch_shapes=[
            pltpu.VMEM((depth, width), jnp.float32),
            pltpu.VMEM((width // 128, n_wide, 128), jnp.float32),
            pltpu.VMEM((width // 256, n_half, 128), jnp.float32),
            pltpu.VMEM((width // 512, rows // 4 + 8, 128), jnp.float32),
        ],
    )(resample_taps, where, low, scenes, high)


def smooth_operator(dates):
    clamp = np.zeros((dates, dates), np.float64)
    near = np.zeros((dates, dates), np.float64)
    for t in range(dates):
        for k in range(9):
            clamp[t, min(max(t + k - 4, 0), dates - 1)] += savgol_coeffs[k]
            if 0 <= t + k - 4 < dates:
                near[t, t + k - 4] = gap_weights[k]
    return clamp.astype(np.float32), near.astype(np.float32)


def smooth_coefficients(clear):
    dates = clear.shape[0]
    clamp, near = smooth_operator(dates)
    hi = lax.Precision.HIGHEST
    weight = 0.1 + 0.9 * clear
    denom = jnp.einsum("su,uxy->sxy", near, weight, precision=hi)
    gap = (1.0 - clear) / denom
    fill = near[:, :, None, None] * weight[None, :] * gap[:, None]
    fill = fill + np.eye(dates, dtype=np.float32)[:, :, None, None] * clear[None, :]
    return jnp.einsum("ts,suxy->tuxy", clamp, fill, precision=hi)


def smooth_level(mask_cols, got_ref, start, piece, coeff_ref, out_ref, section_ref, tiles_ref):
    dates, bands, rows, width = out_ref.shape
    tiles = width // 128
    span = width // mask_cols
    parts = split_two(coeff_ref[...])
    m_at = lax.broadcasted_iota(jnp.int32, (128, 128), 0)
    lane = lax.broadcasted_iota(jnp.int32, (128, 128), 1)
    for j in range(tiles):
        pick = (m_at == (128 * j + lane) // span).astype(jnp.bfloat16)
        grown = mm(parts[0], pick) + mm(parts[1], pick)
        tiles_ref[...] = grown.reshape(tiles_ref.shape)

        step = min(rows, 8)

        def one_block(r, carry):
            r0 = pl.multiple_of(r * step, step)
            values = [
                [got_ref[u, band, pl.ds(start + j * piece + r0, step), :].astype(jnp.float32) for band in range(bands)]
                for u in range(dates)
            ]
            for t in range(dates):
                weights = [tiles_ref[t, u, pl.ds(r0, step), :] for u in range(dates)]
                for band in range(bands):
                    acc = weights[0] * values[0][band]
                    for u in range(1, dates):
                        acc = acc + weights[u] * values[u][band]
                    out_ref[t, band, pl.ds(r0, step), 128 * j : 128 * (j + 1)] = acc.astype(out_ref.dtype)
            return carry

        lax.fori_loop(0, rows // step, one_block, 0, unroll=True)


def smooth_kernel(mask_cols, pieces, got_ref, c0_ref, c1_ref, c2_ref, o0_ref, o1_ref, o2_ref,
                  s0_ref, s1_ref, s2_ref, t0_ref, t1_ref, t2_ref):
    start = 0
    levels = zip(pieces, (c0_ref, c1_ref, c2_ref), (o0_ref, o1_ref, o2_ref), (s0_ref, s1_ref, s2_ref), (t0_ref, t1_ref, t2_ref))
    for piece, c_ref, o_ref, s_ref, t_ref in levels:
        smooth_level(mask_cols, got_ref, start, piece, c_ref, o_ref, s_ref, t_ref)
        start += (o_ref.shape[3] // 128) * piece


def smooth_all(got, coeff, shapes, pieces):
    dates, bands = got.shape[:2]
    mask_cols = coeff.shape[3]
    flat = []
    for shape in shapes:
        grown = jnp.repeat(coeff, shape[2] // coeff.shape[2], axis=2)
        grown = grown.reshape(-1, mask_cols)
        flat.append(jnp.pad(grown, ((0, 0), (0, 128 - mask_cols))))
    full = lambda a: pl.BlockSpec(a.shape, lambda: (0,) * len(a.shape))
    outs = [jax.ShapeDtypeStruct(shape, jnp.bfloat16) for shape in shapes]
    return pl.pallas_call(
        functools.partial(smooth_kernel, mask_cols, pieces),
        in_specs=[full(got)] + [full(g) for g in flat],
        out_specs=[full(o) for o in outs],
        out_shape=outs,
        scratch_shapes=[
            pltpu.VMEM((dates, bands, (shape[3] // 128) * piece, 128), jnp.float32)
            for shape, piece in zip(shapes, pieces)
        ]
        + [pltpu.VMEM((dates, dates, shape[2], 128), jnp.float32) for shape in shapes],
    )(got, *flat)


def local(scenes, resample_taps, clear_mask):
    dates, bands, rows, width = scenes.shape
    band_index = lax.axis_index("row")
    total_rows = rows * lax.axis_size("row")
    ndate = lax.axis_size("date")
    count = lax.axis_size("row")
    forward = [(i, i + 1) for i in range(count - 1)]
    backward = [(target, source) for source, target in forward]
    low = lax.ppermute(scenes[:, :, rows - 8 :], "row", forward)
    high = lax.ppermute(scenes[:, :, :8], "row", backward)
    packed = pyramid(low, scenes, high, resample_taps, band_index, total_rows, ndate)
    coeff = smooth_coefficients(clear_mask.astype(jnp.float32))
    got = lax.all_to_all(packed, "date", split_axis=0, concat_axis=0, tiled=True)
    got = got.reshape((ndate * dates,) + got.shape[2:])
    fine = rows // ndate
    total = ndate * dates
    shapes = (
        (total, bands, fine, width),
        (total, bands, fine // 2, width // 2),
        (total, bands, fine // 4, width // 4),
    )
    return tuple(smooth_all(got, coeff, shapes, piece_rows(rows, ndate)))


def solution(mesh):
    in_specs = (P(("groups", "date"), None, "row", None), P(), P("groups", ("row", "date"), None))
    out_specs = (
        P("groups", None, ("row", "date"), None),
        P("groups", None, ("row", "date"), None),
        P("groups", None, ("row", "date"), None),
    )
    return jax.shard_map(local, mesh=mesh, in_specs=in_specs, out_specs=out_specs, check_vma=False)
```

```python
import functools
import math

import jax
import numpy as np
import jax.numpy as jnp
from jax import lax
from jax.sharding import PartitionSpec as P
from jax.experimental import pallas as pl
from jax.experimental.pallas import tpu as pltpu

gap_weights = [math.exp(-((k - 4) ** 2) / 8.0) for k in range(9)]
savgol_coeffs = [c / 231.0 for c in [-21.0, 14.0, 39.0, 54.0, 59.0, 54.0, 39.0, 14.0, -21.0]]
pyramid_filter = [0.125, 0.375, 0.375, 0.125]


def split_two(a):
    high = a.astype(jnp.bfloat16)
    low = (a - high.astype(jnp.float32)).astype(jnp.bfloat16)
    return high, low


def mm(a, b):
    return jnp.dot(a, b, preferred_element_type=jnp.float32)


def band_table(rows, cols, shift, taps):
    step, weights = taps
    s_at = lax.broadcasted_iota(jnp.int32, (rows, cols), 0)
    c_at = lax.broadcasted_iota(jnp.int32, (rows, cols), 1)
    place = s_at - step * c_at - shift
    total = jnp.zeros((rows, cols), jnp.float32)
    for k, w in enumerate(weights):
        total = total + jnp.where(place == k, w, 0.0)
    return total


def halve_columns(values, table, out_ref):
    width = values.shape[1]
    high, low = split_two(values)
    for j in range(width // 256):
        lo = max(256 * j - 128, 0)
        hi_col = min(256 * j + 384, width)
        first = lo - (256 * j - 128)
        last = first + (hi_col - lo)
        part = table[first:last]
        out_ref[j, 0 : values.shape[0]] = mm(high[:, lo:hi_col], part) + mm(low[:, lo:hi_col], part)


def halve_rows(source_ref, count):
    total = pyramid_filter[0] * source_ref[:, pl.ds(0, count, stride=2), :]
    for p in range(1, 4):
        total = total + pyramid_filter[p] * source_ref[:, pl.ds(p, count, stride=2), :]
    return jnp.concatenate([total[j] for j in range(total.shape[0])], axis=1)


def piece_rows(rows, ndate):
    fine = rows // ndate
    return (fine, max(fine // 2, 8), max(fine // 4, 8))


def pyramid_kernel(ndate, total_rows, taps_ref, where_ref, low_ref, x_ref, high_ref, packed_ref,
                   across_ref, wide_ref, half_ref, quarter_ref):
    b = pl.program_id(1)
    rows = x_ref.shape[2]
    width = x_ref.shape[3]
    edge = low_ref.shape[2]
    tiles = width // 128
    column = [taps_ref[0, b, k] for k in range(7)]
    row = [taps_ref[1, b, k] for k in range(7)]
    table = band_table(3 * 128, 128, 125, (1, column))
    t_high, t_low = split_two(table)
    sources = ((low_ref, 0), (x_ref, edge), (high_ref, edge + rows))
    for source_ref, at in sources:
        x = source_ref[0, 0]
        count = x.shape[0]
        for j in range(tiles):
            lo = max(j - 1, 0) * 128
            hi_col = min(j + 2, tiles) * 128
            first = lo - (j - 1) * 128
            last = first + (hi_col - lo)
            window = x[:, lo:hi_col]
            acc = mm(window, t_high[first:last]) + mm(window, t_low[first:last])
            across_ref[at : at + count, j * 128 : (j + 1) * 128] = acc
    used = 2 * edge + rows
    depth = across_ref.shape[0]
    across_ref[used:depth, :] = jnp.zeros((depth - used, width), jnp.float32)
    band_index = where_ref[0]
    n_wide = wide_ref.shape[1]
    wide_at = lax.broadcasted_iota(jnp.int32, (n_wide, 128), 0)
    wide_row = band_index * rows - 3 + wide_at
    keep_wide = ((wide_row >= 0) & (wide_row < total_rows) & (wide_at < rows + 6)).astype(jnp.float32)
    shift = edge - 6
    for j in range(tiles):
        cols = slice(128 * j, 128 * (j + 1))
        total = row[0] * across_ref[pl.ds(shift, n_wide), cols]
        for k in range(1, 7):
            total = total + row[k] * across_ref[pl.ds(shift + k, n_wide), cols]
        wide_ref[j] = total * keep_wide
    n_half = half_ref.shape[1]
    half_at = lax.broadcasted_iota(jnp.int32, (n_half, 1), 0)
    half_row = band_index * (rows // 2) - 1 + half_at
    keep_half = ((half_row >= 0) & (half_row < total_rows // 2) & (half_at < rows // 2 + 2)).astype(jnp.float32)
    halves = halve_rows(wide_ref, n_half) * keep_half
    down = band_table(512, 128, 127, (2, pyramid_filter)).astype(jnp.bfloat16)
    halve_columns(halves, down, half_ref)
    quarters = halve_rows(half_ref, rows // 4)
    n_quarter = quarter_ref.shape[1]
    quarter_ref[:, rows // 4 : n_quarter, :] = jnp.zeros((tiles // 4, n_quarter - rows // 4, 128), jnp.float32)
    halve_columns(quarters, down, quarter_ref)
    fine, p_half, p_quarter = piece_rows(rows, ndate)
    for q in range(ndate):
        parts = [wide_ref[j, pl.ds(3 + fine * q, fine), :] for j in range(tiles)]
        parts += [half_ref[j, pl.ds(1 + (fine // 2) * q, p_half), :] for j in range(tiles // 2)]
        parts += [quarter_ref[j, pl.ds((fine // 4) * q, p_quarter), :] for j in range(tiles // 4)]
        packed_ref[q, 0, 0] = jnp.concatenate(parts, axis=0).astype(packed_ref.dtype)


def pyramid(low, scenes, high, resample_taps, band_index, total_rows, ndate):
    dates, bands, rows, width = scenes.shape
    edge = low.shape[2]
    n_wide = rows + 24
    n_half = rows // 2 + 8
    depth = max(n_wide + 8, 2 * edge + rows)
    fine, p_half, p_quarter = piece_rows(rows, ndate)
    count = (width // 128) * fine + (width // 256) * p_half + (width // 512) * p_quarter
    where = jnp.reshape(band_index, (1,)).astype(jnp.int32)
    return pl.pallas_call(
        functools.partial(pyramid_kernel, ndate, total_rows),
        grid=(dates, bands),
        in_specs=[
            pl.BlockSpec(memory_space=pltpu.SMEM),
            pl.BlockSpec(memory_space=pltpu.SMEM),
            pl.BlockSpec((1, 1, edge, width), lambda d, b: (d, b, 0, 0)),
            pl.BlockSpec((1, 1, rows, width), lambda d, b: (d, b, 0, 0)),
            pl.BlockSpec((1, 1, edge, width), lambda d, b: (d, b, 0, 0)),
        ],
        out_specs=pl.BlockSpec((ndate, 1, 1, count, 128), lambda d, b: (0, d, b, 0, 0)),
        out_shape=jax.ShapeDtypeStruct((ndate, dates, bands, count, 128), jnp.bfloat16),
        scratch_shapes=[
            pltpu.VMEM((depth, width), jnp.float32),
            pltpu.VMEM((width // 128, n_wide, 128), jnp.float32),
            pltpu.VMEM((width // 256, n_half, 128), jnp.float32),
            pltpu.VMEM((width // 512, rows // 4 + 8, 128), jnp.float32),
        ],
    )(resample_taps, where, low, scenes, high)


def smooth_operator(dates):
    clamp = np.zeros((dates, dates), np.float64)
    near = np.zeros((dates, dates), np.float64)
    for t in range(dates):
        for k in range(9):
            clamp[t, min(max(t + k - 4, 0), dates - 1)] += savgol_coeffs[k]
            if 0 <= t + k - 4 < dates:
                near[t, t + k - 4] = gap_weights[k]
    return clamp.astype(np.float32), near.astype(np.float32)


def smooth_coefficients(clear):
    dates = clear.shape[0]
    clamp, near = smooth_operator(dates)
    hi = lax.Precision.HIGHEST
    weight = 0.1 + 0.9 * clear
    denom = jnp.einsum("su,uxy->sxy", near, weight, precision=hi)
    gap = (1.0 - clear) / denom
    fill = near[:, :, None, None] * weight[None, :] * gap[:, None]
    fill = fill + np.eye(dates, dtype=np.float32)[:, :, None, None] * clear[None, :]
    return jnp.einsum("ts,suxy->tuxy", clamp, fill, precision=hi)


def smooth_level(mask_cols, got_ref, start, piece, coeff_ref, out_ref, section_ref, tiles_ref):
    dates, bands, rows, width = out_ref.shape
    tiles = width // 128
    span = width // mask_cols
    parts = split_two(coeff_ref[...])
    m_at = lax.broadcasted_iota(jnp.int32, (128, 128), 0)
    lane = lax.broadcasted_iota(jnp.int32, (128, 128), 1)
    for j in range(tiles):
        pick = (m_at == (128 * j + lane) // span).astype(jnp.bfloat16)
        grown = mm(parts[0], pick) + mm(parts[1], pick)
        tiles_ref[j % 2] = grown.reshape(tiles_ref.shape[1:])

        step = min(rows, 8)

        def one_block(r, carry):
            r0 = pl.multiple_of(r * step, step)
            values = [
                [got_ref[u, band, pl.ds(start + j * piece + r0, step), :].astype(jnp.float32) for band in range(bands)]
                for u in range(dates)
            ]
            for t in range(dates):
                weights = [tiles_ref[j % 2, t, u, pl.ds(r0, step), :] for u in range(dates)]
                for band in range(bands):
                    acc = weights[0] * values[0][band]
                    for u in range(1, dates):
                        acc = acc + weights[u] * values[u][band]
                    out_ref[t, band, pl.ds(r0, step), 128 * j : 128 * (j + 1)] = acc.astype(out_ref.dtype)
            return carry

        lax.fori_loop(0, rows // step, one_block, 0, unroll=True)


def smooth_kernel(mask_cols, pieces, got_ref, c0_ref, c1_ref, c2_ref, o0_ref, o1_ref, o2_ref,
                  s0_ref, s1_ref, s2_ref, t0_ref, t1_ref, t2_ref):
    start = 0
    levels = zip(pieces, (c0_ref, c1_ref, c2_ref), (o0_ref, o1_ref, o2_ref), (s0_ref, s1_ref, s2_ref), (t0_ref, t1_ref, t2_ref))
    for piece, c_ref, o_ref, s_ref, t_ref in levels:
        smooth_level(mask_cols, got_ref, start, piece, c_ref, o_ref, s_ref, t_ref)
        start += (o_ref.shape[3] // 128) * piece


def smooth_all(got, coeff, shapes, pieces):
    dates, bands = got.shape[:2]
    mask_cols = coeff.shape[3]
    flat = []
    for shape in shapes:
        grown = jnp.repeat(coeff, shape[2] // coeff.shape[2], axis=2)
        grown = grown.reshape(-1, mask_cols)
        flat.append(jnp.pad(grown, ((0, 0), (0, 128 - mask_cols))))
    full = lambda a: pl.BlockSpec(a.shape, lambda: (0,) * len(a.shape))
    outs = [jax.ShapeDtypeStruct(shape, jnp.bfloat16) for shape in shapes]
    return pl.pallas_call(
        functools.partial(smooth_kernel, mask_cols, pieces),
        in_specs=[full(got)] + [full(g) for g in flat],
        out_specs=[full(o) for o in outs],
        out_shape=outs,
        scratch_shapes=[
            pltpu.VMEM((dates, bands, (shape[3] // 128) * piece, 128), jnp.float32)
            for shape, piece in zip(shapes, pieces)
        ]
        + [pltpu.VMEM((2, dates, dates, shape[2], 128), jnp.float32) for shape in shapes],
    )(got, *flat)


def local(scenes, resample_taps, clear_mask):
    dates, bands, rows, width = scenes.shape
    band_index = lax.axis_index("row")
    total_rows = rows * lax.axis_size("row")
    ndate = lax.axis_size("date")
    count = lax.axis_size("row")
    forward = [(i, i + 1) for i in range(count - 1)]
    backward = [(target, source) for source, target in forward]
    low = lax.ppermute(scenes[:, :, rows - 8 :], "row", forward)
    high = lax.ppermute(scenes[:, :, :8], "row", backward)
    packed = pyramid(low, scenes, high, resample_taps, band_index, total_rows, ndate)
    coeff = smooth_coefficients(clear_mask.astype(jnp.float32))
    got = lax.all_to_all(packed, "date", split_axis=0, concat_axis=0, tiled=True)
    got = got.reshape((ndate * dates,) + got.shape[2:])
    fine = rows // ndate
    total = ndate * dates
    shapes = (
        (total, bands, fine, width),
        (total, bands, fine // 2, width // 2),
        (total, bands, fine // 4, width // 4),
    )
    return tuple(smooth_all(got, coeff, shapes, piece_rows(rows, ndate)))


def solution(mesh):
    in_specs = (P(("groups", "date"), None, "row", None), P(), P("groups", ("row", "date"), None))
    out_specs = (
        P("groups", None, ("row", "date"), None),
        P("groups", None, ("row", "date"), None),
        P("groups", None, ("row", "date"), None),
    )
    return jax.shard_map(local, mesh=mesh, in_specs=in_specs, out_specs=out_specs, check_vma=False)
```
